128 devices in a mesh: seq: 16 (over z, y), tp: 8 (over x, core).
Axes of the slice: x: 4, y: 4, z: 4, core: 2. Of those that a mesh axis runs over, the one named last changes fastest.
Arguments:
- tokens: bfloat16 [8192, 3072], P('seq'), may hold values from -6 to 6
- norm_gain: bfloat16 [3072], replicated, may hold values from 0.099609375 to 1.8984375
- w_qkv: bfloat16 [3072, 3, 3072], P(None, None, 'tp'), may hold values from -0.25 to 0.25
- w_out: bfloat16 [3072, 3072], P('tp'), may hold values from -0.0546875 to 0.0546875
- kv_cache: bfloat16 [2, 16, 3584, 3072], P(None, 'seq', None, 'tp')
- cached_lengths: int32 [16], replicated, may hold values from 128 to 3584, as said below
- requests: int32 [16], replicated, may hold values from 8 to 16
- block_start: int32 [16], replicated, may hold values from 0 to 31
Outputs:
- layer_out: bfloat16 [8192, 3072], P(('seq', 'tp'))
- decode_cache: bfloat16 [2, 16, 16, 1, 128, 6144], P(None, 'seq', None, None, None, 'tp')
The draws below stay inside these ranges and needn't reach their ends.
Inputs may be any that keep to these rules, and one draw needn't show every extreme that they name: `cached_lengths`: every entry is a multiple of 128, and some group has exactly 3584 cached positions.
All inputs are finite; a program needn't handle non-finite values.
Results may differ from the reference program's by a relative error of at most 0.014.
The reference program's roundings to bfloat16 on the way count: a program that leaves them out, or rounds other values in their place, can miss the bound.
Values may be sent and summed in bfloat16 or wider, within the bound.
No kernel may reach another device: no remote copies, remote signals or barrier semaphores. Data moves between devices by JAX's collectives and lax.ppermute only.
A program may use at most 192 MiB of HBM per device.

```python
import math
import jax
import jax.numpy as jnp
from jax import lax

D = 3072
H = 32
HD = 96
CTX = 4096
BLK = 128
C = 512
G = 16
TOKENS = 8192
LMAX = 3584
RANKS = 32
SLOTS = 1
N_SEQ = 16
N_TP = 8


def draw_cached_lengths(key, part):
    first_key, second_key = jax.random.split(key)
    block_count = jax.random.randint(first_key, (G,), 1, LMAX // BLK + 1)
    longest = jax.random.randint(second_key, (), 0, G)
    block_count = jnp.where(jnp.arange(G) == longest, LMAX // BLK, block_count)
    return (block_count * BLK).astype(jnp.int32)


def draw_kv_cache(key, part):
    first_key = jax.random.fold_in(jax.random.fold_in(key, 17), 0)
    shape_full = (2, G, LMAX, H * HD)
    drawn = jnp.clip(jax.random.normal(first_key, shape_full, jnp.float32) * 2.5, -15.0, 15.0)
    return drawn.astype(jnp.bfloat16)


def plant(values, own_key, smallest, top_value):
    place = [jax.random.randint(jax.random.fold_in(own_key, axis), (), 0, length) for axis, length in enumerate(values.shape)]
    widest = values.shape.index(max(values.shape))
    neighbour = place[:widest] + [(place[widest] + 1) % values.shape[widest]] + place[widest + 1:]
    return values.at[tuple(place)].set(smallest).at[tuple(neighbour)].set(top_value)


def steps_of(stream_key, extent, cuts, least, largest):
    level = 1.0
    for dim, parts in cuts:
        draws = jax.random.uniform(jax.random.fold_in(jax.random.fold_in(stream_key, 6), dim), (parts,), jnp.float32, least / len(cuts), largest / len(cuts))
        level = level * jnp.repeat(jnp.exp(draws), extent[dim] // parts).reshape((-1,) + (1,) * (len(extent) - 1 - dim))
    return level


def gaussian(rng, extent, spread, most, shards=(), kind=jnp.bfloat16):
    values = jax.random.normal(rng, extent, jnp.float32) * spread
    if len(shards) > 0:
        values = steps_of(rng, extent, shards, -0.22, 0.18) * values
    return jnp.clip(values, min=-most, max=most).astype(kind)


def setup_inputs(seed: int = 0) -> dict:
    keys = jax.random.split(jax.random.key(seed), 9)
    tokens = gaussian(keys[0], (TOKENS, D), 1.0, 6.0, ((0, 16),))
    norm_gain = jnp.clip(1.0 + 0.18 * jax.random.normal(keys[1], (D,), jnp.float32), 0.099609375, 1.8984375).astype(jnp.bfloat16)
    w_qkv = gaussian(keys[2], (D, 3, H * HD), (D // 6) ** -0.5, 0.25, ((2, 8),))
    w_out = gaussian(keys[3], (H * HD, D), (4 * H * HD) ** -0.5, 0.0546875, ((0, 8),))
    kv_cache = draw_kv_cache(jax.random.fold_in(keys[8], 71), 0)
    cached_lengths = draw_cached_lengths(jax.random.fold_in(keys[8], 71), 0)
    requests = plant(jax.random.randint(keys[6], (G,), 8, 17), jax.random.fold_in(keys[6], 1), 8, 16).astype(jnp.int32)
    block_start = plant(jax.random.randint(keys[7], (G,), 0, RANKS), jax.random.fold_in(keys[7], 1), 0, RANKS - 1).astype(jnp.int32)
    return dict(tokens=tokens, norm_gain=norm_gain, w_qkv=w_qkv, w_out=w_out, kv_cache=kv_cache, cached_lengths=cached_lengths, requests=requests, block_start=block_start)


def rope_tables(positions, head_size):
    half_size = head_size // 2
    frequency = jnp.exp(jnp.arange(half_size, dtype=jnp.float32) * (-2.0 * math.log(10000.0) / head_size))
    angles = positions.astype(jnp.float32)[:, None] * frequency[None, :]
    return (jnp.cos(angles), jnp.sin(angles))

def rope_pair(vectors, cosine_table, sine_table):
    half_size = vectors.shape[-1] // 2
    first_half = vectors[..., :half_size]
    second_half = vectors[..., half_size:]
    cos_wide = cosine_table[:, None, :]
    sin_wide = sine_table[:, None, :]
    return jnp.concatenate([first_half * cos_wide - second_half * sin_wide, second_half * cos_wide + first_half * sin_wide], axis=-1)

def visibility(group_len, group_requests, row_index, request, key_pos, tok_count):
    offset_rows = key_pos - group_len
    new_key = (offset_rows >= 0) & (offset_rows < tok_count)
    clipped = jnp.clip(offset_rows, 0, tok_count - 1)
    key_request = clipped * group_requests // tok_count
    return (key_pos[None, :] < group_len) | new_key[None, :] & (key_request[None, :] == request[:, None]) & (clipped[None, :] <= row_index[:, None])

def reference(tokens, norm_gain, w_qkv, w_out, kv_cache, cached_lengths, requests, block_start):
    features = H * HD
    stripe = 2 * features // N_TP
    score_scale = 1.0 / math.sqrt(HD)

    def one_group(items):
        group_tokens, group_cache, group_len, group_requests, group_start = items
        inputs = group_tokens.astype(jnp.float32)
        inverse_rms = lax.rsqrt(lax.optimization_barrier(jnp.mean(inputs * inputs, axis=-1, keepdims=True)) + 1e-05)
        normed = (inputs * inverse_rms * norm_gain.astype(jnp.float32)).astype(jnp.bfloat16)
        projected = jnp.dot(normed, w_qkv.reshape(D, 3 * features), preferred_element_type=jnp.float32).reshape(C, 3, H, HD)
        row_index = jnp.arange(C, dtype=jnp.int32)
        request = row_index * group_requests // C
        first_row = (request * C + group_requests - 1) // group_requests
        positions = group_len + row_index - first_row
        cosine_table, sine_table = rope_tables(positions, HD)
        queries = rope_pair(projected[:, 0], cosine_table, sine_table).astype(jnp.bfloat16)
        new_keys = rope_pair(projected[:, 1], cosine_table, sine_table).astype(jnp.bfloat16).reshape(C, features)
        new_values = projected[:, 2].astype(jnp.bfloat16).reshape(C, features)
        cache_pos = jnp.arange(LMAX, dtype=jnp.int32)
        kept_cache = jnp.where((cache_pos < group_len)[None, :, None], group_cache, jnp.zeros((), jnp.bfloat16))
        padded = jnp.concatenate([kept_cache, jnp.zeros((2, C, features), jnp.bfloat16)], axis=1)
        zero_index = jnp.zeros((), jnp.int32)
        full_cache = lax.dynamic_update_slice(padded, jnp.stack([new_keys, new_values]), (zero_index, group_len.astype(jnp.int32), zero_index))
        key_heads = full_cache[0].reshape(CTX, H, HD)
        value_heads = full_cache[1].reshape(CTX, H, HD)
        scores = jnp.einsum('qhd,khd->hqk', queries.astype(jnp.float32), key_heads.astype(jnp.float32)) * score_scale
        key_pos = jnp.arange(CTX, dtype=jnp.int32)
        visible = visibility(group_len, group_requests, row_index, request, key_pos, C)
        masked = jnp.where(visible[None], scores, -1e+30)
        row_peak = lax.optimization_barrier(jnp.max(masked, axis=-1, keepdims=True))
        weights = jnp.exp(masked - row_peak)
        probabilities = (weights / lax.optimization_barrier(jnp.sum(weights, axis=-1, keepdims=True))).astype(jnp.bfloat16)
        mixed_rows = jnp.einsum('hqk,khd->qhd', probabilities.astype(jnp.float32), value_heads.astype(jnp.float32)).astype(jnp.bfloat16).reshape(C, features)
        layer_rows = (inputs + jnp.dot(mixed_rows, w_out, preferred_element_type=jnp.float32)).astype(jnp.bfloat16)
        blocks = full_cache.reshape(2, SLOTS, RANKS, BLK, features)
        order = (jnp.arange(RANKS, dtype=jnp.int32) - group_start) % RANKS
        rotated = jnp.take(blocks, order, axis=2)
        arranged = rotated.reshape(2, SLOTS, N_SEQ, 2, BLK, N_TP // 2, stripe)
        arranged = arranged.transpose(0, 2, 1, 4, 5, 3, 6).reshape(2, N_SEQ, SLOTS, BLK, 2 * features)
        return (layer_rows, arranged)
    stacked = (tokens.reshape(G, C, D), jnp.transpose(kv_cache, (1, 0, 2, 3)), cached_lengths, requests, block_start)
    layer_rows, arranged = lax.map(one_group, stacked)
    layer_out = layer_rows.reshape(TOKENS, D)
    decode_cache = jnp.transpose(arranged, (1, 2, 0, 3, 4, 5))
    return (layer_out, decode_cache)
```

```python
import math

import jax
import jax.numpy as jnp
from jax import lax
from jax.experimental import pallas as pl
from jax.experimental.pallas import tpu as pltpu
from jax.sharding import Mesh
from jax.sharding import PartitionSpec as P

HD = 96
BLK = 128
ROWS = 128


def rope_tables(positions, head_size):
    half_size = head_size // 2
    frequency = jnp.exp(
        jnp.arange(half_size, dtype=jnp.float32) * (-2.0 * math.log(10000.0) / head_size)
    )
    angles = positions.astype(jnp.float32)[:, None] * frequency[None, :]
    return (jnp.cos(angles), jnp.sin(angles))


def rope_pair(vectors, cosine_table, sine_table):
    half_size = vectors.shape[-1] // 2
    first_half = vectors[..., :half_size]
    second_half = vectors[..., half_size:]
    cos_wide = cosine_table[:, None, :]
    sin_wide = sine_table[:, None, :]
    return jnp.concatenate(
        [
            first_half * cos_wide - second_half * sin_wide,
            second_half * cos_wide + first_half * sin_wide,
        ],
        axis=-1,
    )


def request_of(index, group_requests, tok_count):
    scaled = index * group_requests
    if tok_count & (tok_count - 1) == 0:
        return lax.shift_right_logical(scaled, tok_count.bit_length() - 1)
    return scaled // tok_count


def attention_kernel(meta_ref, q_ref, kc_ref, vc_ref, kn_ref, vn_ref, o_ref):
    group_len = meta_ref[0]
    group_requests = meta_ref[1]
    rows = q_ref.shape[1]
    tok_count = kn_ref.shape[1]
    score_scale = 1.0 / math.sqrt(HD)
    dims = (((1,), (1,)), ((), ()))
    q = q_ref[0]
    s_old = lax.dot_general(q, kc_ref[0], dims, preferred_element_type=jnp.float32) * score_scale
    s_new = lax.dot_general(q, kn_ref[0], dims, preferred_element_type=jnp.float32) * score_scale
    col = lax.broadcasted_iota(jnp.int32, s_old.shape, 1)
    s_old = jnp.where(col < group_len, s_old, -1e30)
    row = pl.program_id(1) * rows + lax.broadcasted_iota(jnp.int32, s_new.shape, 0)
    key = lax.broadcasted_iota(jnp.int32, s_new.shape, 1)
    same = request_of(row, group_requests, tok_count) == request_of(key, group_requests, tok_count)
    s_new = jnp.where(same & (key <= row), s_new, -1e30)
    peak = jnp.maximum(
        jnp.max(s_old, axis=1, keepdims=True), jnp.max(s_new, axis=1, keepdims=True)
    )
    e_old = jnp.exp(s_old - peak)
    e_new = jnp.exp(s_new - peak)
    total = jnp.sum(e_old, axis=1, keepdims=True) + jnp.sum(e_new, axis=1, keepdims=True)
    p_old = (e_old / total).astype(jnp.bfloat16)
    p_new = (e_new / total).astype(jnp.bfloat16)
    out = jnp.dot(p_old, vc_ref[0], preferred_element_type=jnp.float32) + jnp.dot(
        p_new, vn_ref[0], preferred_element_type=jnp.float32
    )
    o_ref[0] = out.astype(jnp.bfloat16)


def attend(meta, queries, cache_k, cache_v, new_k, new_v):
    heads, tok_count, _ = queries.shape
    cache_len = cache_k.shape[1]
    q_spec = pl.BlockSpec((1, ROWS, HD), lambda h, r, m: (h, r, 0))
    c_spec = pl.BlockSpec((1, cache_len, HD), lambda h, r, m: (h, 0, 0))
    n_spec = pl.BlockSpec((1, tok_count, HD), lambda h, r, m: (h, 0, 0))
    return pl.pallas_call(
        attention_kernel,
        out_shape=jax.ShapeDtypeStruct(queries.shape, jnp.bfloat16),
        grid_spec=pltpu.PrefetchScalarGridSpec(
            num_scalar_prefetch=1,
            grid=(heads, tok_count // ROWS),
            in_specs=[q_spec, c_spec, c_spec, n_spec, n_spec],
            out_specs=q_spec,
        ),
    )(meta, queries, cache_k, cache_v, new_k, new_v)


def relay_kernel(meta_ref, cache_hbm, new_hbm, out_hbm, zero_buf, sems):
    len_blocks = meta_ref[0]
    group_start = meta_ref[1]
    rank_count = out_hbm.shape[0]
    new_blocks = new_hbm.shape[1] // BLK
    zero_buf[...] = jnp.zeros(zero_buf.shape, zero_buf.dtype)
    for rank in range(rank_count):
        block = (rank - group_start + rank_count) % rank_count
        target = out_hbm.at[rank]

        @pl.when(block < len_blocks)
        def _():
            start = pl.multiple_of(block * BLK, BLK)
            pltpu.make_async_copy(
                cache_hbm.at[:, pl.ds(start, BLK)], target, sems.at[rank]
            ).start()

        fresh = (block >= len_blocks) & (block < len_blocks + new_blocks)

        @pl.when(fresh)
        def _():
            start = pl.multiple_of((block - len_blocks) * BLK, BLK)
            pltpu.make_async_copy(
                new_hbm.at[:, pl.ds(start, BLK)], target, sems.at[rank]
            ).start()

        @pl.when(block >= len_blocks + new_blocks)
        def _():
            pltpu.make_async_copy(zero_buf, target, sems.at[rank]).start()

    for rank in range(rank_count):
        pltpu.make_async_copy(zero_buf, out_hbm.at[rank], sems.at[rank]).wait()


def relay(meta, cache, new_kv, rank_count):
    _, _, features = cache.shape
    return pl.pallas_call(
        relay_kernel,
        out_shape=jax.ShapeDtypeStruct((rank_count, 2, BLK, features), jnp.bfloat16),
        grid_spec=pltpu.PrefetchScalarGridSpec(
            num_scalar_prefetch=1,
            grid=(),
            in_specs=[pl.BlockSpec(memory_space=pl.ANY), pl.BlockSpec(memory_space=pl.ANY)],
            out_specs=pl.BlockSpec(memory_space=pl.ANY),
            scratch_shapes=[
                pltpu.VMEM((2, BLK, features), jnp.bfloat16),
                pltpu.SemaphoreType.DMA((rank_count,)),
            ],
        ),
    )(meta, cache, new_kv)


def head_major(values, head_count):
    rows = values.shape[0]
    return values.reshape(rows, head_count, HD).transpose(1, 0, 2)


def local(tokens, norm_gain, w_qkv, w_out, kv_cache, cached_lengths, requests, block_start):
    group_idx = lax.axis_index("seq")
    tp_rank = lax.axis_index(("x", "core"))
    tp_count = lax.axis_size(("x", "core"))
    seq_count = lax.axis_size("seq")
    tok_count, model_width = tokens.shape
    features = w_qkv.shape[2]
    head_count = features // HD
    cache_len = kv_cache.shape[2]
    group_len = lax.dynamic_index_in_dim(cached_lengths, group_idx, keepdims=False)
    group_requests = lax.dynamic_index_in_dim(requests, group_idx, keepdims=False)
    group_start = lax.dynamic_index_in_dim(block_start, group_idx, keepdims=False)
    inputs = tokens.astype(jnp.float32)
    inverse_rms = lax.rsqrt(jnp.mean(inputs * inputs, axis=-1, keepdims=True) + 1e-05)
    normed = (inputs * inverse_rms * norm_gain.astype(jnp.float32)).astype(jnp.bfloat16)

    def project(part):
        return jnp.dot(normed, w_qkv[:, part, :], preferred_element_type=jnp.float32)

    row_index = jnp.arange(tok_count, dtype=jnp.int32)
    request = row_index * group_requests // tok_count
    first_row = (request * tok_count + group_requests - 1) // group_requests
    positions = group_len + row_index - first_row
    cosine_table, sine_table = rope_tables(positions, HD)

    def rotate(projected):
        heads = projected.reshape(tok_count, head_count, HD)
        return rope_pair(heads, cosine_table, sine_table).astype(jnp.bfloat16)

    new_keys = rotate(project(1)).reshape(tok_count, features)
    new_values = project(2).astype(jnp.bfloat16)
    cache = kv_cache[:, 0]
    relay_meta = jnp.stack([group_len // BLK, group_start]).astype(jnp.int32)
    rank_count = 2 * seq_count
    send = relay(relay_meta, cache, jnp.stack([new_keys, new_values]), rank_count)
    received = lax.all_to_all(send, ("seq", "core"), 0, 0, tiled=True)
    received = received.reshape(seq_count, 2, 2, BLK, features).transpose(2, 0, 3, 1, 4)
    decode_cache = received.reshape(2, 1, seq_count, 1, BLK, 2 * features)

    queries = rotate(project(0)).transpose(1, 0, 2)
    attn_meta = jnp.stack([group_len, group_requests]).astype(jnp.int32)
    cache_heads = kv_cache.reshape(2, cache_len, head_count, HD).transpose(0, 2, 1, 3)
    attended = attend(
        attn_meta,
        queries,
        cache_heads[0],
        cache_heads[1],
        head_major(new_keys, head_count),
        head_major(new_values, head_count),
    )
    attended = attended.transpose(1, 0, 2).reshape(tok_count, features)
    rows_dev = tok_count // tp_count
    partial = jnp.dot(attended, w_out, preferred_element_type=jnp.float32).astype(jnp.bfloat16)
    summed = lax.dynamic_slice_in_dim(partial, tp_rank * rows_dev, rows_dev, 0).astype(jnp.float32)
    for shift in range(1, tp_count):
        target = (tp_rank + shift) % tp_count
        chunk = lax.dynamic_slice_in_dim(partial, target * rows_dev, rows_dev, 0)
        pairs = [(source, (source + shift) % tp_count) for source in range(tp_count)]
        summed = summed + lax.ppermute(chunk, ("x", "core"), pairs).astype(jnp.float32)
    own_rows = lax.dynamic_slice_in_dim(inputs, tp_rank * rows_dev, rows_dev, 0)
    layer_out = (own_rows + summed).astype(jnp.bfloat16)
    return (layer_out, decode_cache)


def solution(mesh):
    seq_count, tp_count = mesh.devices.shape
    split = Mesh(mesh.devices.reshape(seq_count, tp_count // 2, 2), ("seq", "x", "core"))
    tp = ("x", "core")
    placed = (
        P("seq", None),
        P(),
        P(None, None, tp),
        P(tp, None),
        P(None, "seq", None, tp),
        P(),
        P(),
        P(),
    )
    return jax.shard_map(
        local,
        mesh=split,
        in_specs=placed,
        out_specs=(P(("seq",) + tp, None), P(None, "seq", None, None, None, tp)),
        check_vma=False,
    )
```

```python
import math

import jax
import jax.numpy as jnp
from jax import lax
from jax.experimental import pallas as pl
from jax.experimental.pallas import tpu as pltpu
from jax.sharding import Mesh
from jax.sharding import PartitionSpec as P

HD = 96
BLK = 128
ROWS = 128


def rope_tables(positions, head_size):
    half_size = head_size // 2
    frequency = jnp.exp(
        jnp.arange(half_size, dtype=jnp.float32) * (-2.0 * math.log(10000.0) / head_size)
    )
    angles = positions.astype(jnp.float32)[:, None] * frequency[None, :]
    return (jnp.cos(angles), jnp.sin(angles))


def rope_pair(vectors, cosine_table, sine_table):
    half_size = vectors.shape[-1] // 2
    first_half = vectors[..., :half_size]
    second_half = vectors[..., half_size:]
    cos_wide = cosine_table[:, None, :]
    sin_wide = sine_table[:, None, :]
    return jnp.concatenate(
        [
            first_half * cos_wide - second_half * sin_wide,
            second_half * cos_wide + first_half * sin_wide,
        ],
        axis=-1,
    )


def request_of(index, group_requests, tok_count):
    scaled = index * group_requests
    if tok_count & (tok_count - 1) == 0:
        return lax.shift_right_logical(scaled, tok_count.bit_length() - 1)
    return scaled // tok_count


def head_picker(features, head):
    rows = lax.broadcasted_iota(jnp.int32, (features, HD), 0)
    cols = lax.broadcasted_iota(jnp.int32, (features, HD), 1)
    return (rows == cols + head * HD).astype(jnp.bfloat16)


def attention_kernel(
    meta_ref, q_ref, kc_ref, vc_ref, kn_ref, vn_ref, o_ref, kh_buf, vh_buf, qh_buf, acc_ref
):
    group_len = meta_ref[0]
    group_requests = meta_ref[1]
    head = pl.program_id(0)
    tok_count, features = q_ref.shape
    score_scale = 1.0 / math.sqrt(HD)
    picker = head_picker(features, head)

    def pick(values):
        return jnp.dot(values, picker, preferred_element_type=jnp.float32).astype(jnp.bfloat16)

    kh_buf[...] = pick(kc_ref[0, 0])
    vh_buf[...] = pick(vc_ref[0, 0])
    qh_buf[...] = pick(q_ref[...])
    kn = pick(kn_ref[0])
    vn = pick(vn_ref[0])
    dims = (((1,), (1,)), ((), ()))
    for chunk in range(tok_count // ROWS):
        rows = pl.ds(chunk * ROWS, ROWS)
        q = qh_buf[rows, :]
        s_old = lax.dot_general(q, kh_buf[...], dims, preferred_element_type=jnp.float32)
        s_new = lax.dot_general(q, kn, dims, preferred_element_type=jnp.float32)
        s_old = s_old * score_scale
        s_new = s_new * score_scale
        col = lax.broadcasted_iota(jnp.int32, s_old.shape, 1)
        s_old = jnp.where(col < group_len, s_old, -1e30)
        row = chunk * ROWS + lax.broadcasted_iota(jnp.int32, s_new.shape, 0)
        key = lax.broadcasted_iota(jnp.int32, s_new.shape, 1)
        same = request_of(row, group_requests, tok_count) == request_of(
            key, group_requests, tok_count
        )
        s_new = jnp.where(same & (key <= row), s_new, -1e30)
        peak = jnp.maximum(
            jnp.max(s_old, axis=1, keepdims=True), jnp.max(s_new, axis=1, keepdims=True)
        )
        e_old = jnp.exp(s_old - peak)
        e_new = jnp.exp(s_new - peak)
        total = jnp.sum(e_old, axis=1, keepdims=True) + jnp.sum(e_new, axis=1, keepdims=True)
        p_old = (e_old / total).astype(jnp.bfloat16)
        p_new = (e_new / total).astype(jnp.bfloat16)
        out = jnp.dot(p_old, vh_buf[...], preferred_element_type=jnp.float32) + jnp.dot(
            p_new, vn, preferred_element_type=jnp.float32
        )
        placed = lax.dot_general(
            out.astype(jnp.bfloat16), picker, dims, preferred_element_type=jnp.float32
        )

        @pl.when(head == 0)
        def _():
            acc_ref[rows, :] = placed

        @pl.when(head > 0)
        def _():
            acc_ref[rows, :] = acc_ref[rows, :] + placed

    @pl.when(head == pl.num_programs(0) - 1)
    def _():
        o_ref[...] = acc_ref[...].astype(jnp.bfloat16)


def attend(meta, queries, kv_cache, new_kv):
    tok_count, features = queries.shape
    cache_len = kv_cache.shape[2]
    full_q = pl.BlockSpec((tok_count, features), lambda h, m: (0, 0))
    cache_k = pl.BlockSpec((1, 1, cache_len, features), lambda h, m: (0, 0, 0, 0))
    cache_v = pl.BlockSpec((1, 1, cache_len, features), lambda h, m: (1, 0, 0, 0))
    new_k = pl.BlockSpec((1, tok_count, features), lambda h, m: (0, 0, 0))
    new_v = pl.BlockSpec((1, tok_count, features), lambda h, m: (1, 0, 0))
    return pl.pallas_call(
        attention_kernel,
        out_shape=jax.ShapeDtypeStruct(queries.shape, jnp.bfloat16),
        grid_spec=pltpu.PrefetchScalarGridSpec(
            num_scalar_prefetch=1,
            grid=(features // HD,),
            in_specs=[full_q, cache_k, cache_v, new_k, new_v],
            out_specs=full_q,
            scratch_shapes=[
                pltpu.VMEM((cache_len, HD), jnp.bfloat16),
                pltpu.VMEM((cache_len, HD), jnp.bfloat16),
                pltpu.VMEM((tok_count, HD), jnp.bfloat16),
                pltpu.VMEM((tok_count, features), jnp.float32),
            ],
        ),
    )(meta, queries, kv_cache, kv_cache, new_kv, new_kv)


def relay_kernel(meta_ref, cache_ref, new_ref, out_ref):
    len_blocks = meta_ref[0]
    group_start = meta_ref[1]
    core = meta_ref[2]
    part = pl.program_id(0)
    dest = pl.program_id(1)
    rank_count = 2 * pl.num_programs(1)
    new_blocks = meta_ref[3]
    block = (2 * dest + (core + part) % 2 - group_start + rank_count) % rank_count
    old = block < len_blocks
    fresh = (block >= len_blocks) & (block < len_blocks + new_blocks)
    zero = jnp.zeros(new_ref.shape[1:], new_ref.dtype)
    for kv in range(2):
        out_ref[0, kv, 0] = jnp.where(
            old, cache_ref[kv, 0], jnp.where(fresh, new_ref[kv], zero)
        )


def relay(meta, kv_cache, new_kv, seq_count):
    features = kv_cache.shape[3]
    new_blocks = new_kv.shape[1] // BLK

    def block_of(p, d, m):
        rank_count = 2 * seq_count
        return (2 * d + (m[2] + p) % 2 - m[1] + rank_count) % rank_count

    def cache_map(p, d, m):
        return (0, 0, jnp.clip(block_of(p, d, m), 0, m[0] - 1), 0)

    def new_map(p, d, m):
        return (0, jnp.clip(block_of(p, d, m) - m[0], 0, new_blocks - 1), 0)

    return pl.pallas_call(
        relay_kernel,
        out_shape=jax.ShapeDtypeStruct((2, 2, seq_count, BLK, features), jnp.bfloat16),
        grid_spec=pltpu.PrefetchScalarGridSpec(
            num_scalar_prefetch=1,
            grid=(2, seq_count),
            in_specs=[
                pl.BlockSpec((2, 1, BLK, features), cache_map),
                pl.BlockSpec((2, BLK, features), new_map),
            ],
            out_specs=pl.BlockSpec((1, 2, 1, BLK, features), lambda p, d, m: (p, 0, d, 0, 0)),
        ),
    )(meta, kv_cache, new_kv)


def local(tokens, norm_gain, w_qkv, w_out, kv_cache, cached_lengths, requests, block_start):
    group_idx = lax.axis_index("seq")
    tp_rank = lax.axis_index(("x", "core"))
    tp_count = lax.axis_size(("x", "core"))
    seq_count = lax.axis_size("seq")
    tok_count, model_width = tokens.shape
    features = w_qkv.shape[2]
    head_count = features // HD
    cache_len = kv_cache.shape[2]
    group_len = lax.dynamic_index_in_dim(cached_lengths, group_idx, keepdims=False)
    group_requests = lax.dynamic_index_in_dim(requests, group_idx, keepdims=False)
    group_start = lax.dynamic_index_in_dim(block_start, group_idx, keepdims=False)
    inputs = tokens.astype(jnp.float32)
    inverse_rms = lax.rsqrt(jnp.mean(inputs * inputs, axis=-1, keepdims=True) + 1e-05)
    normed = (inputs * inverse_rms * norm_gain.astype(jnp.float32)).astype(jnp.bfloat16)

    def project(part):
        return jnp.dot(normed, w_qkv[:, part, :], preferred_element_type=jnp.float32)

    row_index = jnp.arange(tok_count, dtype=jnp.int32)
    request = row_index * group_requests // tok_count
    first_row = (request * tok_count + group_requests - 1) // group_requests
    positions = group_len + row_index - first_row
    cosine_table, sine_table = rope_tables(positions, HD)

    def rotate(projected):
        heads = projected.reshape(tok_count, head_count, HD)
        return rope_pair(heads, cosine_table, sine_table).astype(jnp.bfloat16)

    new_keys = rotate(project(1)).reshape(tok_count, features)
    new_values = project(2).astype(jnp.bfloat16)
    new_kv = jnp.stack([new_keys, new_values])
    core = lax.axis_index("core")
    relay_meta = jnp.stack(
        [group_len // BLK, group_start, core, jnp.int32(tok_count // BLK)]
    ).astype(jnp.int32)
    parts = relay(relay_meta, kv_cache, new_kv, seq_count)
    partner = lax.ppermute(parts[1], "core", [(0, 1), (1, 0)])
    lower = jnp.where(core == 0, parts[0], partner)
    upper = jnp.where(core == 0, partner, parts[0])
    joined = jnp.concatenate([lower, upper], axis=-1)
    queries = rotate(project(0)).reshape(tok_count, features)
    joined, queries = lax.optimization_barrier((joined, queries))
    received = lax.all_to_all(joined, "seq", 1, 1, tiled=True)
    decode_cache = received.reshape(2, 1, seq_count, 1, BLK, 2 * features)

    attn_meta = jnp.stack([group_len, group_requests]).astype(jnp.int32)
    attended = attend(attn_meta, queries, kv_cache, new_kv)
    received, attended = lax.optimization_barrier((received, attended))
    rows_dev = tok_count // tp_count
    partial = jnp.dot(attended, w_out, preferred_element_type=jnp.float32).astype(jnp.bfloat16)
    partial = partial.reshape(tp_count, rows_dev, model_width)
    gathered = lax.all_to_all(partial, ("x", "core"), 0, 0, tiled=True)
    summed = jnp.sum(gathered.astype(jnp.float32), axis=0)
    own_rows = lax.dynamic_slice_in_dim(inputs, tp_rank * rows_dev, rows_dev, 0)
    layer_out = (own_rows + summed).astype(jnp.bfloat16)
    return (layer_out, decode_cache)


def solution(mesh):
    seq_count, tp_count = mesh.devices.shape
    split = Mesh(mesh.devices.reshape(seq_count, tp_count // 2, 2), ("seq", "x", "core"))
    tp = ("x", "core")
    placed = (
        P("seq", None),
        P(),
        P(None, None, tp),
        P(tp, None),
        P(None, "seq", None, tp),
        P(),
        P(),
        P(),
    )
    return jax.shard_map(
        local,
        mesh=split,
        in_specs=placed,
        out_specs=(P(("seq",) + tp, None), P(None, "seq", None, None, None, tp)),
        check_vma=False,
    )
```

```python
import math

import jax
import jax.numpy as jnp
from jax import lax
from jax.experimental import pallas as pl
from jax.experimental.pallas import tpu as pltpu
from jax.sharding import Mesh
from jax.sharding import PartitionSpec as P

HD = 96
BLK = 128
ROWS = 128


def rope_tables(positions, head_size):
    half_size = head_size // 2
    frequency = jnp.exp(
        jnp.arange(half_size, dtype=jnp.float32) * (-2.0 * math.log(10000.0) / head_size)
    )
    angles = positions.astype(jnp.float32)[:, None] * frequency[None, :]
    return (jnp.cos(angles), jnp.sin(angles))


def rope_pair(vectors, cosine_table, sine_table):
    half_size = vectors.shape[-1] // 2
    first_half = vectors[..., :half_size]
    second_half = vectors[..., half_size:]
    cos_wide = cosine_table[:, None, :]
    sin_wide = sine_table[:, None, :]
    return jnp.concatenate(
        [
            first_half * cos_wide - second_half * sin_wide,
            second_half * cos_wide + first_half * sin_wide,
        ],
        axis=-1,
    )


def request_of(index, group_requests, tok_count):
    scaled = index * group_requests
    if tok_count & (tok_count - 1) == 0:
        return lax.shift_right_logical(scaled, tok_count.bit_length() - 1)
    return scaled // tok_count


def head_picker(features, head):
    rows = lax.broadcasted_iota(jnp.int32, (features, HD), 0)
    cols = lax.broadcasted_iota(jnp.int32, (features, HD), 1)
    return (rows == cols + head * HD).astype(jnp.bfloat16)


def attention_kernel(
    meta_ref, q_ref, kc_ref, vc_ref, kn_ref, vn_ref, o_ref, kh_buf, vh_buf, qh_buf, acc_ref
):
    group_len = meta_ref[0]
    group_requests = meta_ref[1]
    head = pl.program_id(0)
    tok_count, features = q_ref.shape
    score_scale = 1.0 / math.sqrt(HD)
    picker = head_picker(features, head)

    def pick(values):
        return jnp.dot(values, picker, preferred_element_type=jnp.float32).astype(jnp.bfloat16)

    kh_buf[...] = pick(kc_ref[0, 0])
    vh_buf[...] = pick(vc_ref[0, 0])
    qh_buf[...] = pick(q_ref[...])
    kn = pick(kn_ref[0])
    vn = pick(vn_ref[0])
    dims = (((1,), (1,)), ((), ()))
    for chunk in range(tok_count // ROWS):
        rows = pl.ds(chunk * ROWS, ROWS)
        q = qh_buf[rows, :]
        s_old = lax.dot_general(q, kh_buf[...], dims, preferred_element_type=jnp.float32)
        s_new = lax.dot_general(q, kn, dims, preferred_element_type=jnp.float32)
        s_old = s_old * score_scale
        s_new = s_new * score_scale
        col = lax.broadcasted_iota(jnp.int32, s_old.shape, 1)
        s_old = jnp.where(col < group_len, s_old, -1e30)
        row = chunk * ROWS + lax.broadcasted_iota(jnp.int32, s_new.shape, 0)
        key = lax.broadcasted_iota(jnp.int32, s_new.shape, 1)
        same = request_of(row, group_requests, tok_count) == request_of(
            key, group_requests, tok_count
        )
        s_new = jnp.where(same & (key <= row), s_new, -1e30)
        peak = jnp.maximum(
            jnp.max(s_old, axis=1, keepdims=True), jnp.max(s_new, axis=1, keepdims=True)
        )
        e_old = jnp.exp(s_old - peak)
        e_new = jnp.exp(s_new - peak)
        total = jnp.sum(e_old, axis=1, keepdims=True) + jnp.sum(e_new, axis=1, keepdims=True)
        p_old = (e_old / total).astype(jnp.bfloat16)
        p_new = (e_new / total).astype(jnp.bfloat16)
        out = jnp.dot(p_old, vh_buf[...], preferred_element_type=jnp.float32) + jnp.dot(
            p_new, vn, preferred_element_type=jnp.float32
        )
        placed = lax.dot_general(
            out.astype(jnp.bfloat16), picker, dims, preferred_element_type=jnp.float32
        )

        @pl.when(head == 0)
        def _():
            acc_ref[rows, :] = placed

        @pl.when(head > 0)
        def _():
            acc_ref[rows, :] = acc_ref[rows, :] + placed

    @pl.when(head == pl.num_programs(0) - 1)
    def _():
        o_ref[...] = acc_ref[...].astype(jnp.bfloat16)


def attend(meta, queries, kv_cache, new_kv):
    tok_count, features = queries.shape
    cache_len = kv_cache.shape[2]
    full_q = pl.BlockSpec((tok_count, features), lambda h, m: (0, 0))
    cache_k = pl.BlockSpec((1, 1, cache_len, features), lambda h, m: (0, 0, 0, 0))
    cache_v = pl.BlockSpec((1, 1, cache_len, features), lambda h, m: (1, 0, 0, 0))
    new_k = pl.BlockSpec((1, tok_count, features), lambda h, m: (0, 0, 0))
    new_v = pl.BlockSpec((1, tok_count, features), lambda h, m: (1, 0, 0))
    return pl.pallas_call(
        attention_kernel,
        out_shape=jax.ShapeDtypeStruct(queries.shape, jnp.bfloat16),
        grid_spec=pltpu.PrefetchScalarGridSpec(
            num_scalar_prefetch=1,
            grid=(features // HD,),
            in_specs=[full_q, cache_k, cache_v, new_k, new_v],
            out_specs=full_q,
            scratch_shapes=[
                pltpu.VMEM((cache_len, HD), jnp.bfloat16),
                pltpu.VMEM((cache_len, HD), jnp.bfloat16),
                pltpu.VMEM((tok_count, HD), jnp.bfloat16),
                pltpu.VMEM((tok_count, features), jnp.float32),
            ],
        ),
    )(meta, queries, kv_cache, kv_cache, new_kv, new_kv)


def relay_kernel(meta_ref, own_c, own_n, other_c, other_n, own_ref, other_ref):
    len_blocks = meta_ref[0]
    group_start = meta_ref[1]
    core = meta_ref[2]
    new_blocks = meta_ref[3]
    dest = pl.program_id(0)
    rank_count = 2 * pl.num_programs(0)
    zero = jnp.zeros(own_n.shape[1:], own_n.dtype)
    for part, cache_ref, new_ref, out_ref in ((0, own_c, own_n, own_ref), (1, other_c, other_n, other_ref)):
        block = (2 * dest + (core + part) % 2 - group_start + rank_count) % rank_count
        old = block < len_blocks
        fresh = (block >= len_blocks) & (block < len_blocks + new_blocks)
        for kv in range(2):
            out_ref[0, kv] = jnp.where(
                old, cache_ref[kv, 0], jnp.where(fresh, new_ref[kv], zero)
            )


def relay(meta, kv_cache, new_kv, seq_count):
    features = kv_cache.shape[3]
    new_blocks = new_kv.shape[1] // BLK
    rank_count = 2 * seq_count

    def block_of(part, d, m):
        return (2 * d + (m[2] + part) % 2 - m[1] + rank_count) % rank_count

    def cache_spec(part):
        return pl.BlockSpec(
            (2, 1, BLK, features),
            lambda d, m: (0, 0, jnp.clip(block_of(part, d, m), 0, m[0] - 1), 0),
        )

    def new_spec(part):
        return pl.BlockSpec(
            (2, BLK, features),
            lambda d, m: (0, jnp.clip(block_of(part, d, m) - m[0], 0, new_blocks - 1), 0),
        )

    return pl.pallas_call(
        relay_kernel,
        out_shape=(
            jax.ShapeDtypeStruct((seq_count, 2, BLK, 2 * features), jnp.bfloat16),
            jax.ShapeDtypeStruct((seq_count, 2, BLK, features), jnp.bfloat16),
        ),
        grid_spec=pltpu.PrefetchScalarGridSpec(
            num_scalar_prefetch=1,
            grid=(seq_count,),
            in_specs=[cache_spec(0), new_spec(0), cache_spec(1), new_spec(1)],
            out_specs=(
                pl.BlockSpec((1, 2, BLK, features), lambda d, m: (d, 0, 0, m[2])),
                pl.BlockSpec((1, 2, BLK, features), lambda d, m: (d, 0, 0, 0)),
            ),
        ),
    )(meta, kv_cache, new_kv, kv_cache, new_kv)


def projection_kernel(x_ref, w_ref, o_ref):
    o_ref[0] = jnp.dot(x_ref[...], w_ref[0], preferred_element_type=jnp.float32)


def project_all(normed, weights):
    parts, width, features = weights.shape
    rows = normed.shape[0]
    return pl.pallas_call(
        projection_kernel,
        out_shape=jax.ShapeDtypeStruct((parts, rows, features), jnp.float32),
        grid=(parts,),
        in_specs=[
            pl.BlockSpec((rows, width), lambda k: (0, 0)),
            pl.BlockSpec((1, width, features), lambda k: (k, 0, 0)),
        ],
        out_specs=pl.BlockSpec((1, rows, features), lambda k: (k, 0, 0)),
    )(normed, weights)


def local(tokens, norm_gain, w_qkv, w_out, kv_cache, cached_lengths, requests, block_start):
    group_idx = lax.axis_index("seq")
    tp_rank = lax.axis_index(("x", "core"))
    tp_count = lax.axis_size(("x", "core"))
    seq_count = lax.axis_size("seq")
    tok_count, model_width = tokens.shape
    features = w_qkv.shape[2]
    head_count = features // HD
    cache_len = kv_cache.shape[2]
    group_len = lax.dynamic_index_in_dim(cached_lengths, group_idx, keepdims=False)
    group_requests = lax.dynamic_index_in_dim(requests, group_idx, keepdims=False)
    group_start = lax.dynamic_index_in_dim(block_start, group_idx, keepdims=False)
    inputs = tokens.astype(jnp.float32)
    inverse_rms = lax.rsqrt(jnp.mean(inputs * inputs, axis=-1, keepdims=True) + 1e-05)
    normed = (inputs * inverse_rms * norm_gain.astype(jnp.float32)).astype(jnp.bfloat16)

    projected = project_all(normed, jnp.transpose(w_qkv, (1, 0, 2)))

    def project(part):
        return projected[part]

    row_index = jnp.arange(tok_count, dtype=jnp.int32)
    request = row_index * group_requests // tok_count
    first_row = (request * tok_count + group_requests - 1) // group_requests
    positions = group_len + row_index - first_row
    cosine_table, sine_table = rope_tables(positions, HD)

    def rotate(projected):
        heads = projected.reshape(tok_count, head_count, HD)
        return rope_pair(heads, cosine_table, sine_table).astype(jnp.bfloat16)

    new_keys = rotate(project(1)).reshape(tok_count, features)
    new_values = project(2).astype(jnp.bfloat16)
    new_kv = jnp.stack([new_keys, new_values])
    core = lax.axis_index("core")
    relay_meta = jnp.stack(
        [group_len // BLK, group_start, core, jnp.int32(tok_count // BLK)]
    ).astype(jnp.int32)
    own, other = relay(relay_meta, kv_cache, new_kv, seq_count)
    partner = lax.ppermute(other, "core", [(0, 1), (1, 0)])
    zero_index = jnp.zeros((), jnp.int32)
    joined = lax.dynamic_update_slice(
        own, partner, (zero_index, zero_index, zero_index, (1 - core) * features)
    )
    queries = rotate(project(0)).reshape(tok_count, features)
    joined, queries = lax.optimization_barrier((joined, queries))
    received = lax.all_to_all(joined, "seq", 0, 0, tiled=True)
    decode_cache = received.transpose(1, 0, 2, 3).reshape(2, 1, seq_count, 1, BLK, 2 * features)

    attn_meta = jnp.stack([group_len, group_requests]).astype(jnp.int32)
    attended = attend(attn_meta, queries, kv_cache, new_kv)
    rows_dev = tok_count // tp_count
    partial = jnp.dot(attended, w_out, preferred_element_type=jnp.float32).astype(jnp.bfloat16)
    summed = lax.dynamic_slice_in_dim(partial, tp_rank * rows_dev, rows_dev, 0).astype(jnp.float32)
    for shift in range(1, tp_count):
        target = (tp_rank + shift) % tp_count
        chunk = lax.dynamic_slice_in_dim(partial, target * rows_dev, rows_dev, 0)
        pairs = [(source, (source + shift) % tp_count) for source in range(tp_count)]
        summed = summed + lax.ppermute(chunk, ("x", "core"), pairs).astype(jnp.float32)
    own_rows = lax.dynamic_slice_in_dim(inputs, tp_rank * rows_dev, rows_dev, 0)
    layer_out = (own_rows + summed).astype(jnp.bfloat16)
    return (layer_out, decode_cache)


def solution(mesh):
    seq_count, tp_count = mesh.devices.shape
    split = Mesh(mesh.devices.reshape(seq_count, tp_count // 2, 2), ("seq", "x", "core"))
    tp = ("x", "core")
    placed = (
        P("seq", None),
        P(),
        P(None, None, tp),
        P(tp, None),
        P(None, "seq", None, tp),
        P(),
        P(),
        P(),
    )
    return jax.shard_map(
        local,
        mesh=split,
        in_specs=placed,
        out_specs=(P(("seq",) + tp, None), P(None, "seq", None, None, None, tp)),
        check_vma=False,
    )
```

```python
import math

import jax
import jax.numpy as jnp
from jax import lax
from jax.experimental import pallas as pl
from jax.experimental.pallas import tpu as pltpu
from jax.sharding import Mesh
from jax.sharding import PartitionSpec as P

HD = 96
BLK = 128
ROWS = 128


def rope_tables(positions, head_size):
    half_size = head_size // 2
    frequency = jnp.exp(
        jnp.arange(half_size, dtype=jnp.float32) * (-2.0 * math.log(10000.0) / head_size)
    )
    angles = positions.astype(jnp.float32)[:, None] * frequency[None, :]
    return (jnp.cos(angles), jnp.sin(angles))


def rope_pair(vectors, cosine_table, sine_table):
    half_size = vectors.shape[-1] // 2
    first_half = vectors[..., :half_size]
    second_half = vectors[..., half_size:]
    cos_wide = cosine_table[:, None, :]
    sin_wide = sine_table[:, None, :]
    return jnp.concatenate(
        [
            first_half * cos_wide - second_half * sin_wide,
            second_half * cos_wide + first_half * sin_wide,
        ],
        axis=-1,
    )


def request_of(index, group_requests, tok_count):
    scaled = index * group_requests
    if tok_count & (tok_count - 1) == 0:
        return lax.shift_right_logical(scaled, tok_count.bit_length() - 1)
    return scaled // tok_count


def head_picker(features, head):
    rows = lax.broadcasted_iota(jnp.int32, (features, HD), 0)
    cols = lax.broadcasted_iota(jnp.int32, (features, HD), 1)
    return (rows == cols + head * HD).astype(jnp.bfloat16)


def attention_kernel(
    meta_ref, q_ref, kc_ref, vc_ref, kn_ref, vn_ref, o_ref, kh_buf, vh_buf, qh_buf, acc_ref
):
    group_len = meta_ref[0]
    group_requests = meta_ref[1]
    head = pl.program_id(0)
    tok_count, features = q_ref.shape
    score_scale = 1.0 / math.sqrt(HD)
    picker = head_picker(features, head)

    def pick(values):
        return jnp.dot(values, picker, preferred_element_type=jnp.float32).astype(jnp.bfloat16)

    kh_buf[...] = pick(kc_ref[0, 0])
    vh_buf[...] = pick(vc_ref[0, 0])
    qh_buf[...] = pick(q_ref[...])
    kn = pick(kn_ref[0])
    vn = pick(vn_ref[0])
    dims = (((1,), (1,)), ((), ()))
    for chunk in range(tok_count // ROWS):
        rows = pl.ds(chunk * ROWS, ROWS)
        q = qh_buf[rows, :]
        s_old = lax.dot_general(q, kh_buf[...], dims, preferred_element_type=jnp.float32)
        s_new = lax.dot_general(q, kn, dims, preferred_element_type=jnp.float32)
        s_old = s_old * score_scale
        s_new = s_new * score_scale
        col = lax.broadcasted_iota(jnp.int32, s_old.shape, 1)
        s_old = jnp.where(col < group_len, s_old, -1e30)
        row = chunk * ROWS + lax.broadcasted_iota(jnp.int32, s_new.shape, 0)
        key = lax.broadcasted_iota(jnp.int32, s_new.shape, 1)
        same = request_of(row, group_requests, tok_count) == request_of(
            key, group_requests, tok_count
        )
        s_new = jnp.where(same & (key <= row), s_new, -1e30)
        peak = jnp.maximum(
            jnp.max(s_old, axis=1, keepdims=True), jnp.max(s_new, axis=1, keepdims=True)
        )
        e_old = jnp.exp(s_old - peak)
        e_new = jnp.exp(s_new - peak)
        total = jnp.sum(e_old, axis=1, keepdims=True) + jnp.sum(e_new, axis=1, keepdims=True)
        p_old = (e_old / total).astype(jnp.bfloat16)
        p_new = (e_new / total).astype(jnp.bfloat16)
        out = jnp.dot(p_old, vh_buf[...], preferred_element_type=jnp.float32) + jnp.dot(
            p_new, vn, preferred_element_type=jnp.float32
        )
        placed = lax.dot_general(
            out.astype(jnp.bfloat16), picker, dims, preferred_element_type=jnp.float32
        )

        @pl.when(head == 0)
        def _():
            acc_ref[rows, :] = placed

        @pl.when(head > 0)
        def _():
            acc_ref[rows, :] = acc_ref[rows, :] + placed

    @pl.when(head == pl.num_programs(0) - 1)
    def _():
        o_ref[...] = acc_ref[...].astype(jnp.bfloat16)


def attend(meta, queries, kv_cache, new_kv):
    tok_count, features = queries.shape
    cache_len = kv_cache.shape[2]
    full_q = pl.BlockSpec((tok_count, features), lambda h, m: (0, 0))
    cache_k = pl.BlockSpec((1, 1, cache_len, features), lambda h, m: (0, 0, 0, 0))
    cache_v = pl.BlockSpec((1, 1, cache_len, features), lambda h, m: (1, 0, 0, 0))
    new_k = pl.BlockSpec((1, tok_count, features), lambda h, m: (0, 0, 0))
    new_v = pl.BlockSpec((1, tok_count, features), lambda h, m: (1, 0, 0))
    return pl.pallas_call(
        attention_kernel,
        out_shape=jax.ShapeDtypeStruct(queries.shape, jnp.bfloat16),
        grid_spec=pltpu.PrefetchScalarGridSpec(
            num_scalar_prefetch=1,
            grid=(features // HD,),
            in_specs=[full_q, cache_k, cache_v, new_k, new_v],
            out_specs=full_q,
            scratch_shapes=[
                pltpu.VMEM((cache_len, HD), jnp.bfloat16),
                pltpu.VMEM((cache_len, HD), jnp.bfloat16),
                pltpu.VMEM((tok_count, HD), jnp.bfloat16),
                pltpu.VMEM((tok_count, features), jnp.float32),
            ],
        ),
    )(meta, queries, kv_cache, kv_cache, new_kv, new_kv)


def relay_kernel(meta_ref, own_c, own_n, other_c, other_n, own_ref, other_ref):
    len_blocks = meta_ref[0]
    group_start = meta_ref[1]
    core = meta_ref[2]
    new_blocks = meta_ref[3]
    dest = pl.program_id(0)
    rank_count = 2 * pl.num_programs(0)
    zero = jnp.zeros(own_n.shape[1:], own_n.dtype)
    for part, cache_ref, new_ref, out_ref in ((0, own_c, own_n, own_ref), (1, other_c, other_n, other_ref)):
        block = (2 * dest + (core + part) % 2 - group_start + rank_count) % rank_count
        old = block < len_blocks
        fresh = (block >= len_blocks) & (block < len_blocks + new_blocks)
        for kv in range(2):
            out_ref[0, kv] = jnp.where(
                old, cache_ref[kv, 0], jnp.where(fresh, new_ref[kv], zero)
            )


def relay(meta, kv_cache, new_kv, seq_count):
    features = kv_cache.shape[3]
    new_blocks = new_kv.shape[1] // BLK
    rank_count = 2 * seq_count

    def block_of(part, d, m):
        return (2 * d + (m[2] + part) % 2 - m[1] + rank_count) % rank_count

    def cache_spec(part):
        return pl.BlockSpec(
            (2, 1, BLK, features),
            lambda d, m: (0, 0, jnp.clip(block_of(part, d, m), 0, m[0] - 1), 0),
        )

    def new_spec(part):
        return pl.BlockSpec(
            (2, BLK, features),
            lambda d, m: (0, jnp.clip(block_of(part, d, m) - m[0], 0, new_blocks - 1), 0),
        )

    return pl.pallas_call(
        relay_kernel,
        out_shape=(
            jax.ShapeDtypeStruct((seq_count, 2, BLK, 2 * features), jnp.bfloat16),
            jax.ShapeDtypeStruct((seq_count, 2, BLK, features), jnp.bfloat16),
        ),
        grid_spec=pltpu.PrefetchScalarGridSpec(
            num_scalar_prefetch=1,
            grid=(seq_count,),
            in_specs=[cache_spec(0), new_spec(0), cache_spec(1), new_spec(1)],
            out_specs=(
                pl.BlockSpec((1, 2, BLK, features), lambda d, m: (d, 0, 0, m[2])),
                pl.BlockSpec((1, 2, BLK, features), lambda d, m: (d, 0, 0, 0)),
            ),
        ),
    )(meta, kv_cache, new_kv, kv_cache, new_kv)


def projection_kernel(x_ref, w_ref, o_ref):
    o_ref[...] = jnp.dot(x_ref[...], w_ref[0], preferred_element_type=jnp.float32).astype(
        o_ref.dtype
    )


def rope_projection_kernel(x_ref, w_ref, cos_ref, sin_ref, o_ref):
    weights = w_ref[0]
    features = weights.shape[1]
    half = HD // 2
    rows = lax.broadcasted_iota(jnp.int32, (features, features), 0)
    cols = lax.broadcasted_iota(jnp.int32, (features, features), 1)
    first = cols % HD < half
    swap = jnp.where(
        first & (rows == cols + half),
        -1.0,
        jnp.where(jnp.logical_not(first) & (rows == cols - half), 1.0, 0.0),
    ).astype(jnp.bfloat16)
    swapped = jnp.dot(weights, swap, preferred_element_type=jnp.float32).astype(jnp.bfloat16)
    plain = jnp.dot(x_ref[...], weights, preferred_element_type=jnp.float32)
    paired = jnp.dot(x_ref[...], swapped, preferred_element_type=jnp.float32)
    o_ref[...] = (plain * cos_ref[...] + paired * sin_ref[...]).astype(o_ref.dtype)


def project(normed, weights, part, tables=None):
    _, width, features = weights.shape
    rows = normed.shape[0]
    x_spec = pl.BlockSpec((rows, width), lambda i: (0, 0))
    w_spec = pl.BlockSpec((1, width, features), lambda i: (part, 0, 0))
    o_spec = pl.BlockSpec((rows, features), lambda i: (0, 0))
    out_shape = jax.ShapeDtypeStruct((rows, features), jnp.bfloat16)
    if tables is None:
        return pl.pallas_call(
            projection_kernel,
            out_shape=out_shape,
            grid=(1,),
            in_specs=[x_spec, w_spec],
            out_specs=o_spec,
        )(normed, weights)
    return pl.pallas_call(
        rope_projection_kernel,
        out_shape=out_shape,
        grid=(1,),
        in_specs=[x_spec, w_spec, o_spec, o_spec],
        out_specs=o_spec,
    )(normed, weights, *tables)


def local(tokens, norm_gain, w_qkv, w_out, kv_cache, cached_lengths, requests, block_start):
    group_idx = lax.axis_index("seq")
    tp_rank = lax.axis_index(("x", "core"))
    tp_count = lax.axis_size(("x", "core"))
    seq_count = lax.axis_size("seq")
    tok_count, model_width = tokens.shape
    features = w_qkv.shape[2]
    head_count = features // HD
    cache_len = kv_cache.shape[2]
    group_len = lax.dynamic_index_in_dim(cached_lengths, group_idx, keepdims=False)
    group_requests = lax.dynamic_index_in_dim(requests, group_idx, keepdims=False)
    group_start = lax.dynamic_index_in_dim(block_start, group_idx, keepdims=False)
    inputs = tokens.astype(jnp.float32)
    inverse_rms = lax.rsqrt(jnp.mean(inputs * inputs, axis=-1, keepdims=True) + 1e-05)
    normed = (inputs * inverse_rms * norm_gain.astype(jnp.float32)).astype(jnp.bfloat16)

    weights = jnp.transpose(w_qkv, (1, 0, 2))
    row_index = jnp.arange(tok_count, dtype=jnp.int32)
    request = row_index * group_requests // tok_count
    first_row = (request * tok_count + group_requests - 1) // group_requests
    positions = group_len + row_index - first_row
    cosine_table, sine_table = rope_tables(positions, HD)
    repeat = (1, features // (HD // 2))
    tables = (jnp.tile(cosine_table, repeat), jnp.tile(sine_table, repeat))
    new_keys = project(normed, weights, 1, tables)
    new_values = project(normed, weights, 2)
    new_kv = jnp.stack([new_keys, new_values])
    core = lax.axis_index("core")
    relay_meta = jnp.stack(
        [group_len // BLK, group_start, core, jnp.int32(tok_count // BLK)]
    ).astype(jnp.int32)
    own, other = relay(relay_meta, kv_cache, new_kv, seq_count)
    partner = lax.ppermute(other, "core", [(0, 1), (1, 0)])
    zero_index = jnp.zeros((), jnp.int32)
    joined = lax.dynamic_update_slice(
        own, partner, (zero_index, zero_index, zero_index, (1 - core) * features)
    )
    queries = project(normed, weights, 0, tables)
    joined, queries = lax.optimization_barrier((joined, queries))
    received = lax.all_to_all(joined, "seq", 0, 0, tiled=True)
    decode_cache = received.transpose(1, 0, 2, 3).reshape(2, 1, seq_count, 1, BLK, 2 * features)

    attn_meta = jnp.stack([group_len, group_requests]).astype(jnp.int32)
    attended = attend(attn_meta, queries, kv_cache, new_kv)
    rows_dev = tok_count // tp_count
    partial = jnp.dot(attended, w_out, preferred_element_type=jnp.float32).astype(jnp.bfloat16)
    summed = lax.dynamic_slice_in_dim(partial, tp_rank * rows_dev, rows_dev, 0).astype(jnp.float32)
    for shift in range(1, tp_count):
        target = (tp_rank + shift) % tp_count
        chunk = lax.dynamic_slice_in_dim(partial, target * rows_dev, rows_dev, 0)
        pairs = [(source, (source + shift) % tp_count) for source in range(tp_count)]
        summed = summed + lax.ppermute(chunk, ("x", "core"), pairs).astype(jnp.float32)
    own_rows = lax.dynamic_slice_in_dim(inputs, tp_rank * rows_dev, rows_dev, 0)
    layer_out = (own_rows + summed).astype(jnp.bfloat16)
    return (layer_out, decode_cache)


def solution(mesh):
    seq_count, tp_count = mesh.devices.shape
    split = Mesh(mesh.devices.reshape(seq_count, tp_count // 2, 2), ("seq", "x", "core"))
    tp = ("x", "core")
    placed = (
        P("seq", None),
        P(),
        P(None, None, tp),
        P(tp, None),
        P(None, "seq", None, tp),
        P(),
        P(),
        P(),
    )
    return jax.shard_map(
        local,
        mesh=split,
        in_specs=placed,
        out_specs=(P(("seq",) + tp, None), P(None, "seq", None, None, None, tp)),
        check_vma=False,
    )
```

```python
import math

import jax
import jax.numpy as jnp
from jax import lax
from jax.experimental import pallas as pl
from jax.experimental.pallas import tpu as pltpu
from jax.sharding import Mesh
from jax.sharding import PartitionSpec as P

HD = 96
BLK = 128
ROWS = 128


def rope_tables(positions, head_size):
    half_size = head_size // 2
    frequency = jnp.exp(
        jnp.arange(half_size, dtype=jnp.float32) * (-2.0 * math.log(10000.0) / head_size)
    )
    angles = positions.astype(jnp.float32)[:, None] * frequency[None, :]
    return (jnp.cos(angles), jnp.sin(angles))


def rope_pair(vectors, cosine_table, sine_table):
    half_size = vectors.shape[-1] // 2
    first_half = vectors[..., :half_size]
    second_half = vectors[..., half_size:]
    cos_wide = cosine_table[:, None, :]
    sin_wide = sine_table[:, None, :]
    return jnp.concatenate(
        [
            first_half * cos_wide - second_half * sin_wide,
            second_half * cos_wide + first_half * sin_wide,
        ],
        axis=-1,
    )


def request_of(index, group_requests, tok_count):
    scaled = index * group_requests
    if tok_count & (tok_count - 1) == 0:
        return lax.shift_right_logical(scaled, tok_count.bit_length() - 1)
    return scaled // tok_count


def head_picker(features, head):
    rows = lax.broadcasted_iota(jnp.int32, (features, HD), 0)
    cols = lax.broadcasted_iota(jnp.int32, (features, HD), 1)
    return (rows == cols + head * HD).astype(jnp.bfloat16)


def attention_kernel(
    meta_ref, q_ref, kc_ref, vc_ref, kn_ref, vn_ref, o_ref, kh_buf, vh_buf, qh_buf, acc_ref
):
    group_len = meta_ref[0]
    group_requests = meta_ref[1]
    head = pl.program_id(0)
    tok_count, features = q_ref.shape
    score_scale = 1.0 / math.sqrt(HD)
    picker = head_picker(features, head)

    def pick(values):
        return jnp.dot(values, picker, preferred_element_type=jnp.float32).astype(jnp.bfloat16)

    kh_buf[...] = pick(kc_ref[0, 0])
    vh_buf[...] = pick(vc_ref[0, 0])
    qh_buf[...] = pick(q_ref[...])
    kn = pick(kn_ref[0])
    vn = pick(vn_ref[0])
    dims = (((1,), (1,)), ((), ()))
    for chunk in range(tok_count // ROWS):
        rows = pl.ds(chunk * ROWS, ROWS)
        q = qh_buf[rows, :]
        s_old = lax.dot_general(q, kh_buf[...], dims, preferred_element_type=jnp.float32)
        s_new = lax.dot_general(q, kn, dims, preferred_element_type=jnp.float32)
        s_old = s_old * score_scale
        s_new = s_new * score_scale
        col = lax.broadcasted_iota(jnp.int32, s_old.shape, 1)
        s_old = jnp.where(col < group_len, s_old, -1e30)
        row = chunk * ROWS + lax.broadcasted_iota(jnp.int32, s_new.shape, 0)
        key = lax.broadcasted_iota(jnp.int32, s_new.shape, 1)
        same = request_of(row, group_requests, tok_count) == request_of(
            key, group_requests, tok_count
        )
        s_new = jnp.where(same & (key <= row), s_new, -1e30)
        peak = jnp.maximum(
            jnp.max(s_old, axis=1, keepdims=True), jnp.max(s_new, axis=1, keepdims=True)
        )
        e_old = jnp.exp(s_old - peak)
        e_new = jnp.exp(s_new - peak)
        total = jnp.sum(e_old, axis=1, keepdims=True) + jnp.sum(e_new, axis=1, keepdims=True)
        p_old = (e_old / total).astype(jnp.bfloat16)
        p_new = (e_new / total).astype(jnp.bfloat16)
        out = jnp.dot(p_old, vh_buf[...], preferred_element_type=jnp.float32) + jnp.dot(
            p_new, vn, preferred_element_type=jnp.float32
        )
        placed = lax.dot_general(
            out.astype(jnp.bfloat16), picker, dims, preferred_element_type=jnp.float32
        )

        @pl.when(head == 0)
        def _():
            acc_ref[rows, :] = placed

        @pl.when(head > 0)
        def _():
            acc_ref[rows, :] = acc_ref[rows, :] + placed

    @pl.when(head == pl.num_programs(0) - 1)
    def _():
        o_ref[...] = acc_ref[...].astype(jnp.bfloat16)


def attend(meta, queries, kv_cache, new_kv):
    tok_count, features = queries.shape
    cache_len = kv_cache.shape[2]
    full_q = pl.BlockSpec((tok_count, features), lambda h, m: (0, 0))
    cache_k = pl.BlockSpec((1, 1, cache_len, features), lambda h, m: (0, 0, 0, 0))
    cache_v = pl.BlockSpec((1, 1, cache_len, features), lambda h, m: (1, 0, 0, 0))
    new_k = pl.BlockSpec((1, tok_count, features), lambda h, m: (0, 0, 0))
    new_v = pl.BlockSpec((1, tok_count, features), lambda h, m: (1, 0, 0))
    return pl.pallas_call(
        attention_kernel,
        out_shape=jax.ShapeDtypeStruct(queries.shape, jnp.bfloat16),
        grid_spec=pltpu.PrefetchScalarGridSpec(
            num_scalar_prefetch=1,
            grid=(features // HD,),
            in_specs=[full_q, cache_k, cache_v, new_k, new_v],
            out_specs=full_q,
            scratch_shapes=[
                pltpu.VMEM((cache_len, HD), jnp.bfloat16),
                pltpu.VMEM((cache_len, HD), jnp.bfloat16),
                pltpu.VMEM((tok_count, HD), jnp.bfloat16),
                pltpu.VMEM((tok_count, features), jnp.float32),
            ],
        ),
    )(meta, queries, kv_cache, kv_cache, new_kv, new_kv)


def relay_kernel(meta_ref, own_c, own_n, other_c, other_n, own_ref, other_ref):
    len_blocks = meta_ref[0]
    group_start = meta_ref[1]
    core = meta_ref[2]
    new_blocks = meta_ref[3]
    dest = pl.program_id(0)
    rank_count = 2 * pl.num_programs(0)
    zero = jnp.zeros(own_n.shape[1:], own_n.dtype)
    for part, cache_ref, new_ref, out_ref in ((0, own_c, own_n, own_ref), (1, other_c, other_n, other_ref)):
        block = (2 * dest + (core + part) % 2 - group_start + rank_count) % rank_count
        old = block < len_blocks
        fresh = (block >= len_blocks) & (block < len_blocks + new_blocks)
        for kv in range(2):
            out_ref[0, kv] = jnp.where(
                old, cache_ref[kv, 0], jnp.where(fresh, new_ref[kv], zero)
            )


def relay(meta, kv_cache, new_kv, seq_count):
    features = kv_cache.shape[3]
    new_blocks = new_kv.shape[1] // BLK
    rank_count = 2 * seq_count

    def block_of(part, d, m):
        return (2 * d + (m[2] + part) % 2 - m[1] + rank_count) % rank_count

    def cache_spec(part):
        return pl.BlockSpec(
            (2, 1, BLK, features),
            lambda d, m: (0, 0, jnp.clip(block_of(part, d, m), 0, m[0] - 1), 0),
        )

    def new_spec(part):
        return pl.BlockSpec(
            (2, BLK, features),
            lambda d, m: (0, jnp.clip(block_of(part, d, m) - m[0], 0, new_blocks - 1), 0),
        )

    return pl.pallas_call(
        relay_kernel,
        out_shape=(
            jax.ShapeDtypeStruct((seq_count, 2, BLK, 2 * features), jnp.bfloat16),
            jax.ShapeDtypeStruct((seq_count, 2, BLK, features), jnp.bfloat16),
        ),
        grid_spec=pltpu.PrefetchScalarGridSpec(
            num_scalar_prefetch=1,
            grid=(seq_count,),
            in_specs=[cache_spec(0), new_spec(0), cache_spec(1), new_spec(1)],
            out_specs=(
                pl.BlockSpec((1, 2, BLK, features), lambda d, m: (d, 0, 0, m[2])),
                pl.BlockSpec((1, 2, BLK, features), lambda d, m: (d, 0, 0, 0)),
            ),
        ),
    )(meta, kv_cache, new_kv, kv_cache, new_kv)


def half_swap(features):
    half = HD // 2
    rows = lax.broadcasted_iota(jnp.int32, (features, features), 0)
    cols = lax.broadcasted_iota(jnp.int32, (features, features), 1)
    first = cols % HD < half
    return jnp.where(
        first & (rows == cols + half),
        -1.0,
        jnp.where(jnp.logical_not(first) & (rows == cols - half), 1.0, 0.0),
    ).astype(jnp.bfloat16)


def projection_kernel(x_ref, scale_ref, gain_ref, w_ref, cos_ref, sin_ref, q_ref, k_ref, v_ref, acc_ref):
    step = pl.program_id(0)
    features = w_ref.shape[2]
    swap = half_swap(features)
    normed = (x_ref[...].astype(jnp.float32) * scale_ref[...] * gain_ref[...]).astype(
        jnp.bfloat16
    )

    @pl.when(step == 0)
    def _():
        acc_ref[...] = jnp.zeros(acc_ref.shape, acc_ref.dtype)

    for part in range(2):
        weights = w_ref[part]
        swapped = jnp.dot(weights, swap, preferred_element_type=jnp.float32).astype(jnp.bfloat16)
        acc_ref[2 * part] += jnp.dot(normed, weights, preferred_element_type=jnp.float32)
        acc_ref[2 * part + 1] += jnp.dot(normed, swapped, preferred_element_type=jnp.float32)
    acc_ref[4] += jnp.dot(normed, w_ref[2], preferred_element_type=jnp.float32)

    @pl.when(step == pl.num_programs(0) - 1)
    def _():
        for part, out_ref in ((0, q_ref), (1, k_ref)):
            rotated = acc_ref[2 * part] * cos_ref[...] + acc_ref[2 * part + 1] * sin_ref[...]
            out_ref[...] = rotated.astype(out_ref.dtype)
        v_ref[...] = acc_ref[4].astype(v_ref.dtype)


def project(tokens, scale, gain, weights, tables):
    parts, width, features = weights.shape
    rows = tokens.shape[0]
    chunk = 512 if width % 512 == 0 else width
    full = pl.BlockSpec((rows, features), lambda k: (0, 0))
    out = jax.ShapeDtypeStruct((rows, features), jnp.bfloat16)
    return pl.pallas_call(
        projection_kernel,
        out_shape=(out, out, out),
        grid=(width // chunk,),
        in_specs=[
            pl.BlockSpec((rows, chunk), lambda k: (0, k)),
            pl.BlockSpec((rows, 1), lambda k: (0, 0)),
            pl.BlockSpec((1, chunk), lambda k: (0, k)),
            pl.BlockSpec((parts, chunk, features), lambda k: (0, k, 0)),
            full,
            full,
        ],
        out_specs=(full, full, full),
        scratch_shapes=[pltpu.VMEM((5, rows, features), jnp.float32)],
    )(tokens, scale, gain, weights, *tables)


def local(tokens, norm_gain, w_qkv, w_out, kv_cache, cached_lengths, requests, block_start):
    group_idx = lax.axis_index("seq")
    tp_rank = lax.axis_index(("x", "core"))
    tp_count = lax.axis_size(("x", "core"))
    seq_count = lax.axis_size("seq")
    tok_count, model_width = tokens.shape
    features = w_qkv.shape[2]
    head_count = features // HD
    cache_len = kv_cache.shape[2]
    group_len = lax.dynamic_index_in_dim(cached_lengths, group_idx, keepdims=False)
    group_requests = lax.dynamic_index_in_dim(requests, group_idx, keepdims=False)
    group_start = lax.dynamic_index_in_dim(block_start, group_idx, keepdims=False)
    inputs = tokens.astype(jnp.float32)
    inverse_rms = lax.rsqrt(jnp.mean(inputs * inputs, axis=-1, keepdims=True) + 1e-05)

    weights = jnp.transpose(w_qkv, (1, 0, 2))
    row_index = jnp.arange(tok_count, dtype=jnp.int32)
    request = row_index * group_requests // tok_count
    first_row = (request * tok_count + group_requests - 1) // group_requests
    positions = group_len + row_index - first_row
    cosine_table, sine_table = rope_tables(positions, HD)
    repeat = (1, features // (HD // 2))
    tables = (jnp.tile(cosine_table, repeat), jnp.tile(sine_table, repeat))
    queries, new_keys, new_values = project(
        tokens, inverse_rms, norm_gain.astype(jnp.float32).reshape(1, model_width), weights, tables
    )
    new_kv = jnp.stack([new_keys, new_values])
    core = lax.axis_index("core")
    relay_meta = jnp.stack(
        [group_len // BLK, group_start, core, jnp.int32(tok_count // BLK)]
    ).astype(jnp.int32)
    own, other = relay(relay_meta, kv_cache, new_kv, seq_count)
    partner = lax.ppermute(other, "core", [(0, 1), (1, 0)])
    zero_index = jnp.zeros((), jnp.int32)
    joined = lax.dynamic_update_slice(
        own, partner, (zero_index, zero_index, zero_index, (1 - core) * features)
    )
    joined, queries = lax.optimization_barrier((joined, queries))
    received = lax.all_to_all(joined, "seq", 0, 0, tiled=True)
    decode_cache = received.transpose(1, 0, 2, 3).reshape(2, 1, seq_count, 1, BLK, 2 * features)

    attn_meta = jnp.stack([group_len, group_requests]).astype(jnp.int32)
    attended = attend(attn_meta, queries, kv_cache, new_kv)
    rows_dev = tok_count // tp_count
    partial = jnp.dot(attended, w_out, preferred_element_type=jnp.float32).astype(jnp.bfloat16)
    summed = lax.dynamic_slice_in_dim(partial, tp_rank * rows_dev, rows_dev, 0).astype(jnp.float32)
    for shift in range(1, tp_count):
        target = (tp_rank + shift) % tp_count
        chunk = lax.dynamic_slice_in_dim(partial, target * rows_dev, rows_dev, 0)
        pairs = [(source, (source + shift) % tp_count) for source in range(tp_count)]
        summed = summed + lax.ppermute(chunk, ("x", "core"), pairs).astype(jnp.float32)
    own_rows = lax.dynamic_slice_in_dim(inputs, tp_rank * rows_dev, rows_dev, 0)
    layer_out = (own_rows + summed).astype(jnp.bfloat16)
    return (layer_out, decode_cache)


def solution(mesh):
    seq_count, tp_count = mesh.devices.shape
    split = Mesh(mesh.devices.reshape(seq_count, tp_count // 2, 2), ("seq", "x", "core"))
    tp = ("x", "core")
    placed = (
        P("seq", None),
        P(),
        P(None, None, tp),
        P(tp, None),
        P(None, "seq", None, tp),
        P(),
        P(),
        P(),
    )
    return jax.shard_map(
        local,
        mesh=split,
        in_specs=placed,
        out_specs=(P(("seq",) + tp, None), P(None, "seq", None, None, None, tp)),
        check_vma=False,
    )
```

```python
import math

import jax
import jax.numpy as jnp
from jax import lax
from jax.experimental import pallas as pl
from jax.experimental.pallas import tpu as pltpu
from jax.sharding import Mesh
from jax.sharding import PartitionSpec as P

HD = 96
BLK = 128
ROWS = 128


def rope_tables(positions, head_size):
    half_size = head_size // 2
    frequency = jnp.exp(
        jnp.arange(half_size, dtype=jnp.float32) * (-2.0 * math.log(10000.0) / head_size)
    )
    angles = positions.astype(jnp.float32)[:, None] * frequency[None, :]
    return (jnp.cos(angles), jnp.sin(angles))


def rope_pair(vectors, cosine_table, sine_table):
    half_size = vectors.shape[-1] // 2
    first_half = vectors[..., :half_size]
    second_half = vectors[..., half_size:]
    cos_wide = cosine_table[:, None, :]
    sin_wide = sine_table[:, None, :]
    return jnp.concatenate(
        [
            first_half * cos_wide - second_half * sin_wide,
            second_half * cos_wide + first_half * sin_wide,
        ],
        axis=-1,
    )


def request_of(index, group_requests, tok_count):
    scaled = index * group_requests
    if tok_count & (tok_count - 1) == 0:
        return lax.shift_right_logical(scaled, tok_count.bit_length() - 1)
    return scaled // tok_count


def head_picker(features, head):
    rows = lax.broadcasted_iota(jnp.int32, (features, HD), 0)
    cols = lax.broadcasted_iota(jnp.int32, (features, HD), 1)
    return (rows == cols + head * HD).astype(jnp.bfloat16)


def attention_kernel(
    meta_ref, q_ref, kc_ref, vc_ref, kn_ref, vn_ref, o_ref, kh_buf, vh_buf, qh_buf, acc_ref
):
    group_len = meta_ref[0]
    group_requests = meta_ref[1]
    head = pl.program_id(0)
    tok_count, features = q_ref.shape
    score_scale = 1.0 / math.sqrt(HD)
    picker = head_picker(features, head)

    def pick(values):
        return jnp.dot(values, picker, preferred_element_type=jnp.float32).astype(jnp.bfloat16)

    kh_buf[...] = pick(kc_ref[0, 0])
    vh_buf[...] = pick(vc_ref[0, 0])
    qh_buf[...] = pick(q_ref[...])
    kn = pick(kn_ref[0])
    vn = pick(vn_ref[0])
    dims = (((1,), (1,)), ((), ()))
    for chunk in range(tok_count // ROWS):
        rows = pl.ds(chunk * ROWS, ROWS)
        q = qh_buf[rows, :]
        s_old = lax.dot_general(q, kh_buf[...], dims, preferred_element_type=jnp.float32)
        s_new = lax.dot_general(q, kn, dims, preferred_element_type=jnp.float32)
        s_old = s_old * score_scale
        s_new = s_new * score_scale
        col = lax.broadcasted_iota(jnp.int32, s_old.shape, 1)
        s_old = jnp.where(col < group_len, s_old, -1e30)
        row = chunk * ROWS + lax.broadcasted_iota(jnp.int32, s_new.shape, 0)
        key = lax.broadcasted_iota(jnp.int32, s_new.shape, 1)
        same = request_of(row, group_requests, tok_count) == request_of(
            key, group_requests, tok_count
        )
        s_new = jnp.where(same & (key <= row), s_new, -1e30)
        peak = jnp.maximum(
            jnp.max(s_old, axis=1, keepdims=True), jnp.max(s_new, axis=1, keepdims=True)
        )
        e_old = jnp.exp(s_old - peak)
        e_new = jnp.exp(s_new - peak)
        total = jnp.sum(e_old, axis=1, keepdims=True) + jnp.sum(e_new, axis=1, keepdims=True)
        p_old = (e_old / total).astype(jnp.bfloat16)
        p_new = (e_new / total).astype(jnp.bfloat16)
        out = jnp.dot(p_old, vh_buf[...], preferred_element_type=jnp.float32) + jnp.dot(
            p_new, vn, preferred_element_type=jnp.float32
        )
        placed = lax.dot_general(
            out.astype(jnp.bfloat16), picker, dims, preferred_element_type=jnp.float32
        )

        @pl.when(head == 0)
        def _():
            acc_ref[rows, :] = placed

        @pl.when(head > 0)
        def _():
            acc_ref[rows, :] = acc_ref[rows, :] + placed

    @pl.when(head == pl.num_programs(0) - 1)
    def _():
        o_ref[...] = acc_ref[...].astype(jnp.bfloat16)


def attend(meta, queries, kv_cache, new_kv):
    tok_count, features = queries.shape
    cache_len = kv_cache.shape[2]
    full_q = pl.BlockSpec((tok_count, features), lambda h, m: (0, 0))
    cache_k = pl.BlockSpec((1, 1, cache_len, features), lambda h, m: (0, 0, 0, 0))
    cache_v = pl.BlockSpec((1, 1, cache_len, features), lambda h, m: (1, 0, 0, 0))
    new_k = pl.BlockSpec((1, tok_count, features), lambda h, m: (0, 0, 0))
    new_v = pl.BlockSpec((1, tok_count, features), lambda h, m: (1, 0, 0))
    return pl.pallas_call(
        attention_kernel,
        out_shape=jax.ShapeDtypeStruct(queries.shape, jnp.bfloat16),
        grid_spec=pltpu.PrefetchScalarGridSpec(
            num_scalar_prefetch=1,
            grid=(features // HD,),
            in_specs=[full_q, cache_k, cache_v, new_k, new_v],
            out_specs=full_q,
            scratch_shapes=[
                pltpu.VMEM((cache_len, HD), jnp.bfloat16),
                pltpu.VMEM((cache_len, HD), jnp.bfloat16),
                pltpu.VMEM((tok_count, HD), jnp.bfloat16),
                pltpu.VMEM((tok_count, features), jnp.float32),
            ],
        ),
    )(meta, queries, kv_cache, kv_cache, new_kv, new_kv)


def relay_kernel(meta_ref, own_c, own_n, other_c, other_n, own_ref, other_ref):
    len_blocks = meta_ref[0]
    group_start = meta_ref[1]
    core = meta_ref[2]
    new_blocks = meta_ref[3]
    dest = pl.program_id(0)
    rank_count = 2 * pl.num_programs(0)
    zero = jnp.zeros(own_n.shape[1:], own_n.dtype)
    for part, cache_ref, new_ref, out_ref in ((0, own_c, own_n, own_ref), (1, other_c, other_n, other_ref)):
        block = (2 * dest + (core + part) % 2 - group_start + rank_count) % rank_count
        old = block < len_blocks
        fresh = (block >= len_blocks) & (block < len_blocks + new_blocks)
        for kv in range(2):
            out_ref[0, kv] = jnp.where(
                old, cache_ref[kv, 0], jnp.where(fresh, new_ref[kv], zero)
            )


def relay(meta, kv_cache, new_kv, seq_count):
    features = kv_cache.shape[3]
    new_blocks = new_kv.shape[1] // BLK
    rank_count = 2 * seq_count

    def block_of(part, d, m):
        return (2 * d + (m[2] + part) % 2 - m[1] + rank_count) % rank_count

    def cache_spec(part):
        return pl.BlockSpec(
            (2, 1, BLK, features),
            lambda d, m: (0, 0, jnp.clip(block_of(part, d, m), 0, m[0] - 1), 0),
        )

    def new_spec(part):
        return pl.BlockSpec(
            (2, BLK, features),
            lambda d, m: (0, jnp.clip(block_of(part, d, m) - m[0], 0, new_blocks - 1), 0),
        )

    return pl.pallas_call(
        relay_kernel,
        out_shape=(
            jax.ShapeDtypeStruct((seq_count, 2, BLK, 2 * features), jnp.bfloat16),
            jax.ShapeDtypeStruct((seq_count, 2, BLK, features), jnp.bfloat16),
        ),
        grid_spec=pltpu.PrefetchScalarGridSpec(
            num_scalar_prefetch=1,
            grid=(seq_count,),
            in_specs=[cache_spec(0), new_spec(0), cache_spec(1), new_spec(1)],
            out_specs=(
                pl.BlockSpec((1, 2, BLK, features), lambda d, m: (d, 0, 0, m[2])),
                pl.BlockSpec((1, 2, BLK, features), lambda d, m: (d, 0, 0, 0)),
            ),
        ),
    )(meta, kv_cache, new_kv, kv_cache, new_kv)


def half_swap(features):
    half = HD // 2
    rows = lax.broadcasted_iota(jnp.int32, (features, features), 0)
    cols = lax.broadcasted_iota(jnp.int32, (features, features), 1)
    first = cols % HD < half
    return jnp.where(
        first & (rows == cols + half),
        -1.0,
        jnp.where(jnp.logical_not(first) & (rows == cols - half), 1.0, 0.0),
    ).astype(jnp.bfloat16)


def projection_kernel(x_ref, gain_ref, w_ref, cos_ref, sin_ref, kv_ref, q_ref, normed_ref):
    step = pl.program_id(0)

    @pl.when(step == 0)
    def _():
        inputs = x_ref[...].astype(jnp.float32)
        inverse_rms = lax.rsqrt(jnp.mean(inputs * inputs, axis=-1, keepdims=True) + 1e-05)
        normed_ref[...] = (inputs * inverse_rms * gain_ref[...]).astype(jnp.bfloat16)

    weights = w_ref[0]
    plain = jnp.dot(normed_ref[...], weights, preferred_element_type=jnp.float32)

    def rotated():
        swap = half_swap(weights.shape[1])
        swapped = jnp.dot(weights, swap, preferred_element_type=jnp.float32).astype(jnp.bfloat16)
        paired = jnp.dot(normed_ref[...], swapped, preferred_element_type=jnp.float32)
        return (plain * cos_ref[...] + paired * sin_ref[...]).astype(jnp.bfloat16)

    @pl.when(step == 0)
    def _():
        kv_ref[0] = rotated()

    @pl.when(step == 1)
    def _():
        kv_ref[1] = plain.astype(jnp.bfloat16)

    @pl.when(step == 2)
    def _():
        q_ref[...] = rotated()


def project(tokens, gain, weights, tables):
    parts, width, features = weights.shape
    rows = tokens.shape[0]
    full = pl.BlockSpec((rows, features), lambda s: (0, 0))
    return pl.pallas_call(
        projection_kernel,
        out_shape=(
            jax.ShapeDtypeStruct((2, rows, features), jnp.bfloat16),
            jax.ShapeDtypeStruct((rows, features), jnp.bfloat16),
        ),
        grid=(parts,),
        in_specs=[
            pl.BlockSpec((rows, width), lambda s: (0, 0)),
            pl.BlockSpec((1, width), lambda s: (0, 0)),
            pl.BlockSpec((1, width, features), lambda s: ((s + 1) % parts, 0, 0)),
            full,
            full,
        ],
        out_specs=(pl.BlockSpec((2, rows, features), lambda s: (0, 0, 0)), full),
        scratch_shapes=[pltpu.VMEM((rows, width), jnp.bfloat16)],
    )(tokens, gain, weights, *tables)


def local(tokens, norm_gain, w_qkv, w_out, kv_cache, cached_lengths, requests, block_start):
    group_idx = lax.axis_index("seq")
    tp_rank = lax.axis_index(("x", "core"))
    tp_count = lax.axis_size(("x", "core"))
    seq_count = lax.axis_size("seq")
    tok_count, model_width = tokens.shape
    features = w_qkv.shape[2]
    head_count = features // HD
    cache_len = kv_cache.shape[2]
    group_params = lax.dynamic_index_in_dim(
        jnp.stack([cached_lengths, requests, block_start], axis=1), group_idx, keepdims=False
    )
    group_len = group_params[0]
    group_requests = group_params[1]
    group_start = group_params[2]
    inputs = tokens.astype(jnp.float32)

    weights = jnp.transpose(w_qkv, (1, 0, 2))
    row_index = jnp.arange(tok_count, dtype=jnp.int32)
    request = row_index * group_requests // tok_count
    first_row = (request * tok_count + group_requests - 1) // group_requests
    positions = group_len + row_index - first_row
    cosine_table, sine_table = rope_tables(positions, HD)
    repeat = (1, features // (HD // 2))
    tables = (jnp.tile(cosine_table, repeat), jnp.tile(sine_table, repeat))
    new_kv, queries = project(
        tokens, norm_gain.astype(jnp.float32).reshape(1, model_width), weights, tables
    )
    core = lax.axis_index("core")
    relay_meta = jnp.stack(
        [group_len // BLK, group_start, core, jnp.int32(tok_count // BLK)]
    ).astype(jnp.int32)
    own, other = relay(relay_meta, kv_cache, new_kv, seq_count)
    partner = lax.ppermute(other, "core", [(0, 1), (1, 0)])
    zero_index = jnp.zeros((), jnp.int32)
    joined = lax.dynamic_update_slice(
        own, partner, (zero_index, zero_index, zero_index, (1 - core) * features)
    )
    joined, queries = lax.optimization_barrier((joined, queries))
    received = lax.all_to_all(joined, "seq", 0, 0, tiled=True)
    decode_cache = received.transpose(1, 0, 2, 3).reshape(2, 1, seq_count, 1, BLK, 2 * features)

    attn_meta = jnp.stack([group_len, group_requests]).astype(jnp.int32)
    attended = attend(attn_meta, queries, kv_cache, new_kv)
    rows_dev = tok_count // tp_count
    partial = jnp.dot(attended, w_out, preferred_element_type=jnp.float32).astype(jnp.bfloat16)
    summed = lax.dynamic_slice_in_dim(partial, tp_rank * rows_dev, rows_dev, 0).astype(jnp.float32)
    for shift in range(1, tp_count):
        target = (tp_rank + shift) % tp_count
        chunk = lax.dynamic_slice_in_dim(partial, target * rows_dev, rows_dev, 0)
        pairs = [(source, (source + shift) % tp_count) for source in range(tp_count)]
        summed = summed + lax.ppermute(chunk, ("x", "core"), pairs).astype(jnp.float32)
    own_rows = lax.dynamic_slice_in_dim(inputs, tp_rank * rows_dev, rows_dev, 0)
    layer_out = (own_rows + summed).astype(jnp.bfloat16)
    return (layer_out, decode_cache)


def solution(mesh):
    seq_count, tp_count = mesh.devices.shape
    split = Mesh(mesh.devices.reshape(seq_count, tp_count // 2, 2), ("seq", "x", "core"))
    tp = ("x", "core")
    placed = (
        P("seq", None),
        P(),
        P(None, None, tp),
        P(tp, None),
        P(None, "seq", None, tp),
        P(),
        P(),
        P(),
    )
    return jax.shard_map(
        local,
        mesh=split,
        in_specs=placed,
        out_specs=(P(("seq",) + tp, None), P(None, "seq", None, None, None, tp)),
        check_vma=False,
    )
```

```python
import functools
import math

import jax
import jax.numpy as jnp
from jax import lax
from jax.experimental import pallas as pl
from jax.experimental.pallas import tpu as pltpu
from jax.sharding import Mesh
from jax.sharding import PartitionSpec as P

HD = 96
BLK = 128
ROWS = 128


def rope_tables(positions, head_size):
    half_size = head_size // 2
    frequency = jnp.exp(
        jnp.arange(half_size, dtype=jnp.float32) * (-2.0 * math.log(10000.0) / head_size)
    )
    angles = positions.astype(jnp.float32)[:, None] * frequency[None, :]
    return (jnp.cos(angles), jnp.sin(angles))


def rope_pair(vectors, cosine_table, sine_table):
    half_size = vectors.shape[-1] // 2
    first_half = vectors[..., :half_size]
    second_half = vectors[..., half_size:]
    cos_wide = cosine_table[:, None, :]
    sin_wide = sine_table[:, None, :]
    return jnp.concatenate(
        [
            first_half * cos_wide - second_half * sin_wide,
            second_half * cos_wide + first_half * sin_wide,
        ],
        axis=-1,
    )


def request_of(index, group_requests, tok_count):
    scaled = index * group_requests
    if tok_count & (tok_count - 1) == 0:
        return lax.shift_right_logical(scaled, tok_count.bit_length() - 1)
    return scaled // tok_count


def head_picker(features, head):
    rows = lax.broadcasted_iota(jnp.int32, (features, HD), 0)
    cols = lax.broadcasted_iota(jnp.int32, (features, HD), 1)
    return (rows == cols + head * HD).astype(jnp.bfloat16)


def attention_kernel(
    meta_ref, q_ref, kc_ref, vc_ref, kn_ref, vn_ref, o_ref, kh_buf, vh_buf, qh_buf, acc_ref
):
    group_len = meta_ref[0]
    group_requests = meta_ref[1]
    head = pl.program_id(0)
    tok_count, features = q_ref.shape
    score_scale = 1.0 / math.sqrt(HD)
    picker = head_picker(features, head)

    def pick(values):
        return jnp.dot(values, picker, preferred_element_type=jnp.float32).astype(jnp.bfloat16)

    kh_buf[...] = pick(kc_ref[0, 0])
    vh_buf[...] = pick(vc_ref[0, 0])
    qh_buf[...] = pick(q_ref[...])
    kn = pick(kn_ref[0])
    vn = pick(vn_ref[0])
    dims = (((1,), (1,)), ((), ()))
    for chunk in range(tok_count // ROWS):
        rows = pl.ds(chunk * ROWS, ROWS)
        q = qh_buf[rows, :]
        s_old = lax.dot_general(q, kh_buf[...], dims, preferred_element_type=jnp.float32)
        s_new = lax.dot_general(q, kn, dims, preferred_element_type=jnp.float32)
        s_old = s_old * score_scale
        s_new = s_new * score_scale
        col = lax.broadcasted_iota(jnp.int32, s_old.shape, 1)
        s_old = jnp.where(col < group_len, s_old, -1e30)
        row = chunk * ROWS + lax.broadcasted_iota(jnp.int32, s_new.shape, 0)
        key = lax.broadcasted_iota(jnp.int32, s_new.shape, 1)
        same = request_of(row, group_requests, tok_count) == request_of(
            key, group_requests, tok_count
        )
        s_new = jnp.where(same & (key <= row), s_new, -1e30)
        peak = jnp.maximum(
            jnp.max(s_old, axis=1, keepdims=True), jnp.max(s_new, axis=1, keepdims=True)
        )
        e_old = jnp.exp(s_old - peak)
        e_new = jnp.exp(s_new - peak)
        total = jnp.sum(e_old, axis=1, keepdims=True) + jnp.sum(e_new, axis=1, keepdims=True)
        p_old = (e_old / total).astype(jnp.bfloat16)
        p_new = (e_new / total).astype(jnp.bfloat16)
        out = jnp.dot(p_old, vh_buf[...], preferred_element_type=jnp.float32) + jnp.dot(
            p_new, vn, preferred_element_type=jnp.float32
        )
        placed = lax.dot_general(
            out.astype(jnp.bfloat16), picker, dims, preferred_element_type=jnp.float32
        )

        @pl.when(head == 0)
        def _():
            acc_ref[rows, :] = placed

        @pl.when(head > 0)
        def _():
            acc_ref[rows, :] = acc_ref[rows, :] + placed

    @pl.when(head == pl.num_programs(0) - 1)
    def _():
        o_ref[...] = acc_ref[...].astype(jnp.bfloat16)


def attend(meta, queries, kv_cache, new_kv):
    tok_count, features = queries.shape
    cache_len = kv_cache.shape[2]
    full_q = pl.BlockSpec((tok_count, features), lambda h, m: (0, 0))
    cache_k = pl.BlockSpec((1, 1, cache_len, features), lambda h, m: (0, 0, 0, 0))
    cache_v = pl.BlockSpec((1, 1, cache_len, features), lambda h, m: (1, 0, 0, 0))
    new_k = pl.BlockSpec((1, tok_count, features), lambda h, m: (0, 0, 0))
    new_v = pl.BlockSpec((1, tok_count, features), lambda h, m: (1, 0, 0))
    return pl.pallas_call(
        attention_kernel,
        out_shape=jax.ShapeDtypeStruct(queries.shape, jnp.bfloat16),
        grid_spec=pltpu.PrefetchScalarGridSpec(
            num_scalar_prefetch=1,
            grid=(features // HD,),
            in_specs=[full_q, cache_k, cache_v, new_k, new_v],
            out_specs=full_q,
            scratch_shapes=[
                pltpu.VMEM((cache_len, HD), jnp.bfloat16),
                pltpu.VMEM((cache_len, HD), jnp.bfloat16),
                pltpu.VMEM((tok_count, HD), jnp.bfloat16),
                pltpu.VMEM((tok_count, features), jnp.float32),
            ],
        ),
    )(meta, queries, kv_cache, kv_cache, new_kv, new_kv)


def relay_kernel(meta_ref, own_c, own_n, mate_c, mate_n, out_ref):
    len_blocks = meta_ref[0]
    group_start = meta_ref[1]
    core = meta_ref[2]
    new_blocks = meta_ref[3]
    dest = pl.program_id(0)
    rank_count = 2 * pl.num_programs(0)
    features = own_n.shape[2]
    block = (2 * dest + core - group_start + rank_count) % rank_count
    old = block < len_blocks
    fresh = (block >= len_blocks) & (block < len_blocks + new_blocks)
    zero = jnp.zeros(own_n.shape[1:], own_n.dtype)
    first = core == 0
    for kv in range(2):
        mine = jnp.where(old, own_c[kv, 0], jnp.where(fresh, own_n[kv], zero))
        mate = jnp.where(old, mate_c[kv, 0], jnp.where(fresh, mate_n[kv], zero))
        out_ref[0, kv, :, :features] = jnp.where(first, mine, mate)
        out_ref[0, kv, :, features:] = jnp.where(first, mate, mine)


def relay(meta, kv_cache, new_kv, mate_cache, mate_new, seq_count):
    features = kv_cache.shape[3]
    new_blocks = new_kv.shape[1] // BLK
    rank_count = 2 * seq_count

    def block_of(d, m):
        return (2 * d + m[2] - m[1] + rank_count) % rank_count

    cache_spec = pl.BlockSpec(
        (2, 1, BLK, features),
        lambda d, m: (0, 0, jnp.clip(block_of(d, m), 0, m[0] - 1), 0),
    )
    new_spec = pl.BlockSpec(
        (2, BLK, features),
        lambda d, m: (0, jnp.clip(block_of(d, m) - m[0], 0, new_blocks - 1), 0),
    )
    return pl.pallas_call(
        relay_kernel,
        out_shape=jax.ShapeDtypeStruct((seq_count, 2, BLK, 2 * features), jnp.bfloat16),
        grid_spec=pltpu.PrefetchScalarGridSpec(
            num_scalar_prefetch=1,
            grid=(seq_count,),
            in_specs=[cache_spec, new_spec, cache_spec, new_spec],
            out_specs=pl.BlockSpec((1, 2, BLK, 2 * features), lambda d, m: (d, 0, 0, 0)),
        ),
    )(meta, kv_cache, new_kv, mate_cache, mate_new)


def half_swap(features):
    half = HD // 2
    rows = lax.broadcasted_iota(jnp.int32, (features, features), 0)
    cols = lax.broadcasted_iota(jnp.int32, (features, features), 1)
    first = cols % HD < half
    return jnp.where(
        first & (rows == cols + half),
        -1.0,
        jnp.where(jnp.logical_not(first) & (rows == cols - half), 1.0, 0.0),
    ).astype(jnp.bfloat16)


def projection_kernel(part_ref, x_ref, gain_ref, w_ref, cos_ref, sin_ref, *refs, parts):
    out_refs = refs[:-1]
    normed_ref = refs[-1]
    step = pl.program_id(0)

    @pl.when(step == 0)
    def _():
        inputs = x_ref[...].astype(jnp.float32)
        inverse_rms = lax.rsqrt(jnp.mean(inputs * inputs, axis=-1, keepdims=True) + 1e-05)
        normed_ref[...] = (inputs * inverse_rms * gain_ref[...]).astype(jnp.bfloat16)

    weights = w_ref[0]
    plain = jnp.dot(normed_ref[...], weights, preferred_element_type=jnp.float32)

    def rotated():
        swap = half_swap(weights.shape[1])
        swapped = jnp.dot(weights, swap, preferred_element_type=jnp.float32).astype(jnp.bfloat16)
        paired = jnp.dot(normed_ref[...], swapped, preferred_element_type=jnp.float32)
        return (plain * cos_ref[...] + paired * sin_ref[...]).astype(jnp.bfloat16)

    for index, part in enumerate(parts):

        @pl.when(step == index)
        def _():
            value = rotated() if part < 2 else plain.astype(jnp.bfloat16)
            out_refs[index][...] = value


def project(tokens, gain, weights, tables, parts):
    _, width, features = weights.shape
    rows = tokens.shape[0]
    full = pl.BlockSpec((rows, features), lambda s: (0, 0))
    table = jnp.asarray(parts, jnp.int32)
    out = jax.ShapeDtypeStruct((rows, features), jnp.bfloat16)
    return pl.pallas_call(
        functools.partial(projection_kernel, parts=parts),
        out_shape=tuple(out for _ in parts),
        grid_spec=pltpu.PrefetchScalarGridSpec(
            num_scalar_prefetch=1,
            grid=(len(parts),),
            in_specs=[
                pl.BlockSpec((rows, width), lambda s, t: (0, 0)),
                pl.BlockSpec((1, width), lambda s, t: (0, 0)),
                pl.BlockSpec((1, width, features), lambda s, t: (t[s], 0, 0)),
                pl.BlockSpec((rows, features), lambda s, t: (0, 0)),
                pl.BlockSpec((rows, features), lambda s, t: (0, 0)),
            ],
            out_specs=tuple(pl.BlockSpec((rows, features), lambda s, t: (0, 0)) for _ in parts),
            scratch_shapes=[pltpu.VMEM((rows, width), jnp.bfloat16)],
        ),
    )(table, tokens, gain, weights, *tables)


def local(tokens, norm_gain, w_qkv, w_out, kv_cache, cached_lengths, requests, block_start):
    group_idx = lax.axis_index("seq")
    tp_rank = lax.axis_index(("x", "core"))
    tp_count = lax.axis_size(("x", "core"))
    seq_count = lax.axis_size("seq")
    tok_count, model_width = tokens.shape
    features = w_qkv.shape[2]
    head_count = features // HD
    cache_len = kv_cache.shape[2]
    group_params = lax.dynamic_index_in_dim(
        jnp.stack([cached_lengths, requests, block_start], axis=1), group_idx, keepdims=False
    )
    group_len = group_params[0]
    group_requests = group_params[1]
    group_start = group_params[2]
    inputs = tokens.astype(jnp.float32)

    weights = jnp.transpose(w_qkv, (1, 0, 2))
    row_index = jnp.arange(tok_count, dtype=jnp.int32)
    request = row_index * group_requests // tok_count
    first_row = (request * tok_count + group_requests - 1) // group_requests
    positions = group_len + row_index - first_row
    half_size = HD // 2
    frequency = jnp.exp(
        jnp.arange(half_size, dtype=jnp.float32) * (-2.0 * math.log(10000.0) / HD)
    )
    angles = positions.astype(jnp.float32)[:, None] * jnp.tile(frequency, features // half_size)
    tables = (jnp.cos(angles), jnp.sin(angles))
    gain = norm_gain.astype(jnp.float32).reshape(1, model_width)
    core = lax.axis_index("core")
    swap_cores = [(0, 1), (1, 0)]
    mate_cache = lax.ppermute(kv_cache, "core", swap_cores)
    new_keys, new_values = project(tokens, gain, weights, tables, (1, 2))
    new_kv = jnp.stack([new_keys, new_values])
    mate_new = lax.ppermute(new_kv, "core", swap_cores)
    relay_meta = jnp.stack(
        [group_len // BLK, group_start, core, jnp.int32(tok_count // BLK)]
    ).astype(jnp.int32)
    joined = relay(relay_meta, kv_cache, new_kv, mate_cache, mate_new, seq_count)
    (queries,) = project(tokens, gain, weights, tables, (0,))
    joined, attn_kv = lax.optimization_barrier((joined, new_kv))
    received = lax.all_to_all(joined, "seq", 0, 0, tiled=True)
    decode_cache = received.transpose(1, 0, 2, 3).reshape(2, 1, seq_count, 1, BLK, 2 * features)

    attn_meta = jnp.stack([group_len, group_requests]).astype(jnp.int32)
    attended = attend(attn_meta, queries, kv_cache, attn_kv)
    rows_dev = tok_count // tp_count
    partial = jnp.dot(attended, w_out, preferred_element_type=jnp.float32).astype(jnp.bfloat16)
    summed = lax.dynamic_slice_in_dim(partial, tp_rank * rows_dev, rows_dev, 0).astype(jnp.float32)
    for shift in range(1, tp_count):
        target = (tp_rank + shift) % tp_count
        chunk = lax.dynamic_slice_in_dim(partial, target * rows_dev, rows_dev, 0)
        pairs = [(source, (source + shift) % tp_count) for source in range(tp_count)]
        summed = summed + lax.ppermute(chunk, ("x", "core"), pairs).astype(jnp.float32)
    own_rows = lax.dynamic_slice_in_dim(inputs, tp_rank * rows_dev, rows_dev, 0)
    layer_out = (own_rows + summed).astype(jnp.bfloat16)
    return (layer_out, decode_cache)


def solution(mesh):
    seq_count, tp_count = mesh.devices.shape
    split = Mesh(mesh.devices.reshape(seq_count, tp_count // 2, 2), ("seq", "x", "core"))
    tp = ("x", "core")
    placed = (
        P("seq", None),
        P(),
        P(None, None, tp),
        P(tp, None),
        P(None, "seq", None, tp),
        P(),
        P(),
        P(),
    )
    return jax.shard_map(
        local,
        mesh=split,
        in_specs=placed,
        out_specs=(P(("seq",) + tp, None), P(None, "seq", None, None, None, tp)),
        check_vma=False,
    )
```

```python
import functools
import math

import jax
import jax.numpy as jnp
from jax import lax
from jax.experimental import pallas as pl
from jax.experimental.pallas import tpu as pltpu
from jax.sharding import Mesh
from jax.sharding import PartitionSpec as P

HD = 96
BLK = 128
ROWS = 128


def rope_tables(positions, head_size):
    half_size = head_size // 2
    frequency = jnp.exp(
        jnp.arange(half_size, dtype=jnp.float32) * (-2.0 * math.log(10000.0) / head_size)
    )
    angles = positions.astype(jnp.float32)[:, None] * frequency[None, :]
    return (jnp.cos(angles), jnp.sin(angles))


def rope_pair(vectors, cosine_table, sine_table):
    half_size = vectors.shape[-1] // 2
    first_half = vectors[..., :half_size]
    second_half = vectors[..., half_size:]
    cos_wide = cosine_table[:, None, :]
    sin_wide = sine_table[:, None, :]
    return jnp.concatenate(
        [
            first_half * cos_wide - second_half * sin_wide,
            second_half * cos_wide + first_half * sin_wide,
        ],
        axis=-1,
    )


def request_of(index, group_requests, tok_count):
    scaled = index * group_requests
    if tok_count & (tok_count - 1) == 0:
        return lax.shift_right_logical(scaled, tok_count.bit_length() - 1)
    return scaled // tok_count


def head_picker(features, head):
    rows = lax.broadcasted_iota(jnp.int32, (features, HD), 0)
    cols = lax.broadcasted_iota(jnp.int32, (features, HD), 1)
    return (rows == cols + head * HD).astype(jnp.bfloat16)


def attention_kernel(
    meta_ref, q_ref, kc_ref, vc_ref, kn_ref, vn_ref, o_ref, kh_buf, vh_buf, qh_buf, acc_ref
):
    group_len = meta_ref[0]
    group_requests = meta_ref[1]
    head = pl.program_id(0)
    tok_count, features = q_ref.shape
    score_scale = 1.0 / math.sqrt(HD)
    picker = head_picker(features, head)

    def pick(values):
        return jnp.dot(values, picker, preferred_element_type=jnp.float32).astype(jnp.bfloat16)

    kh_buf[...] = pick(kc_ref[0, 0])
    vh_buf[...] = pick(vc_ref[0, 0])
    qh_buf[...] = pick(q_ref[...])
    kn = pick(kn_ref[0])
    vn = pick(vn_ref[0])
    dims = (((1,), (1,)), ((), ()))
    for chunk in range(tok_count // ROWS):
        rows = pl.ds(chunk * ROWS, ROWS)
        q = qh_buf[rows, :]
        s_old = lax.dot_general(q, kh_buf[...], dims, preferred_element_type=jnp.float32)
        s_new = lax.dot_general(q, kn, dims, preferred_element_type=jnp.float32)
        s_old = s_old * score_scale
        s_new = s_new * score_scale
        col = lax.broadcasted_iota(jnp.int32, s_old.shape, 1)
        s_old = jnp.where(col < group_len, s_old, -1e30)
        row = chunk * ROWS + lax.broadcasted_iota(jnp.int32, s_new.shape, 0)
        key = lax.broadcasted_iota(jnp.int32, s_new.shape, 1)
        same = request_of(row, group_requests, tok_count) == request_of(
            key, group_requests, tok_count
        )
        s_new = jnp.where(same & (key <= row), s_new, -1e30)
        peak = jnp.maximum(
            jnp.max(s_old, axis=1, keepdims=True), jnp.max(s_new, axis=1, keepdims=True)
        )
        e_old = jnp.exp(s_old - peak)
        e_new = jnp.exp(s_new - peak)
        total = jnp.sum(e_old, axis=1, keepdims=True) + jnp.sum(e_new, axis=1, keepdims=True)
        p_old = (e_old / total).astype(jnp.bfloat16)
        p_new = (e_new / total).astype(jnp.bfloat16)
        out = jnp.dot(p_old, vh_buf[...], preferred_element_type=jnp.float32) + jnp.dot(
            p_new, vn, preferred_element_type=jnp.float32
        )
        placed = lax.dot_general(
            out.astype(jnp.bfloat16), picker, dims, preferred_element_type=jnp.float32
        )

        @pl.when(head == 0)
        def _():
            acc_ref[rows, :] = placed

        @pl.when(head > 0)
        def _():
            acc_ref[rows, :] = acc_ref[rows, :] + placed

    @pl.when(head == pl.num_programs(0) - 1)
    def _():
        o_ref[...] = acc_ref[...].astype(jnp.bfloat16)


def attend(meta, queries, kv_cache, new_kv):
    tok_count, features = queries.shape
    cache_len = kv_cache.shape[2]
    full_q = pl.BlockSpec((tok_count, features), lambda h, m: (0, 0))
    cache_k = pl.BlockSpec((1, 1, cache_len, features), lambda h, m: (0, 0, 0, 0))
    cache_v = pl.BlockSpec((1, 1, cache_len, features), lambda h, m: (1, 0, 0, 0))
    new_k = pl.BlockSpec((1, tok_count, features), lambda h, m: (0, 0, 0))
    new_v = pl.BlockSpec((1, tok_count, features), lambda h, m: (1, 0, 0))
    return pl.pallas_call(
        attention_kernel,
        out_shape=jax.ShapeDtypeStruct(queries.shape, jnp.bfloat16),
        grid_spec=pltpu.PrefetchScalarGridSpec(
            num_scalar_prefetch=1,
            grid=(features // HD,),
            in_specs=[full_q, cache_k, cache_v, new_k, new_v],
            out_specs=full_q,
            scratch_shapes=[
                pltpu.VMEM((cache_len, HD), jnp.bfloat16),
                pltpu.VMEM((cache_len, HD), jnp.bfloat16),
                pltpu.VMEM((tok_count, HD), jnp.bfloat16),
                pltpu.VMEM((tok_count, features), jnp.float32),
            ],
        ),
    )(meta, queries, kv_cache, kv_cache, new_kv, new_kv)


def relay_kernel(meta_ref, own_c, own_n, mate_c, mate_n, out_ref):
    len_blocks = meta_ref[0]
    group_start = meta_ref[1]
    core = meta_ref[2]
    new_blocks = meta_ref[3]
    dest = pl.program_id(0)
    rank_count = 2 * pl.num_programs(0)
    features = own_n.shape[2]
    block = (2 * dest + core - group_start + rank_count) % rank_count
    old = block < len_blocks
    fresh = (block >= len_blocks) & (block < len_blocks + new_blocks)
    zero = jnp.zeros(own_n.shape[1:], own_n.dtype)
    first = core == 0
    for kv in range(2):
        mine = jnp.where(old, own_c[kv, 0], jnp.where(fresh, own_n[kv], zero))
        mate = jnp.where(old, mate_c[kv, 0], jnp.where(fresh, mate_n[kv], zero))
        out_ref[0, kv, :, :features] = jnp.where(first, mine, mate)
        out_ref[0, kv, :, features:] = jnp.where(first, mate, mine)


def relay(meta, kv_cache, new_kv, mate_cache, mate_new, seq_count):
    features = kv_cache.shape[3]
    new_blocks = new_kv.shape[1] // BLK
    rank_count = 2 * seq_count

    def block_of(d, m):
        return (2 * d + m[2] - m[1] + rank_count) % rank_count

    cache_spec = pl.BlockSpec(
        (2, 1, BLK, features),
        lambda d, m: (0, 0, jnp.clip(block_of(d, m), 0, m[0] - 1), 0),
    )
    new_spec = pl.BlockSpec(
        (2, BLK, features),
        lambda d, m: (0, jnp.clip(block_of(d, m) - m[0], 0, new_blocks - 1), 0),
    )
    return pl.pallas_call(
        relay_kernel,
        out_shape=jax.ShapeDtypeStruct((seq_count, 2, BLK, 2 * features), jnp.bfloat16),
        grid_spec=pltpu.PrefetchScalarGridSpec(
            num_scalar_prefetch=1,
            grid=(seq_count,),
            in_specs=[cache_spec, new_spec, cache_spec, new_spec],
            out_specs=pl.BlockSpec((1, 2, BLK, 2 * features), lambda d, m: (d, 0, 0, 0)),
        ),
    )(meta, kv_cache, new_kv, mate_cache, mate_new)


def half_swap(features):
    half = HD // 2
    rows = lax.broadcasted_iota(jnp.int32, (features, features), 0)
    cols = lax.broadcasted_iota(jnp.int32, (features, features), 1)
    first = cols % HD < half
    return jnp.where(
        first & (rows == cols + half),
        -1.0,
        jnp.where(jnp.logical_not(first) & (rows == cols - half), 1.0, 0.0),
    ).astype(jnp.bfloat16)


def projection_kernel(part_ref, x_ref, gain_ref, w_ref, cos_ref, sin_ref, *refs, parts):
    out_refs = refs[:-1]
    normed_ref = refs[-1]
    step = pl.program_id(0)

    @pl.when(step == 0)
    def _():
        inputs = x_ref[...].astype(jnp.float32)
        inverse_rms = lax.rsqrt(jnp.mean(inputs * inputs, axis=-1, keepdims=True) + 1e-05)
        normed_ref[...] = (inputs * inverse_rms * gain_ref[...]).astype(jnp.bfloat16)

    weights = w_ref[0]
    plain = jnp.dot(normed_ref[...], weights, preferred_element_type=jnp.float32)

    def rotated():
        features = plain.shape[1]
        half = HD // 2
        lane = lax.broadcasted_iota(jnp.int32, plain.shape, 1)
        ahead = pltpu.roll(plain, features - half, 1)
        behind = pltpu.roll(plain, half, 1)
        paired = jnp.where(lane % HD < half, -ahead, behind)
        return (plain * cos_ref[...] + paired * sin_ref[...]).astype(jnp.bfloat16)

    for index, part in enumerate(parts):

        @pl.when(step == index)
        def _():
            value = rotated() if part < 2 else plain.astype(jnp.bfloat16)
            out_refs[index][...] = value


def project(tokens, gain, weights, tables, parts):
    _, width, features = weights.shape
    rows = tokens.shape[0]
    full = pl.BlockSpec((rows, features), lambda s: (0, 0))
    table = jnp.asarray(parts, jnp.int32)
    out = jax.ShapeDtypeStruct((rows, features), jnp.bfloat16)
    return pl.pallas_call(
        functools.partial(projection_kernel, parts=parts),
        out_shape=tuple(out for _ in parts),
        grid_spec=pltpu.PrefetchScalarGridSpec(
            num_scalar_prefetch=1,
            grid=(len(parts),),
            in_specs=[
                pl.BlockSpec((rows, width), lambda s, t: (0, 0)),
                pl.BlockSpec((1, width), lambda s, t: (0, 0)),
                pl.BlockSpec((1, width, features), lambda s, t: (t[s], 0, 0)),
                pl.BlockSpec((rows, features), lambda s, t: (0, 0)),
                pl.BlockSpec((rows, features), lambda s, t: (0, 0)),
            ],
            out_specs=tuple(pl.BlockSpec((rows, features), lambda s, t: (0, 0)) for _ in parts),
            scratch_shapes=[pltpu.VMEM((rows, width), jnp.bfloat16)],
        ),
    )(table, tokens, gain, weights, *tables)


def local(tokens, norm_gain, w_qkv, w_out, kv_cache, cached_lengths, requests, block_start):
    group_idx = lax.axis_index("seq")
    tp_rank = lax.axis_index(("x", "core"))
    tp_count = lax.axis_size(("x", "core"))
    seq_count = lax.axis_size("seq")
    tok_count, model_width = tokens.shape
    features = w_qkv.shape[2]
    head_count = features // HD
    cache_len = kv_cache.shape[2]
    group_params = lax.dynamic_index_in_dim(
        jnp.stack([cached_lengths, requests, block_start], axis=1), group_idx, keepdims=False
    )
    group_len = group_params[0]
    group_requests = group_params[1]
    group_start = group_params[2]
    inputs = tokens.astype(jnp.float32)

    weights = jnp.transpose(w_qkv, (1, 0, 2))
    row_index = jnp.arange(tok_count, dtype=jnp.int32)
    request = row_index * group_requests // tok_count
    first_row = (request * tok_count + group_requests - 1) // group_requests
    positions = group_len + row_index - first_row
    half_size = HD // 2
    frequency = jnp.exp(
        jnp.arange(half_size, dtype=jnp.float32) * (-2.0 * math.log(10000.0) / HD)
    )
    angles = positions.astype(jnp.float32)[:, None] * jnp.tile(frequency, features // half_size)
    tables = (jnp.cos(angles), jnp.sin(angles))
    gain = norm_gain.astype(jnp.float32).reshape(1, model_width)
    core = lax.axis_index("core")
    swap_cores = [(0, 1), (1, 0)]
    mate_cache = lax.ppermute(kv_cache, "core", swap_cores)
    new_keys, new_values = project(tokens, gain, weights, tables, (1, 2))
    new_kv = jnp.stack([new_keys, new_values])
    mate_new = lax.ppermute(new_kv, "core", swap_cores)
    relay_meta = jnp.stack(
        [group_len // BLK, group_start, core, jnp.int32(tok_count // BLK)]
    ).astype(jnp.int32)
    joined = relay(relay_meta, kv_cache, new_kv, mate_cache, mate_new, seq_count)
    (queries,) = project(tokens, gain, weights, tables, (0,))
    joined, attn_kv = lax.optimization_barrier((joined, new_kv))
    received = lax.all_to_all(joined, "seq", 0, 0, tiled=True)
    decode_cache = received.transpose(1, 0, 2, 3).reshape(2, 1, seq_count, 1, BLK, 2 * features)

    attn_meta = jnp.stack([group_len, group_requests]).astype(jnp.int32)
    attended = attend(attn_meta, queries, kv_cache, attn_kv)
    rows_dev = tok_count // tp_count
    partial = jnp.dot(attended, w_out, preferred_element_type=jnp.float32).astype(jnp.bfloat16)
    x_count = tp_count // 2
    x_rank = lax.axis_index("x")
    by_owner = partial.reshape(x_count, 2, rows_dev, model_width)
    mine = lax.dynamic_index_in_dim(by_owner, core, 1, keepdims=False)
    theirs = lax.dynamic_index_in_dim(by_owner, 1 - core, 1, keepdims=False)
    pair_sum = mine.astype(jnp.float32) + lax.ppermute(theirs, "core", swap_cores).astype(
        jnp.float32
    )
    pair_sent = pair_sum.astype(jnp.bfloat16)
    summed = lax.dynamic_index_in_dim(pair_sum, x_rank, 0, keepdims=False)
    for shift in range(1, x_count):
        target = (x_rank + shift) % x_count
        chunk = lax.dynamic_index_in_dim(pair_sent, target, 0, keepdims=False)
        pairs = [(source, (source + shift) % x_count) for source in range(x_count)]
        summed = summed + lax.ppermute(chunk, "x", pairs).astype(jnp.float32)
    own_rows = lax.dynamic_slice_in_dim(inputs, tp_rank * rows_dev, rows_dev, 0)
    layer_out = (own_rows + summed).astype(jnp.bfloat16)
    return (layer_out, decode_cache)


def solution(mesh):
    seq_count, tp_count = mesh.devices.shape
    split = Mesh(mesh.devices.reshape(seq_count, tp_count // 2, 2), ("seq", "x", "core"))
    tp = ("x", "core")
    placed = (
        P("seq", None),
        P(),
        P(None, None, tp),
        P(tp, None),
        P(None, "seq", None, tp),
        P(),
        P(),
        P(),
    )
    return jax.shard_map(
        local,
        mesh=split,
        in_specs=placed,
        out_specs=(P(("seq",) + tp, None), P(None, "seq", None, None, None, tp)),
        check_vma=False,
    )
```

```python
import functools
import math

import jax
import jax.numpy as jnp
from jax import lax
from jax.experimental import pallas as pl
from jax.experimental.pallas import tpu as pltpu
from jax.sharding import Mesh
from jax.sharding import PartitionSpec as P

HD = 96
BLK = 128
ROWS = 128


def rope_tables(positions, head_size):
    half_size = head_size // 2
    frequency = jnp.exp(
        jnp.arange(half_size, dtype=jnp.float32) * (-2.0 * math.log(10000.0) / head_size)
    )
    angles = positions.astype(jnp.float32)[:, None] * frequency[None, :]
    return (jnp.cos(angles), jnp.sin(angles))


def rope_pair(vectors, cosine_table, sine_table):
    half_size = vectors.shape[-1] // 2
    first_half = vectors[..., :half_size]
    second_half = vectors[..., half_size:]
    cos_wide = cosine_table[:, None, :]
    sin_wide = sine_table[:, None, :]
    return jnp.concatenate(
        [
            first_half * cos_wide - second_half * sin_wide,
            second_half * cos_wide + first_half * sin_wide,
        ],
        axis=-1,
    )


def request_of(index, group_requests, tok_count):
    scaled = index * group_requests
    if tok_count & (tok_count - 1) == 0:
        return lax.shift_right_logical(scaled, tok_count.bit_length() - 1)
    return scaled // tok_count


def head_picker(features, head):
    rows = lax.broadcasted_iota(jnp.int32, (features, HD), 0)
    cols = lax.broadcasted_iota(jnp.int32, (features, HD), 1)
    return (rows == cols + head * HD).astype(jnp.bfloat16)


def attention_kernel(
    meta_ref, q_ref, kc_ref, vc_ref, kn_ref, vn_ref, o_ref, kh_buf, vh_buf, qh_buf, acc_ref
):
    group_len = meta_ref[0]
    group_requests = meta_ref[1]
    head = pl.program_id(0)
    tok_count, features = q_ref.shape
    score_scale = 1.0 / math.sqrt(HD)
    picker = head_picker(features, head)

    def pick(values):
        return jnp.dot(values, picker, preferred_element_type=jnp.float32).astype(jnp.bfloat16)

    kh_buf[...] = pick(kc_ref[0, 0])
    vh_buf[...] = pick(vc_ref[0, 0])
    qh_buf[...] = pick(q_ref[...])
    kn = pick(kn_ref[0])
    vn = pick(vn_ref[0])
    dims = (((1,), (1,)), ((), ()))
    for chunk in range(tok_count // ROWS):
        rows = pl.ds(chunk * ROWS, ROWS)
        q = qh_buf[rows, :]
        s_old = lax.dot_general(q, kh_buf[...], dims, preferred_element_type=jnp.float32)
        s_new = lax.dot_general(q, kn, dims, preferred_element_type=jnp.float32)
        s_old = s_old * score_scale
        s_new = s_new * score_scale
        col = lax.broadcasted_iota(jnp.int32, s_old.shape, 1)
        s_old = jnp.where(col < group_len, s_old, -1e30)
        row = chunk * ROWS + lax.broadcasted_iota(jnp.int32, s_new.shape, 0)
        key = lax.broadcasted_iota(jnp.int32, s_new.shape, 1)
        same = request_of(row, group_requests, tok_count) == request_of(
            key, group_requests, tok_count
        )
        s_new = jnp.where(same & (key <= row), s_new, -1e30)
        peak = jnp.maximum(
            jnp.max(s_old, axis=1, keepdims=True), jnp.max(s_new, axis=1, keepdims=True)
        )
        e_old = jnp.exp(s_old - peak)
        e_new = jnp.exp(s_new - peak)
        total = jnp.sum(e_old, axis=1, keepdims=True) + jnp.sum(e_new, axis=1, keepdims=True)
        p_old = (e_old / total).astype(jnp.bfloat16)
        p_new = (e_new / total).astype(jnp.bfloat16)
        out = jnp.dot(p_old, vh_buf[...], preferred_element_type=jnp.float32) + jnp.dot(
            p_new, vn, preferred_element_type=jnp.float32
        )
        placed = lax.dot_general(
            out.astype(jnp.bfloat16), picker, dims, preferred_element_type=jnp.float32
        )

        @pl.when(head == 0)
        def _():
            acc_ref[rows, :] = placed

        @pl.when(head > 0)
        def _():
            acc_ref[rows, :] = acc_ref[rows, :] + placed

    @pl.when(head == pl.num_programs(0) - 1)
    def _():
        o_ref[...] = acc_ref[...].astype(jnp.bfloat16)


def attend(meta, queries, kv_cache, new_kv):
    tok_count, features = queries.shape
    cache_len = kv_cache.shape[2]
    full_q = pl.BlockSpec((tok_count, features), lambda h, m: (0, 0))
    cache_k = pl.BlockSpec((1, 1, cache_len, features), lambda h, m: (0, 0, 0, 0))
    cache_v = pl.BlockSpec((1, 1, cache_len, features), lambda h, m: (1, 0, 0, 0))
    new_k = pl.BlockSpec((1, tok_count, features), lambda h, m: (0, 0, 0))
    new_v = pl.BlockSpec((1, tok_count, features), lambda h, m: (1, 0, 0))
    return pl.pallas_call(
        attention_kernel,
        out_shape=jax.ShapeDtypeStruct(queries.shape, jnp.bfloat16),
        grid_spec=pltpu.PrefetchScalarGridSpec(
            num_scalar_prefetch=1,
            grid=(features // HD,),
            in_specs=[full_q, cache_k, cache_v, new_k, new_v],
            out_specs=full_q,
            scratch_shapes=[
                pltpu.VMEM((cache_len, HD), jnp.bfloat16),
                pltpu.VMEM((cache_len, HD), jnp.bfloat16),
                pltpu.VMEM((tok_count, HD), jnp.bfloat16),
                pltpu.VMEM((tok_count, features), jnp.float32),
            ],
        ),
    )(meta, queries, kv_cache, kv_cache, new_kv, new_kv)


def relay_kernel(meta_ref, *refs):
    out_ref = refs[-1]
    sources = refs[:-1]
    len_blocks = meta_ref[0]
    group_start = meta_ref[1]
    core = meta_ref[2]
    new_blocks = meta_ref[3]
    per_step = out_ref.shape[0]
    rank_count = 2 * pl.num_programs(0) * per_step
    features = sources[1].shape[2]
    zero = jnp.zeros(sources[1].shape[1:], sources[1].dtype)
    first = core == 0
    for slot in range(per_step):
        own_c, own_n, mate_c, mate_n = sources[4 * slot : 4 * slot + 4]
        dest = pl.program_id(0) * per_step + slot
        block = (2 * dest + core - group_start + rank_count) % rank_count
        old = block < len_blocks
        fresh = (block >= len_blocks) & (block < len_blocks + new_blocks)
        for kv in range(2):
            mine = jnp.where(old, own_c[kv, 0], jnp.where(fresh, own_n[kv], zero))
            mate = jnp.where(old, mate_c[kv, 0], jnp.where(fresh, mate_n[kv], zero))
            out_ref[slot, kv, :, :features] = jnp.where(first, mine, mate)
            out_ref[slot, kv, :, features:] = jnp.where(first, mate, mine)


def relay(meta, kv_cache, new_kv, mate_cache, mate_new, seq_count):
    features = kv_cache.shape[3]
    new_blocks = new_kv.shape[1] // BLK
    rank_count = 2 * seq_count
    per_step = 2 if seq_count % 2 == 0 else 1

    def block_of(d, slot, m):
        return (2 * (d * per_step + slot) + m[2] - m[1] + rank_count) % rank_count

    def cache_spec(slot):
        return pl.BlockSpec(
            (2, 1, BLK, features),
            lambda d, m: (0, 0, jnp.clip(block_of(d, slot, m), 0, m[0] - 1), 0),
        )

    def new_spec(slot):
        return pl.BlockSpec(
            (2, BLK, features),
            lambda d, m: (0, jnp.clip(block_of(d, slot, m) - m[0], 0, new_blocks - 1), 0),
        )

    in_specs = []
    operands = []
    for slot in range(per_step):
        in_specs += [cache_spec(slot), new_spec(slot), cache_spec(slot), new_spec(slot)]
        operands += [kv_cache, new_kv, mate_cache, mate_new]
    return pl.pallas_call(
        relay_kernel,
        out_shape=jax.ShapeDtypeStruct((seq_count, 2, BLK, 2 * features), jnp.bfloat16),
        grid_spec=pltpu.PrefetchScalarGridSpec(
            num_scalar_prefetch=1,
            grid=(seq_count // per_step,),
            in_specs=in_specs,
            out_specs=pl.BlockSpec(
                (per_step, 2, BLK, 2 * features), lambda d, m: (d, 0, 0, 0)
            ),
        ),
    )(meta, *operands)


def half_swap(features):
    half = HD // 2
    rows = lax.broadcasted_iota(jnp.int32, (features, features), 0)
    cols = lax.broadcasted_iota(jnp.int32, (features, features), 1)
    first = cols % HD < half
    return jnp.where(
        first & (rows == cols + half),
        -1.0,
        jnp.where(jnp.logical_not(first) & (rows == cols - half), 1.0, 0.0),
    ).astype(jnp.bfloat16)


def projection_kernel(part_ref, x_ref, gain_ref, w_ref, cos_ref, sin_ref, *refs, parts):
    out_refs = refs[:-1]
    normed_ref = refs[-1]
    step = pl.program_id(0)

    @pl.when(step == 0)
    def _():
        inputs = x_ref[...].astype(jnp.float32)
        inverse_rms = lax.rsqrt(jnp.mean(inputs * inputs, axis=-1, keepdims=True) + 1e-05)
        normed_ref[...] = (inputs * inverse_rms * gain_ref[...]).astype(jnp.bfloat16)

    weights = w_ref[0]
    plain = jnp.dot(normed_ref[...], weights, preferred_element_type=jnp.float32)

    def rotated():
        features = plain.shape[1]
        half = HD // 2
        lane = lax.broadcasted_iota(jnp.int32, plain.shape, 1)
        ahead = pltpu.roll(plain, features - half, 1)
        behind = pltpu.roll(plain, half, 1)
        paired = jnp.where(lane % HD < half, -ahead, behind)
        return (plain * cos_ref[...] + paired * sin_ref[...]).astype(jnp.bfloat16)

    for index, part in enumerate(parts):

        @pl.when(step == index)
        def _():
            value = rotated() if part < 2 else plain.astype(jnp.bfloat16)
            out_refs[0][index] = value


def project(tokens, gain, weights, tables, parts):
    _, width, features = weights.shape
    rows = tokens.shape[0]
    full = pl.BlockSpec((rows, features), lambda s: (0, 0))
    table = jnp.asarray(parts, jnp.int32)
    out = jax.ShapeDtypeStruct((len(parts), rows, features), jnp.bfloat16)
    return pl.pallas_call(
        functools.partial(projection_kernel, parts=parts),
        out_shape=out,
        grid_spec=pltpu.PrefetchScalarGridSpec(
            num_scalar_prefetch=1,
            grid=(len(parts),),
            in_specs=[
                pl.BlockSpec((rows, width), lambda s, t: (0, 0)),
                pl.BlockSpec((1, width), lambda s, t: (0, 0)),
                pl.BlockSpec((1, width, features), lambda s, t: (t[s], 0, 0)),
                pl.BlockSpec((rows, features), lambda s, t: (0, 0)),
                pl.BlockSpec((rows, features), lambda s, t: (0, 0)),
            ],
            out_specs=pl.BlockSpec((len(parts), rows, features), lambda s, t: (0, 0, 0)),
            scratch_shapes=[pltpu.VMEM((rows, width), jnp.bfloat16)],
        ),
    )(table, tokens, gain, weights, *tables)


def local(tokens, norm_gain, w_qkv, w_out, kv_cache, cached_lengths, requests, block_start):
    group_idx = lax.axis_index("seq")
    tp_rank = lax.axis_index(("x", "core"))
    tp_count = lax.axis_size(("x", "core"))
    seq_count = lax.axis_size("seq")
    tok_count, model_width = tokens.shape
    features = w_qkv.shape[2]
    head_count = features // HD
    cache_len = kv_cache.shape[2]
    group_params = lax.dynamic_index_in_dim(
        jnp.stack([cached_lengths, requests, block_start], axis=1), group_idx, keepdims=False
    )
    group_len = group_params[0]
    group_requests = group_params[1]
    group_start = group_params[2]
    inputs = tokens.astype(jnp.float32)

    weights = jnp.transpose(w_qkv, (1, 0, 2))
    row_index = jnp.arange(tok_count, dtype=jnp.int32)
    request = row_index * group_requests // tok_count
    first_row = (request * tok_count + group_requests - 1) // group_requests
    positions = group_len + row_index - first_row
    half_size = HD // 2
    frequency = jnp.exp(
        jnp.arange(half_size, dtype=jnp.float32) * (-2.0 * math.log(10000.0) / HD)
    )
    angles = positions.astype(jnp.float32)[:, None] * frequency[None, :]
    repeat = (1, features // half_size)
    tables = (jnp.tile(jnp.cos(angles), repeat), jnp.tile(jnp.sin(angles), repeat))
    gain = norm_gain.astype(jnp.float32).reshape(1, model_width)
    core = lax.axis_index("core")
    swap_cores = [(0, 1), (1, 0)]
    mate_cache = lax.ppermute(kv_cache, "core", swap_cores)
    new_kv = project(tokens, gain, weights, tables, (1, 2))
    mate_new = lax.ppermute(new_kv, "core", swap_cores)
    relay_meta = jnp.stack(
        [group_len // BLK, group_start, core, jnp.int32(tok_count // BLK)]
    ).astype(jnp.int32)
    joined = relay(relay_meta, kv_cache, new_kv, mate_cache, mate_new, seq_count)
    queries = project(tokens, gain, weights, tables, (0,))[0]
    joined, attn_kv = lax.optimization_barrier((joined, new_kv))
    received = lax.all_to_all(joined, "seq", 0, 0, tiled=True)
    decode_cache = received.transpose(1, 0, 2, 3).reshape(2, 1, seq_count, 1, BLK, 2 * features)

    attn_meta = jnp.stack([group_len, group_requests]).astype(jnp.int32)
    attended = attend(attn_meta, queries, kv_cache, attn_kv)
    rows_dev = tok_count // tp_count
    partial = jnp.dot(attended, w_out, preferred_element_type=jnp.float32).astype(jnp.bfloat16)
    x_count = tp_count // 2
    x_rank = lax.axis_index("x")
    by_owner = partial.reshape(x_count, 2, rows_dev, model_width)
    mine = lax.dynamic_index_in_dim(by_owner, core, 1, keepdims=False)
    theirs = lax.dynamic_index_in_dim(by_owner, 1 - core, 1, keepdims=False)
    pair_sum = mine.astype(jnp.float32) + lax.ppermute(theirs, "core", swap_cores).astype(
        jnp.float32
    )
    pair_sent = pair_sum.astype(jnp.bfloat16)
    summed = lax.dynamic_index_in_dim(pair_sum, x_rank, 0, keepdims=False)
    for shift in range(1, x_count):
        target = (x_rank + shift) % x_count
        chunk = lax.dynamic_index_in_dim(pair_sent, target, 0, keepdims=False)
        pairs = [(source, (source + shift) % x_count) for source in range(x_count)]
        summed = summed + lax.ppermute(chunk, "x", pairs).astype(jnp.float32)
    own_rows = lax.dynamic_slice_in_dim(inputs, tp_rank * rows_dev, rows_dev, 0)
    layer_out = (own_rows + summed).astype(jnp.bfloat16)
    return (layer_out, decode_cache)


def solution(mesh):
    seq_count, tp_count = mesh.devices.shape
    split = Mesh(mesh.devices.reshape(seq_count, tp_count // 2, 2), ("seq", "x", "core"))
    tp = ("x", "core")
    placed = (
        P("seq", None),
        P(),
        P(None, None, tp),
        P(tp, None),
        P(None, "seq", None, tp),
        P(),
        P(),
        P(),
    )
    return jax.shard_map(
        local,
        mesh=split,
        in_specs=placed,
        out_specs=(P(("seq",) + tp, None), P(None, "seq", None, None, None, tp)),
        check_vma=False,
    )
```

```python
import functools
import math

import jax
import jax.numpy as jnp
from jax import lax
from jax.experimental import pallas as pl
from jax.experimental.pallas import tpu as pltpu
from jax.sharding import Mesh
from jax.sharding import PartitionSpec as P

HD = 96
BLK = 128
ROWS = 128


def rope_tables(positions, head_size):
    half_size = head_size // 2
    frequency = jnp.exp(
        jnp.arange(half_size, dtype=jnp.float32) * (-2.0 * math.log(10000.0) / head_size)
    )
    angles = positions.astype(jnp.float32)[:, None] * frequency[None, :]
    return (jnp.cos(angles), jnp.sin(angles))


def rope_pair(vectors, cosine_table, sine_table):
    half_size = vectors.shape[-1] // 2
    first_half = vectors[..., :half_size]
    second_half = vectors[..., half_size:]
    cos_wide = cosine_table[:, None, :]
    sin_wide = sine_table[:, None, :]
    return jnp.concatenate(
        [
            first_half * cos_wide - second_half * sin_wide,
            second_half * cos_wide + first_half * sin_wide,
        ],
        axis=-1,
    )


def request_of(index, group_requests, tok_count):
    scaled = index * group_requests
    if tok_count & (tok_count - 1) == 0:
        return lax.shift_right_logical(scaled, tok_count.bit_length() - 1)
    return scaled // tok_count


def head_picker(features, head):
    rows = lax.broadcasted_iota(jnp.int32, (features, HD), 0)
    cols = lax.broadcasted_iota(jnp.int32, (features, HD), 1)
    return (rows == cols + head * HD).astype(jnp.bfloat16)


def attention_kernel(
    meta_ref, q_ref, kc_ref, vc_ref, kn_ref, vn_ref, o_ref, kh_buf, vh_buf, qh_buf, acc_ref
):
    group_len = meta_ref[0]
    group_requests = meta_ref[1]
    head = pl.program_id(0)
    tok_count, features = q_ref.shape
    score_scale = 1.0 / math.sqrt(HD)
    picker = head_picker(features, head)

    def pick(values):
        return jnp.dot(values, picker, preferred_element_type=jnp.float32).astype(jnp.bfloat16)

    kh_buf[...] = pick(kc_ref[0, 0])
    vh_buf[...] = pick(vc_ref[0, 0])
    qh_buf[...] = pick(q_ref[...])
    kn = pick(kn_ref[0])
    vn = pick(vn_ref[0])
    dims = (((1,), (1,)), ((), ()))
    for chunk in range(tok_count // ROWS):
        rows = pl.ds(chunk * ROWS, ROWS)
        q = qh_buf[rows, :]
        s_old = lax.dot_general(q, kh_buf[...], dims, preferred_element_type=jnp.float32)
        s_new = lax.dot_general(q, kn, dims, preferred_element_type=jnp.float32)
        s_old = s_old * score_scale
        s_new = s_new * score_scale
        col = lax.broadcasted_iota(jnp.int32, s_old.shape, 1)
        s_old = jnp.where(col < group_len, s_old, -1e30)
        row = chunk * ROWS + lax.broadcasted_iota(jnp.int32, s_new.shape, 0)
        key = lax.broadcasted_iota(jnp.int32, s_new.shape, 1)
        same = request_of(row, group_requests, tok_count) == request_of(
            key, group_requests, tok_count
        )
        s_new = jnp.where(same & (key <= row), s_new, -1e30)
        peak = jnp.maximum(
            jnp.max(s_old, axis=1, keepdims=True), jnp.max(s_new, axis=1, keepdims=True)
        )
        e_old = jnp.exp(s_old - peak)
        e_new = jnp.exp(s_new - peak)
        total = jnp.sum(e_old, axis=1, keepdims=True) + jnp.sum(e_new, axis=1, keepdims=True)
        p_old = (e_old / total).astype(jnp.bfloat16)
        p_new = (e_new / total).astype(jnp.bfloat16)
        out = jnp.dot(p_old, vh_buf[...], preferred_element_type=jnp.float32) + jnp.dot(
            p_new, vn, preferred_element_type=jnp.float32
        )
        placed = lax.dot_general(
            out.astype(jnp.bfloat16), picker, dims, preferred_element_type=jnp.float32
        )

        @pl.when(head == 0)
        def _():
            acc_ref[rows, :] = placed

        @pl.when(head > 0)
        def _():
            acc_ref[rows, :] = acc_ref[rows, :] + placed

    @pl.when(head == pl.num_programs(0) - 1)
    def _():
        o_ref[...] = acc_ref[...].astype(jnp.bfloat16)


def attend(meta, queries, kv_cache, new_kv):
    tok_count, features = queries.shape
    cache_len = kv_cache.shape[2]
    full_q = pl.BlockSpec((tok_count, features), lambda h, m: (0, 0))
    cache_k = pl.BlockSpec((1, 1, cache_len, features), lambda h, m: (0, 0, 0, 0))
    cache_v = pl.BlockSpec((1, 1, cache_len, features), lambda h, m: (1, 0, 0, 0))
    new_k = pl.BlockSpec((1, tok_count, features), lambda h, m: (0, 0, 0))
    new_v = pl.BlockSpec((1, tok_count, features), lambda h, m: (1, 0, 0))
    return pl.pallas_call(
        attention_kernel,
        out_shape=jax.ShapeDtypeStruct(queries.shape, jnp.bfloat16),
        grid_spec=pltpu.PrefetchScalarGridSpec(
            num_scalar_prefetch=1,
            grid=(features // HD,),
            in_specs=[full_q, cache_k, cache_v, new_k, new_v],
            out_specs=full_q,
            scratch_shapes=[
                pltpu.VMEM((cache_len, HD), jnp.bfloat16),
                pltpu.VMEM((cache_len, HD), jnp.bfloat16),
                pltpu.VMEM((tok_count, HD), jnp.bfloat16),
                pltpu.VMEM((tok_count, features), jnp.float32),
            ],
        ),
    )(meta, queries, kv_cache, kv_cache, new_kv, new_kv)


def relay_kernel(meta_ref, *refs, new_blocks):
    out_ref = refs[-1]
    sources = refs[:-1]
    len_blocks = meta_ref[0] // BLK
    group_start = meta_ref[2]
    core = meta_ref[3]
    per_step = out_ref.shape[0]
    rank_count = 2 * pl.num_programs(0) * per_step
    features = sources[1].shape[2]
    zero = jnp.zeros(sources[1].shape[1:], sources[1].dtype)
    first = core == 0
    for slot in range(per_step):
        own_c, own_n, mate_c, mate_n = sources[4 * slot : 4 * slot + 4]
        dest = pl.program_id(0) * per_step + slot
        block = (2 * dest + core - group_start + rank_count) % rank_count
        old = block < len_blocks
        fresh = (block >= len_blocks) & (block < len_blocks + new_blocks)
        for kv in range(2):
            mine = jnp.where(old, own_c[kv, 0], jnp.where(fresh, own_n[kv], zero))
            mate = jnp.where(old, mate_c[kv, 0], jnp.where(fresh, mate_n[kv], zero))
            out_ref[slot, kv, :, :features] = jnp.where(first, mine, mate)
            out_ref[slot, kv, :, features:] = jnp.where(first, mate, mine)


def relay(meta, kv_cache, new_kv, mate_cache, mate_new, seq_count):
    features = kv_cache.shape[3]
    new_blocks = new_kv.shape[1] // BLK
    rank_count = 2 * seq_count
    per_step = 2 if seq_count % 2 == 0 else 1

    def block_of(d, slot, m):
        return (2 * (d * per_step + slot) + m[3] - m[2] + rank_count) % rank_count

    def cache_spec(slot):
        return pl.BlockSpec(
            (2, 1, BLK, features),
            lambda d, m: (0, 0, jnp.clip(block_of(d, slot, m), 0, m[0] // BLK - 1), 0),
        )

    def new_spec(slot):
        return pl.BlockSpec(
            (2, BLK, features),
            lambda d, m: (
                0,
                jnp.clip(block_of(d, slot, m) - m[0] // BLK, 0, new_blocks - 1),
                0,
            ),
        )

    in_specs = []
    operands = []
    for slot in range(per_step):
        in_specs += [cache_spec(slot), new_spec(slot), cache_spec(slot), new_spec(slot)]
        operands += [kv_cache, new_kv, mate_cache, mate_new]
    return pl.pallas_call(
        functools.partial(relay_kernel, new_blocks=new_blocks),
        out_shape=jax.ShapeDtypeStruct((seq_count, 2, BLK, 2 * features), jnp.bfloat16),
        grid_spec=pltpu.PrefetchScalarGridSpec(
            num_scalar_prefetch=1,
            grid=(seq_count // per_step,),
            in_specs=in_specs,
            out_specs=pl.BlockSpec(
                (per_step, 2, BLK, 2 * features), lambda d, m: (d, 0, 0, 0)
            ),
        ),
    )(meta, *operands)


def half_swap(features):
    half = HD // 2
    rows = lax.broadcasted_iota(jnp.int32, (features, features), 0)
    cols = lax.broadcasted_iota(jnp.int32, (features, features), 1)
    first = cols % HD < half
    return jnp.where(
        first & (rows == cols + half),
        -1.0,
        jnp.where(jnp.logical_not(first) & (rows == cols - half), 1.0, 0.0),
    ).astype(jnp.bfloat16)


def projection_kernel(part_ref, meta_ref, x_ref, gain_ref, w_ref, freq_ref, *refs, parts):
    out_refs = refs[:-1]
    normed_ref = refs[-1]
    step = pl.program_id(0)

    @pl.when(step == 0)
    def _():
        inputs = x_ref[...].astype(jnp.float32)
        inverse_rms = lax.rsqrt(jnp.mean(inputs * inputs, axis=-1, keepdims=True) + 1e-05)
        normed_ref[...] = (inputs * inverse_rms * gain_ref[...]).astype(jnp.bfloat16)

    weights = w_ref[0]
    plain = jnp.dot(normed_ref[...], weights, preferred_element_type=jnp.float32)

    def rotated():
        rows, features = plain.shape
        half = HD // 2
        group_len = meta_ref[0]
        group_requests = meta_ref[1]
        row = lax.broadcasted_iota(jnp.int32, (rows, 1), 0)
        request = request_of(row, group_requests, rows)
        count = (jnp.zeros((rows, 1), jnp.int32) + group_requests).astype(jnp.float32)
        first = jnp.ceil((request * rows).astype(jnp.float32) / count).astype(jnp.int32)
        positions = (group_len + row - first).astype(jnp.float32)
        angles = positions * freq_ref[...]
        lane = lax.broadcasted_iota(jnp.int32, plain.shape, 1)
        ahead = pltpu.roll(plain, features - half, 1)
        behind = pltpu.roll(plain, half, 1)
        paired = jnp.where(lane % HD < half, -ahead, behind)
        return (plain * jnp.cos(angles) + paired * jnp.sin(angles)).astype(jnp.bfloat16)

    for index, part in enumerate(parts):

        @pl.when(step == index)
        def _():
            value = rotated() if part < 2 else plain.astype(jnp.bfloat16)
            out_refs[0][index] = value


def project(meta, tokens, gain, weights, frequency, parts):
    _, width, features = weights.shape
    rows = tokens.shape[0]
    table = jnp.asarray(parts, jnp.int32)
    out = jax.ShapeDtypeStruct((len(parts), rows, features), jnp.bfloat16)
    return pl.pallas_call(
        functools.partial(projection_kernel, parts=parts),
        out_shape=out,
        grid_spec=pltpu.PrefetchScalarGridSpec(
            num_scalar_prefetch=2,
            grid=(len(parts),),
            in_specs=[
                pl.BlockSpec((rows, width), lambda s, t, m: (0, 0)),
                pl.BlockSpec((1, width), lambda s, t, m: (0, 0)),
                pl.BlockSpec((1, width, features), lambda s, t, m: (t[s], 0, 0)),
                pl.BlockSpec((1, features), lambda s, t, m: (0, 0)),
            ],
            out_specs=pl.BlockSpec((len(parts), rows, features), lambda s, t, m: (0, 0, 0)),
            scratch_shapes=[pltpu.VMEM((rows, width), jnp.bfloat16)],
        ),
    )(table, meta, tokens, gain, weights, frequency)


def local(tokens, norm_gain, w_qkv, w_out, kv_cache, cached_lengths, requests, block_start):
    group_idx = lax.axis_index("seq")
    tp_rank = lax.axis_index(("x", "core"))
    tp_count = lax.axis_size(("x", "core"))
    seq_count = lax.axis_size("seq")
    tok_count, model_width = tokens.shape
    features = w_qkv.shape[2]
    head_count = features // HD
    cache_len = kv_cache.shape[2]
    group_params = lax.dynamic_index_in_dim(
        jnp.stack([cached_lengths, requests, block_start], axis=1), group_idx, keepdims=False
    )
    group_len = group_params[0]
    group_requests = group_params[1]
    group_start = group_params[2]
    inputs = tokens.astype(jnp.float32)

    weights = jnp.transpose(w_qkv, (1, 0, 2))
    half_size = HD // 2
    frequency = jnp.exp(
        jnp.arange(half_size, dtype=jnp.float32) * (-2.0 * math.log(10000.0) / HD)
    )
    frequency = jnp.tile(frequency, features // half_size).reshape(1, features)
    gain = norm_gain.astype(jnp.float32).reshape(1, model_width)
    core = lax.axis_index("core")
    swap_cores = [(0, 1), (1, 0)]
    mate_cache = lax.ppermute(kv_cache, "core", swap_cores)
    meta = jnp.concatenate([group_params, jnp.reshape(core, (1,))]).astype(jnp.int32)
    new_kv = project(meta, tokens, gain, weights, frequency, (1, 2))
    mate_new = lax.ppermute(new_kv, "core", swap_cores)
    joined = relay(meta, kv_cache, new_kv, mate_cache, mate_new, seq_count)
    queries = project(meta, tokens, gain, weights, frequency, (0,))[0]
    joined, attn_kv = lax.optimization_barrier((joined, new_kv))
    received = lax.all_to_all(joined, "seq", 0, 0, tiled=True)
    decode_cache = received.transpose(1, 0, 2, 3).reshape(2, 1, seq_count, 1, BLK, 2 * features)

    attended = attend(meta, queries, kv_cache, attn_kv)
    rows_dev = tok_count // tp_count
    partial = jnp.dot(attended, w_out, preferred_element_type=jnp.float32).astype(jnp.bfloat16)
    x_count = tp_count // 2
    x_rank = lax.axis_index("x")
    by_owner = partial.reshape(x_count, 2, rows_dev, model_width)
    mine = lax.dynamic_index_in_dim(by_owner, core, 1, keepdims=False)
    theirs = lax.dynamic_index_in_dim(by_owner, 1 - core, 1, keepdims=False)
    pair_sum = mine.astype(jnp.float32) + lax.ppermute(theirs, "core", swap_cores).astype(
        jnp.float32
    )
    pair_sent = pair_sum.astype(jnp.bfloat16)
    summed = lax.dynamic_index_in_dim(pair_sum, x_rank, 0, keepdims=False)
    for shift in range(1, x_count):
        target = (x_rank + shift) % x_count
        chunk = lax.dynamic_index_in_dim(pair_sent, target, 0, keepdims=False)
        pairs = [(source, (source + shift) % x_count) for source in range(x_count)]
        summed = summed + lax.ppermute(chunk, "x", pairs).astype(jnp.float32)
    own_rows = lax.dynamic_slice_in_dim(inputs, tp_rank * rows_dev, rows_dev, 0)
    layer_out = (own_rows + summed).astype(jnp.bfloat16)
    return (layer_out, decode_cache)


def solution(mesh):
    seq_count, tp_count = mesh.devices.shape
    split = Mesh(mesh.devices.reshape(seq_count, tp_count // 2, 2), ("seq", "x", "core"))
    tp = ("x", "core")
    placed = (
        P("seq", None),
        P(),
        P(None, None, tp),
        P(tp, None),
        P(None, "seq", None, tp),
        P(),
        P(),
        P(),
    )
    return jax.shard_map(
        local,
        mesh=split,
        in_specs=placed,
        out_specs=(P(("seq",) + tp, None), P(None, "seq", None, None, None, tp)),
        check_vma=False,
    )
```

```python
import functools
import math

import jax
import jax.numpy as jnp
from jax import lax
from jax.experimental import pallas as pl
from jax.experimental.pallas import tpu as pltpu
from jax.sharding import Mesh
from jax.sharding import PartitionSpec as P

HD = 96
BLK = 128
ROWS = 128


def rope_tables(positions, head_size):
    half_size = head_size // 2
    frequency = jnp.exp(
        jnp.arange(half_size, dtype=jnp.float32) * (-2.0 * math.log(10000.0) / head_size)
    )
    angles = positions.astype(jnp.float32)[:, None] * frequency[None, :]
    return (jnp.cos(angles), jnp.sin(angles))


def rope_pair(vectors, cosine_table, sine_table):
    half_size = vectors.shape[-1] // 2
    first_half = vectors[..., :half_size]
    second_half = vectors[..., half_size:]
    cos_wide = cosine_table[:, None, :]
    sin_wide = sine_table[:, None, :]
    return jnp.concatenate(
        [
            first_half * cos_wide - second_half * sin_wide,
            second_half * cos_wide + first_half * sin_wide,
        ],
        axis=-1,
    )


def request_of(index, group_requests, tok_count):
    scaled = index * group_requests
    if tok_count & (tok_count - 1) == 0:
        return lax.shift_right_logical(scaled, tok_count.bit_length() - 1)
    return scaled // tok_count


def head_picker(features, head):
    rows = lax.broadcasted_iota(jnp.int32, (features, HD), 0)
    cols = lax.broadcasted_iota(jnp.int32, (features, HD), 1)
    return (rows == cols + head * HD).astype(jnp.bfloat16)


def attention_kernel(
    meta_ref, q_ref, kc_ref, vc_ref, kn_ref, vn_ref, o_ref, kh_buf, vh_buf, qh_buf, acc_ref
):
    group_len = meta_ref[0]
    group_requests = meta_ref[1]
    head = pl.program_id(0)
    tok_count, features = q_ref.shape
    score_scale = 1.0 / math.sqrt(HD)
    picker = head_picker(features, head)

    def pick(values):
        return jnp.dot(values, picker, preferred_element_type=jnp.float32).astype(jnp.bfloat16)

    kh_buf[...] = pick(kc_ref[0, 0])
    vh_buf[...] = pick(vc_ref[0, 0])
    qh_buf[...] = pick(q_ref[...])
    kn = pick(kn_ref[0])
    vn = pick(vn_ref[0])
    dims = (((1,), (1,)), ((), ()))
    for chunk in range(tok_count // ROWS):
        rows = pl.ds(chunk * ROWS, ROWS)
        q = qh_buf[rows, :]
        s_old = lax.dot_general(q, kh_buf[...], dims, preferred_element_type=jnp.float32)
        s_new = lax.dot_general(q, kn, dims, preferred_element_type=jnp.float32)
        s_old = s_old * score_scale
        s_new = s_new * score_scale
        col = lax.broadcasted_iota(jnp.int32, s_old.shape, 1)
        s_old = jnp.where(col < group_len, s_old, -1e30)
        row = chunk * ROWS + lax.broadcasted_iota(jnp.int32, s_new.shape, 0)
        key = lax.broadcasted_iota(jnp.int32, s_new.shape, 1)
        same = request_of(row, group_requests, tok_count) == request_of(
            key, group_requests, tok_count
        )
        s_new = jnp.where(same & (key <= row), s_new, -1e30)
        peak = jnp.maximum(
            jnp.max(s_old, axis=1, keepdims=True), jnp.max(s_new, axis=1, keepdims=True)
        )
        e_old = jnp.exp(s_old - peak)
        e_new = jnp.exp(s_new - peak)
        total = jnp.sum(e_old, axis=1, keepdims=True) + jnp.sum(e_new, axis=1, keepdims=True)
        p_old = (e_old / total).astype(jnp.bfloat16)
        p_new = (e_new / total).astype(jnp.bfloat16)
        out = jnp.dot(p_old, vh_buf[...], preferred_element_type=jnp.float32) + jnp.dot(
            p_new, vn, preferred_element_type=jnp.float32
        )
        placed = lax.dot_general(
            out.astype(jnp.bfloat16), picker, dims, preferred_element_type=jnp.float32
        )

        @pl.when(head == 0)
        def _():
            acc_ref[rows, :] = placed

        @pl.when(head > 0)
        def _():
            acc_ref[rows, :] = acc_ref[rows, :] + placed

    @pl.when(head == pl.num_programs(0) - 1)
    def _():
        o_ref[...] = acc_ref[...].astype(jnp.bfloat16)


def attend(meta, queries, kv_cache, new_kv):
    tok_count, features = queries.shape
    cache_len = kv_cache.shape[2]
    full_q = pl.BlockSpec((tok_count, features), lambda h, m: (0, 0))
    cache_k = pl.BlockSpec((1, 1, cache_len, features), lambda h, m: (0, 0, 0, 0))
    cache_v = pl.BlockSpec((1, 1, cache_len, features), lambda h, m: (1, 0, 0, 0))
    new_k = pl.BlockSpec((1, tok_count, features), lambda h, m: (0, 0, 0))
    new_v = pl.BlockSpec((1, tok_count, features), lambda h, m: (1, 0, 0))
    return pl.pallas_call(
        attention_kernel,
        out_shape=jax.ShapeDtypeStruct(queries.shape, jnp.bfloat16),
        grid_spec=pltpu.PrefetchScalarGridSpec(
            num_scalar_prefetch=1,
            grid=(features // HD,),
            in_specs=[full_q, cache_k, cache_v, new_k, new_v],
            out_specs=full_q,
            scratch_shapes=[
                pltpu.VMEM((cache_len, HD), jnp.bfloat16),
                pltpu.VMEM((cache_len, HD), jnp.bfloat16),
                pltpu.VMEM((tok_count, HD), jnp.bfloat16),
                pltpu.VMEM((tok_count, features), jnp.float32),
            ],
        ),
    )(meta, queries, kv_cache, kv_cache, new_kv, new_kv)


def relay_kernel(meta_ref, *refs, new_blocks):
    out_ref = refs[-1]
    sources = refs[:-1]
    len_blocks = meta_ref[0] // BLK
    group_start = meta_ref[2]
    core = meta_ref[3]
    per_step = out_ref.shape[0]
    rank_count = 2 * pl.num_programs(0) * per_step
    features = sources[1].shape[2]
    zero = jnp.zeros(sources[1].shape[1:], sources[1].dtype)
    first = core == 0
    for slot in range(per_step):
        own_c, own_n, mate_c, mate_n = sources[4 * slot : 4 * slot + 4]
        dest = pl.program_id(0) * per_step + slot
        block = (2 * dest + core - group_start + rank_count) % rank_count
        old = block < len_blocks
        fresh = (block >= len_blocks) & (block < len_blocks + new_blocks)
        for kv in range(2):
            mine = jnp.where(old, own_c[kv, 0], jnp.where(fresh, own_n[kv], zero))
            mate = jnp.where(old, mate_c[kv, 0], jnp.where(fresh, mate_n[kv], zero))
            out_ref[slot, kv, :, :features] = jnp.where(first, mine, mate)
            out_ref[slot, kv, :, features:] = jnp.where(first, mate, mine)


def relay(meta, kv_cache, new_kv, mate_cache, mate_new, seq_count):
    features = kv_cache.shape[3]
    new_blocks = new_kv.shape[1] // BLK
    rank_count = 2 * seq_count
    per_step = 4 if seq_count % 4 == 0 else 1

    def block_of(d, slot, m):
        return (2 * (d * per_step + slot) + m[3] - m[2] + rank_count) % rank_count

    def cache_spec(slot):
        return pl.BlockSpec(
            (2, 1, BLK, features),
            lambda d, m: (0, 0, jnp.clip(block_of(d, slot, m), 0, m[0] // BLK - 1), 0),
        )

    def new_spec(slot):
        return pl.BlockSpec(
            (2, BLK, features),
            lambda d, m: (
                0,
                jnp.clip(block_of(d, slot, m) - m[0] // BLK, 0, new_blocks - 1),
                0,
            ),
        )

    in_specs = []
    operands = []
    for slot in range(per_step):
        in_specs += [cache_spec(slot), new_spec(slot), cache_spec(slot), new_spec(slot)]
        operands += [kv_cache, new_kv, mate_cache, mate_new]
    return pl.pallas_call(
        functools.partial(relay_kernel, new_blocks=new_blocks),
        out_shape=jax.ShapeDtypeStruct((seq_count, 2, BLK, 2 * features), jnp.bfloat16),
        grid_spec=pltpu.PrefetchScalarGridSpec(
            num_scalar_prefetch=1,
            grid=(seq_count // per_step,),
            in_specs=in_specs,
            out_specs=pl.BlockSpec(
                (per_step, 2, BLK, 2 * features), lambda d, m: (d, 0, 0, 0)
            ),
        ),
    )(meta, *operands)


def half_swap(features):
    half = HD // 2
    rows = lax.broadcasted_iota(jnp.int32, (features, features), 0)
    cols = lax.broadcasted_iota(jnp.int32, (features, features), 1)
    first = cols % HD < half
    return jnp.where(
        first & (rows == cols + half),
        -1.0,
        jnp.where(jnp.logical_not(first) & (rows == cols - half), 1.0, 0.0),
    ).astype(jnp.bfloat16)


def projection_kernel(part_ref, meta_ref, x_ref, gain_ref, w_ref, freq_ref, *refs, parts):
    out_refs = refs[:-1]
    normed_ref = refs[-1]
    step = pl.program_id(0)

    @pl.when(step == 0)
    def _():
        inputs = x_ref[...].astype(jnp.float32)
        inverse_rms = lax.rsqrt(jnp.mean(inputs * inputs, axis=-1, keepdims=True) + 1e-05)
        gain = gain_ref[...].astype(jnp.float32)
        normed_ref[...] = (inputs * inverse_rms * gain).astype(jnp.bfloat16)

    weights = w_ref[0]
    plain = jnp.dot(normed_ref[...], weights, preferred_element_type=jnp.float32)

    def rotated():
        rows, features = plain.shape
        half = HD // 2
        group_len = meta_ref[0]
        group_requests = meta_ref[1]
        row = lax.broadcasted_iota(jnp.int32, (rows, 1), 0)
        request = request_of(row, group_requests, rows)
        count = (jnp.zeros((rows, 1), jnp.int32) + group_requests).astype(jnp.float32)
        first = jnp.ceil((request * rows).astype(jnp.float32) / count).astype(jnp.int32)
        positions = (group_len + row - first).astype(jnp.float32)
        angles = positions * freq_ref[...]
        lane = lax.broadcasted_iota(jnp.int32, plain.shape, 1)
        ahead = pltpu.roll(plain, features - half, 1)
        behind = pltpu.roll(plain, half, 1)
        paired = jnp.where(lane % HD < half, -ahead, behind)
        return (plain * jnp.cos(angles) + paired * jnp.sin(angles)).astype(jnp.bfloat16)

    for index, part in enumerate(parts):

        @pl.when(step == index)
        def _():
            value = rotated() if part < 2 else plain.astype(jnp.bfloat16)
            out_refs[0][index] = value


def project(meta, tokens, gain, weights, frequency, parts):
    _, width, features = weights.shape
    rows = tokens.shape[0]
    table = jnp.asarray(parts, jnp.int32)
    out = jax.ShapeDtypeStruct((len(parts), rows, features), jnp.bfloat16)
    return pl.pallas_call(
        functools.partial(projection_kernel, parts=parts),
        out_shape=out,
        grid_spec=pltpu.PrefetchScalarGridSpec(
            num_scalar_prefetch=2,
            grid=(len(parts),),
            in_specs=[
                pl.BlockSpec((rows, width), lambda s, t, m: (0, 0)),
                pl.BlockSpec((1, width), lambda s, t, m: (0, 0)),
                pl.BlockSpec((1, width, features), lambda s, t, m: (t[s], 0, 0)),
                pl.BlockSpec((1, features), lambda s, t, m: (0, 0)),
            ],
            out_specs=pl.BlockSpec((len(parts), rows, features), lambda s, t, m: (0, 0, 0)),
            scratch_shapes=[pltpu.VMEM((rows, width), jnp.bfloat16)],
        ),
    )(table, meta, tokens, gain, weights, frequency)


def local(tokens, norm_gain, w_qkv, w_out, kv_cache, cached_lengths, requests, block_start):
    group_idx = lax.axis_index("seq")
    tp_rank = lax.axis_index(("x", "core"))
    tp_count = lax.axis_size(("x", "core"))
    seq_count = lax.axis_size("seq")
    tok_count, model_width = tokens.shape
    features = w_qkv.shape[2]
    head_count = features // HD
    cache_len = kv_cache.shape[2]
    group_params = lax.dynamic_index_in_dim(
        jnp.stack([cached_lengths, requests, block_start], axis=1), group_idx, keepdims=False
    )
    group_len = group_params[0]
    group_requests = group_params[1]
    group_start = group_params[2]
    inputs = tokens.astype(jnp.float32)

    weights = jnp.transpose(w_qkv, (1, 0, 2))
    half_size = HD // 2
    frequency = jnp.exp(
        jnp.arange(half_size, dtype=jnp.float32) * (-2.0 * math.log(10000.0) / HD)
    )
    frequency = jnp.tile(frequency, features // half_size).reshape(1, features)
    gain = norm_gain.reshape(1, model_width)
    core = lax.axis_index("core")
    swap_cores = [(0, 1), (1, 0)]
    mate_cache = lax.ppermute(kv_cache, "core", swap_cores)
    meta = jnp.concatenate([group_params, jnp.reshape(core, (1,))]).astype(jnp.int32)
    new_kv = project(meta, tokens, gain, weights, frequency, (1, 2))
    mate_new = lax.ppermute(new_kv, "core", swap_cores)
    joined = relay(meta, kv_cache, new_kv, mate_cache, mate_new, seq_count)
    queries = project(meta, tokens, gain, weights, frequency, (0,))[0]
    joined, attn_kv = lax.optimization_barrier((joined, new_kv))
    received = lax.all_to_all(joined, "seq", 0, 0, tiled=True)
    decode_cache = received.transpose(1, 0, 2, 3).reshape(2, 1, seq_count, 1, BLK, 2 * features)

    attended = attend(meta, queries, kv_cache, attn_kv)
    rows_dev = tok_count // tp_count
    partial = jnp.dot(attended, w_out, preferred_element_type=jnp.float32).astype(jnp.bfloat16)
    x_count = tp_count // 2
    x_rank = lax.axis_index("x")
    by_owner = partial.reshape(x_count, 2, rows_dev, model_width)
    mine = lax.dynamic_index_in_dim(by_owner, core, 1, keepdims=False)
    theirs = lax.dynamic_index_in_dim(by_owner, 1 - core, 1, keepdims=False)
    pair_sum = mine.astype(jnp.float32) + lax.ppermute(theirs, "core", swap_cores).astype(
        jnp.float32
    )
    pair_sent = pair_sum.astype(jnp.bfloat16)
    summed = lax.dynamic_index_in_dim(pair_sum, x_rank, 0, keepdims=False)
    for shift in range(1, x_count):
        target = (x_rank + shift) % x_count
        chunk = lax.dynamic_index_in_dim(pair_sent, target, 0, keepdims=False)
        pairs = [(source, (source + shift) % x_count) for source in range(x_count)]
        summed = summed + lax.ppermute(chunk, "x", pairs).astype(jnp.float32)
    own_rows = lax.dynamic_slice_in_dim(inputs, tp_rank * rows_dev, rows_dev, 0)
    layer_out = (own_rows + summed).astype(jnp.bfloat16)
    return (layer_out, decode_cache)


def solution(mesh):
    seq_count, tp_count = mesh.devices.shape
    split = Mesh(mesh.devices.reshape(seq_count, tp_count // 2, 2), ("seq", "x", "core"))
    tp = ("x", "core")
    placed = (
        P("seq", None),
        P(),
        P(None, None, tp),
        P(tp, None),
        P(None, "seq", None, tp),
        P(),
        P(),
        P(),
    )
    return jax.shard_map(
        local,
        mesh=split,
        in_specs=placed,
        out_specs=(P(("seq",) + tp, None), P(None, "seq", None, None, None, tp)),
        check_vma=False,
    )
```

```python
import functools
import math

import jax
import jax.numpy as jnp
from jax import lax
from jax.experimental import pallas as pl
from jax.experimental.pallas import tpu as pltpu
from jax.sharding import Mesh
from jax.sharding import PartitionSpec as P

HD = 96
BLK = 128
ROWS = 128


def rope_tables(positions, head_size):
    half_size = head_size // 2
    frequency = jnp.exp(
        jnp.arange(half_size, dtype=jnp.float32) * (-2.0 * math.log(10000.0) / head_size)
    )
    angles = positions.astype(jnp.float32)[:, None] * frequency[None, :]
    return (jnp.cos(angles), jnp.sin(angles))


def rope_pair(vectors, cosine_table, sine_table):
    half_size = vectors.shape[-1] // 2
    first_half = vectors[..., :half_size]
    second_half = vectors[..., half_size:]
    cos_wide = cosine_table[:, None, :]
    sin_wide = sine_table[:, None, :]
    return jnp.concatenate(
        [
            first_half * cos_wide - second_half * sin_wide,
            second_half * cos_wide + first_half * sin_wide,
        ],
        axis=-1,
    )


def request_of(index, group_requests, tok_count):
    scaled = index * group_requests
    if tok_count & (tok_count - 1) == 0:
        return lax.shift_right_logical(scaled, tok_count.bit_length() - 1)
    return scaled // tok_count


def head_picker(features, head):
    rows = lax.broadcasted_iota(jnp.int32, (features, HD), 0)
    cols = lax.broadcasted_iota(jnp.int32, (features, HD), 1)
    return (rows == cols + head * HD).astype(jnp.bfloat16)


def attention_kernel(
    meta_ref, q_ref, kc_ref, vc_ref, kn_ref, vn_ref, o_ref, kh_buf, vh_buf, qh_buf, acc_ref
):
    group_len = meta_ref[0]
    group_requests = meta_ref[1]
    head = pl.program_id(0)
    tok_count, features = q_ref.shape
    score_scale = 1.0 / math.sqrt(HD)
    picker = head_picker(features, head)

    def pick(values):
        return jnp.dot(values, picker, preferred_element_type=jnp.float32).astype(jnp.bfloat16)

    kh_buf[...] = pick(kc_ref[0, 0])
    vh_buf[...] = pick(vc_ref[0, 0])
    qh_buf[...] = pick(q_ref[...])
    kn = pick(kn_ref[0])
    vn = pick(vn_ref[0])
    dims = (((1,), (1,)), ((), ()))
    for chunk in range(tok_count // ROWS):
        rows = pl.ds(chunk * ROWS, ROWS)
        q = qh_buf[rows, :]
        s_old = lax.dot_general(q, kh_buf[...], dims, preferred_element_type=jnp.float32)
        s_new = lax.dot_general(q, kn, dims, preferred_element_type=jnp.float32)
        s_old = s_old * score_scale
        s_new = s_new * score_scale
        col = lax.broadcasted_iota(jnp.int32, s_old.shape, 1)
        s_old = jnp.where(col < group_len, s_old, -1e30)
        row = chunk * ROWS + lax.broadcasted_iota(jnp.int32, s_new.shape, 0)
        key = lax.broadcasted_iota(jnp.int32, s_new.shape, 1)
        same = request_of(row, group_requests, tok_count) == request_of(
            key, group_requests, tok_count
        )
        s_new = jnp.where(same & (key <= row), s_new, -1e30)
        peak = jnp.maximum(
            jnp.max(s_old, axis=1, keepdims=True), jnp.max(s_new, axis=1, keepdims=True)
        )
        e_old = jnp.exp(s_old - peak)
        e_new = jnp.exp(s_new - peak)
        total = jnp.sum(e_old, axis=1, keepdims=True) + jnp.sum(e_new, axis=1, keepdims=True)
        p_old = (e_old / total).astype(jnp.bfloat16)
        p_new = (e_new / total).astype(jnp.bfloat16)
        out = jnp.dot(p_old, vh_buf[...], preferred_element_type=jnp.float32) + jnp.dot(
            p_new, vn, preferred_element_type=jnp.float32
        )
        placed = lax.dot_general(
            out.astype(jnp.bfloat16), picker, dims, preferred_element_type=jnp.float32
        )

        @pl.when(head == 0)
        def _():
            acc_ref[rows, :] = placed

        @pl.when(head > 0)
        def _():
            acc_ref[rows, :] = acc_ref[rows, :] + placed

    @pl.when(head == pl.num_programs(0) - 1)
    def _():
        o_ref[...] = acc_ref[...].astype(jnp.bfloat16)


def attend(meta, queries, kv_cache, new_kv):
    tok_count, features = queries.shape
    cache_len = kv_cache.shape[2]
    full_q = pl.BlockSpec((tok_count, features), lambda h, m: (0, 0))
    cache_k = pl.BlockSpec((1, 1, cache_len, features), lambda h, m: (0, 0, 0, 0))
    cache_v = pl.BlockSpec((1, 1, cache_len, features), lambda h, m: (1, 0, 0, 0))
    new_k = pl.BlockSpec((1, tok_count, features), lambda h, m: (0, 0, 0))
    new_v = pl.BlockSpec((1, tok_count, features), lambda h, m: (1, 0, 0))
    return pl.pallas_call(
        attention_kernel,
        out_shape=jax.ShapeDtypeStruct(queries.shape, jnp.bfloat16),
        grid_spec=pltpu.PrefetchScalarGridSpec(
            num_scalar_prefetch=1,
            grid=(features // HD,),
            in_specs=[full_q, cache_k, cache_v, new_k, new_v],
            out_specs=full_q,
            scratch_shapes=[
                pltpu.VMEM((cache_len, HD), jnp.bfloat16),
                pltpu.VMEM((cache_len, HD), jnp.bfloat16),
                pltpu.VMEM((tok_count, HD), jnp.bfloat16),
                pltpu.VMEM((tok_count, features), jnp.float32),
            ],
        ),
    )(meta, queries, kv_cache, kv_cache, new_kv, new_kv)


def relay_kernel(meta_ref, *refs, new_blocks):
    out_ref = refs[-1]
    sources = refs[:-1]
    len_blocks = meta_ref[0] // BLK
    group_start = meta_ref[2]
    core = meta_ref[3]
    per_step = out_ref.shape[0]
    rank_count = 2 * pl.num_programs(0) * per_step
    features = sources[1].shape[2]
    zero = jnp.zeros(sources[1].shape[1:], sources[1].dtype)
    first = core == 0
    for slot in range(per_step):
        own_c, own_n, mate_c, mate_n = sources[4 * slot : 4 * slot + 4]
        dest = pl.program_id(0) * per_step + slot
        block = (2 * dest + core - group_start + rank_count) % rank_count
        old = block < len_blocks
        fresh = (block >= len_blocks) & (block < len_blocks + new_blocks)
        for kv in range(2):
            mine = jnp.where(old, own_c[kv, 0], jnp.where(fresh, own_n[kv], zero))
            mate = jnp.where(old, mate_c[kv, 0], jnp.where(fresh, mate_n[kv], zero))
            out_ref[slot, kv, :, :features] = jnp.where(first, mine, mate)
            out_ref[slot, kv, :, features:] = jnp.where(first, mate, mine)


def relay(meta, kv_cache, new_kv, mate_cache, mate_new, seq_count):
    features = kv_cache.shape[3]
    new_blocks = new_kv.shape[1] // BLK
    rank_count = 2 * seq_count
    per_step = 4 if seq_count % 4 == 0 else 1

    def block_of(d, slot, m):
        return (2 * (d * per_step + slot) + m[3] - m[2] + rank_count) % rank_count

    def cache_spec(slot):
        return pl.BlockSpec(
            (2, 1, BLK, features),
            lambda d, m: (0, 0, jnp.clip(block_of(d, slot, m), 0, m[0] // BLK - 1), 0),
        )

    def new_spec(slot):
        return pl.BlockSpec(
            (2, BLK, features),
            lambda d, m: (
                0,
                jnp.clip(block_of(d, slot, m) - m[0] // BLK, 0, new_blocks - 1),
                0,
            ),
        )

    in_specs = []
    operands = []
    for slot in range(per_step):
        in_specs += [cache_spec(slot), new_spec(slot), cache_spec(slot), new_spec(slot)]
        operands += [kv_cache, new_kv, mate_cache, mate_new]
    return pl.pallas_call(
        functools.partial(relay_kernel, new_blocks=new_blocks),
        out_shape=jax.ShapeDtypeStruct((seq_count, 2, BLK, 2 * features), jnp.bfloat16),
        grid_spec=pltpu.PrefetchScalarGridSpec(
            num_scalar_prefetch=1,
            grid=(seq_count // per_step,),
            in_specs=in_specs,
            out_specs=pl.BlockSpec(
                (per_step, 2, BLK, 2 * features), lambda d, m: (d, 0, 0, 0)
            ),
        ),
    )(meta, *operands)


def regroup_kernel(in_ref, out_ref):
    out_ref[0, 0, :, 0] = in_ref[:, 0]


def regroup(received):
    sources, kinds, rows, width = received.shape
    per_step = 4 if sources % 4 == 0 else 1
    return pl.pallas_call(
        regroup_kernel,
        out_shape=jax.ShapeDtypeStruct((kinds, 1, sources, 1, rows, width), received.dtype),
        grid=(kinds, sources // per_step),
        in_specs=[pl.BlockSpec((per_step, 1, rows, width), lambda k, g: (g, k, 0, 0))],
        out_specs=pl.BlockSpec(
            (1, 1, per_step, 1, rows, width), lambda k, g: (k, 0, g, 0, 0, 0)
        ),
    )(received)


def half_swap(features):
    half = HD // 2
    rows = lax.broadcasted_iota(jnp.int32, (features, features), 0)
    cols = lax.broadcasted_iota(jnp.int32, (features, features), 1)
    first = cols % HD < half
    return jnp.where(
        first & (rows == cols + half),
        -1.0,
        jnp.where(jnp.logical_not(first) & (rows == cols - half), 1.0, 0.0),
    ).astype(jnp.bfloat16)


def projection_kernel(part_ref, meta_ref, x_ref, gain_ref, w_ref, freq_ref, *refs, parts):
    out_refs = refs[:-1]
    normed_ref = refs[-1]
    step = pl.program_id(0)

    @pl.when(step == 0)
    def _():
        inputs = x_ref[...].astype(jnp.float32)
        inverse_rms = lax.rsqrt(jnp.mean(inputs * inputs, axis=-1, keepdims=True) + 1e-05)
        gain = gain_ref[...].astype(jnp.float32)
        normed_ref[...] = (inputs * inverse_rms * gain).astype(jnp.bfloat16)

    weights = w_ref[0]
    plain = jnp.dot(normed_ref[...], weights, preferred_element_type=jnp.float32)

    def rotated():
        rows, features = plain.shape
        half = HD // 2
        group_len = meta_ref[0]
        group_requests = meta_ref[1]
        row = lax.broadcasted_iota(jnp.int32, (rows, 1), 0)
        request = request_of(row, group_requests, rows)
        count = (jnp.zeros((rows, 1), jnp.int32) + group_requests).astype(jnp.float32)
        first = jnp.ceil((request * rows).astype(jnp.float32) / count).astype(jnp.int32)
        positions = (group_len + row - first).astype(jnp.float32)
        angles = positions * freq_ref[...]
        lane = lax.broadcasted_iota(jnp.int32, plain.shape, 1)
        ahead = pltpu.roll(plain, features - half, 1)
        behind = pltpu.roll(plain, half, 1)
        paired = jnp.where(lane % HD < half, -ahead, behind)
        return (plain * jnp.cos(angles) + paired * jnp.sin(angles)).astype(jnp.bfloat16)

    for index, part in enumerate(parts):

        @pl.when(step == index)
        def _():
            value = rotated() if part < 2 else plain.astype(jnp.bfloat16)
            out_refs[0][index] = value


def project(meta, tokens, gain, weights, frequency, parts):
    _, width, features = weights.shape
    rows = tokens.shape[0]
    table = jnp.asarray(parts, jnp.int32)
    out = jax.ShapeDtypeStruct((len(parts), rows, features), jnp.bfloat16)
    return pl.pallas_call(
        functools.partial(projection_kernel, parts=parts),
        out_shape=out,
        grid_spec=pltpu.PrefetchScalarGridSpec(
            num_scalar_prefetch=2,
            grid=(len(parts),),
            in_specs=[
                pl.BlockSpec((rows, width), lambda s, t, m: (0, 0)),
                pl.BlockSpec((1, width), lambda s, t, m: (0, 0)),
                pl.BlockSpec((1, width, features), lambda s, t, m: (t[s], 0, 0)),
                pl.BlockSpec((1, features), lambda s, t, m: (0, 0)),
            ],
            out_specs=pl.BlockSpec((len(parts), rows, features), lambda s, t, m: (0, 0, 0)),
            scratch_shapes=[pltpu.VMEM((rows, width), jnp.bfloat16)],
        ),
    )(table, meta, tokens, gain, weights, frequency)


def local(tokens, norm_gain, w_qkv, w_out, kv_cache, cached_lengths, requests, block_start):
    group_idx = lax.axis_index("seq")
    tp_rank = lax.axis_index(("x", "core"))
    tp_count = lax.axis_size(("x", "core"))
    seq_count = lax.axis_size("seq")
    tok_count, model_width = tokens.shape
    features = w_qkv.shape[2]
    head_count = features // HD
    cache_len = kv_cache.shape[2]
    group_params = lax.dynamic_index_in_dim(
        jnp.stack([cached_lengths, requests, block_start], axis=1), group_idx, keepdims=False
    )
    group_len = group_params[0]
    group_requests = group_params[1]
    group_start = group_params[2]
    inputs = tokens.astype(jnp.float32)

    weights = jnp.transpose(w_qkv, (1, 0, 2))
    half_size = HD // 2
    frequency = jnp.exp(
        jnp.arange(half_size, dtype=jnp.float32) * (-2.0 * math.log(10000.0) / HD)
    )
    frequency = jnp.tile(frequency, features // half_size).reshape(1, features)
    gain = norm_gain.reshape(1, model_width)
    core = lax.axis_index("core")
    swap_cores = [(0, 1), (1, 0)]
    mate_cache = lax.ppermute(kv_cache, "core", swap_cores)
    meta = jnp.concatenate([group_params, jnp.reshape(core, (1,))]).astype(jnp.int32)
    new_kv = project(meta, tokens, gain, weights, frequency, (1, 2))
    mate_new = lax.ppermute(new_kv, "core", swap_cores)
    joined = relay(meta, kv_cache, new_kv, mate_cache, mate_new, seq_count)
    queries = project(meta, tokens, gain, weights, frequency, (0,))[0]
    joined, attn_kv = lax.optimization_barrier((joined, new_kv))
    received = lax.all_to_all(joined, "seq", 0, 0, tiled=True)
    decode_cache = regroup(received)

    attended = attend(meta, queries, kv_cache, attn_kv)
    rows_dev = tok_count // tp_count
    partial = jnp.dot(attended, w_out, preferred_element_type=jnp.float32).astype(jnp.bfloat16)
    x_count = tp_count // 2
    x_rank = lax.axis_index("x")
    by_owner = partial.reshape(x_count, 2, rows_dev, model_width)
    mine = lax.dynamic_index_in_dim(by_owner, core, 1, keepdims=False)
    theirs = lax.dynamic_index_in_dim(by_owner, 1 - core, 1, keepdims=False)
    pair_sum = mine.astype(jnp.float32) + lax.ppermute(theirs, "core", swap_cores).astype(
        jnp.float32
    )
    pair_sent = pair_sum.astype(jnp.bfloat16)
    summed = lax.dynamic_index_in_dim(pair_sum, x_rank, 0, keepdims=False)
    for shift in range(1, x_count):
        target = (x_rank + shift) % x_count
        chunk = lax.dynamic_index_in_dim(pair_sent, target, 0, keepdims=False)
        pairs = [(source, (source + shift) % x_count) for source in range(x_count)]
        summed = summed + lax.ppermute(chunk, "x", pairs).astype(jnp.float32)
    own_rows = lax.dynamic_slice_in_dim(inputs, tp_rank * rows_dev, rows_dev, 0)
    layer_out = (own_rows + summed).astype(jnp.bfloat16)
    return (layer_out, decode_cache)


def solution(mesh):
    seq_count, tp_count = mesh.devices.shape
    split = Mesh(mesh.devices.reshape(seq_count, tp_count // 2, 2), ("seq", "x", "core"))
    tp = ("x", "core")
    placed = (
        P("seq", None),
        P(),
        P(None, None, tp),
        P(tp, None),
        P(None, "seq", None, tp),
        P(),
        P(),
        P(),
    )
    return jax.shard_map(
        local,
        mesh=split,
        in_specs=placed,
        out_specs=(P(("seq",) + tp, None), P(None, "seq", None, None, None, tp)),
        check_vma=False,
    )
```

```python
import functools
import math

import jax
import jax.numpy as jnp
from jax import lax
from jax.experimental import pallas as pl
from jax.experimental.pallas import tpu as pltpu
from jax.sharding import Mesh
from jax.sharding import PartitionSpec as P

HD = 96
BLK = 128
ROWS = 128


def rope_tables(positions, head_size):
    half_size = head_size // 2
    frequency = jnp.exp(
        jnp.arange(half_size, dtype=jnp.float32) * (-2.0 * math.log(10000.0) / head_size)
    )
    angles = positions.astype(jnp.float32)[:, None] * frequency[None, :]
    return (jnp.cos(angles), jnp.sin(angles))


def rope_pair(vectors, cosine_table, sine_table):
    half_size = vectors.shape[-1] // 2
    first_half = vectors[..., :half_size]
    second_half = vectors[..., half_size:]
    cos_wide = cosine_table[:, None, :]
    sin_wide = sine_table[:, None, :]
    return jnp.concatenate(
        [
            first_half * cos_wide - second_half * sin_wide,
            second_half * cos_wide + first_half * sin_wide,
        ],
        axis=-1,
    )


def request_of(index, group_requests, tok_count):
    scaled = index * group_requests
    if tok_count & (tok_count - 1) == 0:
        return lax.shift_right_logical(scaled, tok_count.bit_length() - 1)
    return scaled // tok_count


def head_picker(features, head):
    rows = lax.broadcasted_iota(jnp.int32, (features, HD), 0)
    cols = lax.broadcasted_iota(jnp.int32, (features, HD), 1)
    return (rows == cols + head * HD).astype(jnp.bfloat16)


def attention_kernel(
    meta_ref, q_ref, kc_ref, vc_ref, kn_ref, vn_ref, o_ref, kh_buf, vh_buf, qh_buf, acc_ref
):
    group_len = meta_ref[0]
    group_requests = meta_ref[1]
    head = pl.program_id(0)
    tok_count, features = q_ref.shape
    score_scale = 1.0 / math.sqrt(HD)
    picker = head_picker(features, head)

    def pick(values):
        return jnp.dot(values, picker, preferred_element_type=jnp.float32).astype(jnp.bfloat16)

    kh_buf[...] = pick(kc_ref[0, 0])
    vh_buf[...] = pick(vc_ref[0, 0])
    qh_buf[...] = pick(q_ref[...])
    kn = pick(kn_ref[0])
    vn = pick(vn_ref[0])
    dims = (((1,), (1,)), ((), ()))
    for chunk in range(tok_count // ROWS):
        rows = pl.ds(chunk * ROWS, ROWS)
        q = qh_buf[rows, :]
        s_old = lax.dot_general(q, kh_buf[...], dims, preferred_element_type=jnp.float32)
        s_new = lax.dot_general(q, kn, dims, preferred_element_type=jnp.float32)
        s_old = s_old * score_scale
        s_new = s_new * score_scale
        col = lax.broadcasted_iota(jnp.int32, s_old.shape, 1)
        s_old = jnp.where(col < group_len, s_old, -1e30)
        row = chunk * ROWS + lax.broadcasted_iota(jnp.int32, s_new.shape, 0)
        key = lax.broadcasted_iota(jnp.int32, s_new.shape, 1)
        same = request_of(row, group_requests, tok_count) == request_of(
            key, group_requests, tok_count
        )
        s_new = jnp.where(same & (key <= row), s_new, -1e30)
        peak = jnp.maximum(
            jnp.max(s_old, axis=1, keepdims=True), jnp.max(s_new, axis=1, keepdims=True)
        )
        e_old = jnp.exp(s_old - peak)
        e_new = jnp.exp(s_new - peak)
        total = jnp.sum(e_old, axis=1, keepdims=True) + jnp.sum(e_new, axis=1, keepdims=True)
        p_old = (e_old / total).astype(jnp.bfloat16)
        p_new = (e_new / total).astype(jnp.bfloat16)
        out = jnp.dot(p_old, vh_buf[...], preferred_element_type=jnp.float32) + jnp.dot(
            p_new, vn, preferred_element_type=jnp.float32
        )
        placed = lax.dot_general(
            out.astype(jnp.bfloat16), picker, dims, preferred_element_type=jnp.float32
        )

        @pl.when(head == 0)
        def _():
            acc_ref[rows, :] = placed

        @pl.when(head > 0)
        def _():
            acc_ref[rows, :] = acc_ref[rows, :] + placed

    @pl.when(head == pl.num_programs(0) - 1)
    def _():
        o_ref[...] = acc_ref[...].astype(jnp.bfloat16)


def attend(meta, queries, kv_cache, new_kv):
    tok_count, features = queries.shape
    cache_len = kv_cache.shape[2]
    full_q = pl.BlockSpec((tok_count, features), lambda h, m: (0, 0))
    cache_k = pl.BlockSpec((1, 1, cache_len, features), lambda h, m: (0, 0, 0, 0))
    cache_v = pl.BlockSpec((1, 1, cache_len, features), lambda h, m: (1, 0, 0, 0))
    new_k = pl.BlockSpec((1, tok_count, features), lambda h, m: (0, 0, 0))
    new_v = pl.BlockSpec((1, tok_count, features), lambda h, m: (1, 0, 0))
    return pl.pallas_call(
        attention_kernel,
        out_shape=jax.ShapeDtypeStruct(queries.shape, jnp.bfloat16),
        grid_spec=pltpu.PrefetchScalarGridSpec(
            num_scalar_prefetch=1,
            grid=(features // HD,),
            in_specs=[full_q, cache_k, cache_v, new_k, new_v],
            out_specs=full_q,
            scratch_shapes=[
                pltpu.VMEM((cache_len, HD), jnp.bfloat16),
                pltpu.VMEM((cache_len, HD), jnp.bfloat16),
                pltpu.VMEM((tok_count, HD), jnp.bfloat16),
                pltpu.VMEM((tok_count, features), jnp.float32),
            ],
        ),
    )(meta, queries, kv_cache, kv_cache, new_kv, new_kv)


def relay_kernel(meta_ref, *refs, new_blocks):
    out_ref = refs[-1]
    sources = refs[:-1]
    len_blocks = meta_ref[0] // BLK
    group_start = meta_ref[2]
    core = meta_ref[3]
    per_step = out_ref.shape[0]
    rank_count = 2 * pl.num_programs(0) * per_step
    features = sources[1].shape[2]
    zero = jnp.zeros(sources[1].shape[1:], sources[1].dtype)
    first = core == 0
    for slot in range(per_step):
        own_c, own_n, mate_c, mate_n = sources[4 * slot : 4 * slot + 4]
        dest = pl.program_id(0) * per_step + slot
        block = (2 * dest + core - group_start + rank_count) % rank_count
        old = block < len_blocks
        fresh = (block >= len_blocks) & (block < len_blocks + new_blocks)
        for kv in range(2):
            mine = jnp.where(old, own_c[kv, 0], jnp.where(fresh, own_n[kv], zero))
            mate = jnp.where(old, mate_c[kv, 0], jnp.where(fresh, mate_n[kv], zero))
            out_ref[slot, kv, :, :features] = jnp.where(first, mine, mate)
            out_ref[slot, kv, :, features:] = jnp.where(first, mate, mine)


def relay(meta, kv_cache, new_kv, mate_cache, mate_new, seq_count):
    features = kv_cache.shape[3]
    new_blocks = new_kv.shape[1] // BLK
    rank_count = 2 * seq_count
    per_step = 4 if seq_count % 4 == 0 else 1

    def block_of(d, slot, m):
        return (2 * (d * per_step + slot) + m[3] - m[2] + rank_count) % rank_count

    def cache_spec(slot):
        return pl.BlockSpec(
            (2, 1, BLK, features),
            lambda d, m: (0, 0, jnp.clip(block_of(d, slot, m), 0, m[0] // BLK - 1), 0),
        )

    def new_spec(slot):
        return pl.BlockSpec(
            (2, BLK, features),
            lambda d, m: (
                0,
                jnp.clip(block_of(d, slot, m) - m[0] // BLK, 0, new_blocks - 1),
                0,
            ),
        )

    in_specs = []
    operands = []
    for slot in range(per_step):
        in_specs += [cache_spec(slot), new_spec(slot), cache_spec(slot), new_spec(slot)]
        operands += [kv_cache, new_kv, mate_cache, mate_new]
    return pl.pallas_call(
        functools.partial(relay_kernel, new_blocks=new_blocks),
        out_shape=jax.ShapeDtypeStruct((seq_count, 2, BLK, 2 * features), jnp.bfloat16),
        grid_spec=pltpu.PrefetchScalarGridSpec(
            num_scalar_prefetch=1,
            grid=(seq_count // per_step,),
            in_specs=in_specs,
            out_specs=pl.BlockSpec(
                (per_step, 2, BLK, 2 * features), lambda d, m: (d, 0, 0, 0)
            ),
        ),
    )(meta, *operands)


def half_swap(features):
    half = HD // 2
    rows = lax.broadcasted_iota(jnp.int32, (features, features), 0)
    cols = lax.broadcasted_iota(jnp.int32, (features, features), 1)
    first = cols % HD < half
    return jnp.where(
        first & (rows == cols + half),
        -1.0,
        jnp.where(jnp.logical_not(first) & (rows == cols - half), 1.0, 0.0),
    ).astype(jnp.bfloat16)


def projection_kernel(meta_ref, x_ref, gain_ref, freq_ref, *refs, parts):
    w_refs = refs[: len(parts)]
    out_ref = refs[len(parts)]
    rows = x_ref.shape[0]
    tok_count = rows * pl.num_programs(0)
    inputs = x_ref[...].astype(jnp.float32)
    inverse_rms = lax.rsqrt(jnp.mean(inputs * inputs, axis=-1, keepdims=True) + 1e-05)
    gain = gain_ref[...].astype(jnp.float32)
    normed = (inputs * inverse_rms * gain).astype(jnp.bfloat16)
    for index, part in enumerate(parts):
        plain = jnp.dot(normed, w_refs[index][0], preferred_element_type=jnp.float32)
        if part == 2:
            out_ref[index] = plain.astype(out_ref.dtype)
            continue
        features = plain.shape[1]
        half = HD // 2
        group_len = meta_ref[0]
        group_requests = meta_ref[1]
        row = pl.program_id(0) * rows + lax.broadcasted_iota(jnp.int32, (rows, 1), 0)
        request = request_of(row, group_requests, tok_count)
        count = (jnp.zeros((rows, 1), jnp.int32) + group_requests).astype(jnp.float32)
        first = jnp.ceil((request * tok_count).astype(jnp.float32) / count).astype(jnp.int32)
        positions = (group_len + row - first).astype(jnp.float32)
        angles = positions * freq_ref[...]
        lane = lax.broadcasted_iota(jnp.int32, plain.shape, 1)
        ahead = pltpu.roll(plain, features - half, 1)
        behind = pltpu.roll(plain, half, 1)
        paired = jnp.where(lane % HD < half, -ahead, behind)
        rotated = plain * jnp.cos(angles) + paired * jnp.sin(angles)
        out_ref[index] = rotated.astype(out_ref.dtype)


def project(meta, tokens, gain, weights, frequency, parts):
    _, width, features = weights.shape
    tok_count = tokens.shape[0]
    rows = 128 if tok_count % 128 == 0 else tok_count

    def weight_spec(part):
        return pl.BlockSpec((1, width, features), lambda r, m: (part, 0, 0))

    return pl.pallas_call(
        functools.partial(projection_kernel, parts=parts),
        out_shape=jax.ShapeDtypeStruct((len(parts), tok_count, features), jnp.bfloat16),
        grid_spec=pltpu.PrefetchScalarGridSpec(
            num_scalar_prefetch=1,
            grid=(tok_count // rows,),
            in_specs=[
                pl.BlockSpec((rows, width), lambda r, m: (r, 0)),
                pl.BlockSpec((1, width), lambda r, m: (0, 0)),
                pl.BlockSpec((1, features), lambda r, m: (0, 0)),
            ]
            + [weight_spec(part) for part in parts],
            out_specs=pl.BlockSpec((len(parts), rows, features), lambda r, m: (0, r, 0)),
        ),
    )(meta, tokens, gain, frequency, *(weights for _ in parts))


def local(tokens, norm_gain, w_qkv, w_out, kv_cache, cached_lengths, requests, block_start):
    group_idx = lax.axis_index("seq")
    tp_rank = lax.axis_index(("x", "core"))
    tp_count = lax.axis_size(("x", "core"))
    seq_count = lax.axis_size("seq")
    tok_count, model_width = tokens.shape
    features = w_qkv.shape[2]
    head_count = features // HD
    cache_len = kv_cache.shape[2]
    group_params = lax.dynamic_index_in_dim(
        jnp.stack([cached_lengths, requests, block_start], axis=1), group_idx, keepdims=False
    )
    group_len = group_params[0]
    group_requests = group_params[1]
    group_start = group_params[2]
    inputs = tokens.astype(jnp.float32)

    weights = jnp.transpose(w_qkv, (1, 0, 2))
    half_size = HD // 2
    frequency = jnp.exp(
        jnp.arange(half_size, dtype=jnp.float32) * (-2.0 * math.log(10000.0) / HD)
    )
    frequency = jnp.tile(frequency, features // half_size).reshape(1, features)
    gain = norm_gain.reshape(1, model_width)
    core = lax.axis_index("core")
    swap_cores = [(0, 1), (1, 0)]
    mate_cache = lax.ppermute(kv_cache, "core", swap_cores)
    meta = jnp.concatenate([group_params, jnp.reshape(core, (1,))]).astype(jnp.int32)
    new_kv = project(meta, tokens, gain, weights, frequency, (1, 2))
    mate_new = lax.ppermute(new_kv, "core", swap_cores)
    joined = relay(meta, kv_cache, new_kv, mate_cache, mate_new, seq_count)
    queries = project(meta, tokens, gain, weights, frequency, (0,))[0]
    joined, attn_kv = lax.optimization_barrier((joined, new_kv))
    received = lax.all_to_all(joined, "seq", 0, 0, tiled=True)
    decode_cache = received.transpose(1, 0, 2, 3).reshape(2, 1, seq_count, 1, BLK, 2 * features)

    attended = attend(meta, queries, kv_cache, attn_kv)
    rows_dev = tok_count // tp_count
    partial = jnp.dot(attended, w_out, preferred_element_type=jnp.float32).astype(jnp.bfloat16)
    x_count = tp_count // 2
    x_rank = lax.axis_index("x")
    by_owner = partial.reshape(x_count, 2, rows_dev, model_width)
    mine = lax.dynamic_index_in_dim(by_owner, core, 1, keepdims=False)
    theirs = lax.dynamic_index_in_dim(by_owner, 1 - core, 1, keepdims=False)
    pair_sum = mine.astype(jnp.float32) + lax.ppermute(theirs, "core", swap_cores).astype(
        jnp.float32
    )
    pair_sent = pair_sum.astype(jnp.bfloat16)
    summed = lax.dynamic_index_in_dim(pair_sum, x_rank, 0, keepdims=False)
    for shift in range(1, x_count):
        target = (x_rank + shift) % x_count
        chunk = lax.dynamic_index_in_dim(pair_sent, target, 0, keepdims=False)
        pairs = [(source, (source + shift) % x_count) for source in range(x_count)]
        summed = summed + lax.ppermute(chunk, "x", pairs).astype(jnp.float32)
    own_rows = lax.dynamic_slice_in_dim(inputs, tp_rank * rows_dev, rows_dev, 0)
    layer_out = (own_rows + summed).astype(jnp.bfloat16)
    return (layer_out, decode_cache)


def solution(mesh):
    seq_count, tp_count = mesh.devices.shape
    split = Mesh(mesh.devices.reshape(seq_count, tp_count // 2, 2), ("seq", "x", "core"))
    tp = ("x", "core")
    placed = (
        P("seq", None),
        P(),
        P(None, None, tp),
        P(tp, None),
        P(None, "seq", None, tp),
        P(),
        P(),
        P(),
    )
    return jax.shard_map(
        local,
        mesh=split,
        in_specs=placed,
        out_specs=(P(("seq",) + tp, None), P(None, "seq", None, None, None, tp)),
        check_vma=False,
    )
```

```python
import functools
import math

import jax
import jax.numpy as jnp
from jax import lax
from jax.experimental import pallas as pl
from jax.experimental.pallas import tpu as pltpu
from jax.sharding import Mesh
from jax.sharding import PartitionSpec as P

HD = 96
BLK = 128
ROWS = 128


def rope_tables(positions, head_size):
    half_size = head_size // 2
    frequency = jnp.exp(
        jnp.arange(half_size, dtype=jnp.float32) * (-2.0 * math.log(10000.0) / head_size)
    )
    angles = positions.astype(jnp.float32)[:, None] * frequency[None, :]
    return (jnp.cos(angles), jnp.sin(angles))


def rope_pair(vectors, cosine_table, sine_table):
    half_size = vectors.shape[-1] // 2
    first_half = vectors[..., :half_size]
    second_half = vectors[..., half_size:]
    cos_wide = cosine_table[:, None, :]
    sin_wide = sine_table[:, None, :]
    return jnp.concatenate(
        [
            first_half * cos_wide - second_half * sin_wide,
            second_half * cos_wide + first_half * sin_wide,
        ],
        axis=-1,
    )


def request_of(index, group_requests, tok_count):
    scaled = index * group_requests
    if tok_count & (tok_count - 1) == 0:
        return lax.shift_right_logical(scaled, tok_count.bit_length() - 1)
    return scaled // tok_count


def head_picker(features, head):
    rows = lax.broadcasted_iota(jnp.int32, (features, HD), 0)
    cols = lax.broadcasted_iota(jnp.int32, (features, HD), 1)
    return (rows == cols + head * HD).astype(jnp.bfloat16)


def attention_kernel(
    meta_ref, q_ref, kc_ref, vc_ref, kn_ref, vn_ref, o_ref, kh_buf, vh_buf, qh_buf, acc_ref
):
    group_len = meta_ref[0]
    group_requests = meta_ref[1]
    head = pl.program_id(0)
    tok_count, features = q_ref.shape
    score_scale = 1.0 / math.sqrt(HD)
    picker = head_picker(features, head)

    def pick(values):
        return jnp.dot(values, picker, preferred_element_type=jnp.float32).astype(jnp.bfloat16)

    kh_buf[...] = pick(kc_ref[0, 0])
    vh_buf[...] = pick(vc_ref[0, 0])
    qh_buf[...] = pick(q_ref[...])
    kn = pick(kn_ref[0])
    vn = pick(vn_ref[0])
    dims = (((1,), (1,)), ((), ()))
    for chunk in range(tok_count // ROWS):
        rows = pl.ds(chunk * ROWS, ROWS)
        q = qh_buf[rows, :]
        s_old = lax.dot_general(q, kh_buf[...], dims, preferred_element_type=jnp.float32)
        s_new = lax.dot_general(q, kn, dims, preferred_element_type=jnp.float32)
        s_old = s_old * score_scale
        s_new = s_new * score_scale
        col = lax.broadcasted_iota(jnp.int32, s_old.shape, 1)
        s_old = jnp.where(col < group_len, s_old, -1e30)
        row = chunk * ROWS + lax.broadcasted_iota(jnp.int32, s_new.shape, 0)
        key = lax.broadcasted_iota(jnp.int32, s_new.shape, 1)
        same = request_of(row, group_requests, tok_count) == request_of(
            key, group_requests, tok_count
        )
        s_new = jnp.where(same & (key <= row), s_new, -1e30)
        peak = jnp.maximum(
            jnp.max(s_old, axis=1, keepdims=True), jnp.max(s_new, axis=1, keepdims=True)
        )
        e_old = jnp.exp(s_old - peak)
        e_new = jnp.exp(s_new - peak)
        total = jnp.sum(e_old, axis=1, keepdims=True) + jnp.sum(e_new, axis=1, keepdims=True)
        p_old = (e_old / total).astype(jnp.bfloat16)
        p_new = (e_new / total).astype(jnp.bfloat16)
        out = jnp.dot(p_old, vh_buf[...], preferred_element_type=jnp.float32) + jnp.dot(
            p_new, vn, preferred_element_type=jnp.float32
        )
        placed = lax.dot_general(
            out.astype(jnp.bfloat16), picker, dims, preferred_element_type=jnp.float32
        )

        @pl.when(head == 0)
        def _():
            acc_ref[rows, :] = placed

        @pl.when(head > 0)
        def _():
            acc_ref[rows, :] = acc_ref[rows, :] + placed

    @pl.when(head == pl.num_programs(0) - 1)
    def _():
        o_ref[...] = acc_ref[...].astype(jnp.bfloat16)


def attend(meta, queries, kv_cache, new_kv):
    tok_count, features = queries.shape
    cache_len = kv_cache.shape[2]
    full_q = pl.BlockSpec((tok_count, features), lambda h, m: (0, 0))
    cache_k = pl.BlockSpec((1, 1, cache_len, features), lambda h, m: (0, 0, 0, 0))
    cache_v = pl.BlockSpec((1, 1, cache_len, features), lambda h, m: (1, 0, 0, 0))
    new_k = pl.BlockSpec((1, tok_count, features), lambda h, m: (0, 0, 0))
    new_v = pl.BlockSpec((1, tok_count, features), lambda h, m: (1, 0, 0))
    return pl.pallas_call(
        attention_kernel,
        out_shape=jax.ShapeDtypeStruct(queries.shape, jnp.bfloat16),
        grid_spec=pltpu.PrefetchScalarGridSpec(
            num_scalar_prefetch=1,
            grid=(features // HD,),
            in_specs=[full_q, cache_k, cache_v, new_k, new_v],
            out_specs=full_q,
            scratch_shapes=[
                pltpu.VMEM((cache_len, HD), jnp.bfloat16),
                pltpu.VMEM((cache_len, HD), jnp.bfloat16),
                pltpu.VMEM((tok_count, HD), jnp.bfloat16),
                pltpu.VMEM((tok_count, features), jnp.float32),
            ],
        ),
    )(meta, queries, kv_cache, kv_cache, new_kv, new_kv)


def relay_kernel(meta_ref, *refs, new_blocks):
    out_ref = refs[-1]
    sources = refs[:-1]
    len_blocks = meta_ref[0] // BLK
    group_start = meta_ref[2]
    core = meta_ref[3]
    per_step = out_ref.shape[0]
    rank_count = 2 * pl.num_programs(0) * per_step
    features = sources[1].shape[2]
    zero = jnp.zeros(sources[1].shape[1:], sources[1].dtype)
    first = core == 0
    for slot in range(per_step):
        own_c, own_n, mate_c, mate_n = sources[4 * slot : 4 * slot + 4]
        dest = pl.program_id(0) * per_step + slot
        block = (2 * dest + core - group_start + rank_count) % rank_count
        old = block < len_blocks
        fresh = (block >= len_blocks) & (block < len_blocks + new_blocks)
        for kv in range(2):
            mine = jnp.where(old, own_c[kv, 0], jnp.where(fresh, own_n[kv], zero))
            mate = jnp.where(old, mate_c[kv, 0], jnp.where(fresh, mate_n[kv], zero))
            out_ref[slot, kv, :, :features] = jnp.where(first, mine, mate)
            out_ref[slot, kv, :, features:] = jnp.where(first, mate, mine)


def relay(meta, kv_cache, new_kv, mate_cache, mate_new, seq_count):
    features = kv_cache.shape[3]
    new_blocks = new_kv.shape[1] // BLK
    rank_count = 2 * seq_count
    per_step = 4 if seq_count % 4 == 0 else 1

    def block_of(d, slot, m):
        return (2 * (d * per_step + slot) + m[3] - m[2] + rank_count) % rank_count

    def cache_spec(slot):
        return pl.BlockSpec(
            (2, 1, BLK, features),
            lambda d, m: (0, 0, jnp.clip(block_of(d, slot, m), 0, m[0] // BLK - 1), 0),
        )

    def new_spec(slot):
        return pl.BlockSpec(
            (2, BLK, features),
            lambda d, m: (
                0,
                jnp.clip(block_of(d, slot, m) - m[0] // BLK, 0, new_blocks - 1),
                0,
            ),
        )

    in_specs = []
    operands = []
    for slot in range(per_step):
        in_specs += [cache_spec(slot), new_spec(slot), cache_spec(slot), new_spec(slot)]
        operands += [kv_cache, new_kv, mate_cache, mate_new]
    return pl.pallas_call(
        functools.partial(relay_kernel, new_blocks=new_blocks),
        out_shape=jax.ShapeDtypeStruct((seq_count, 2, BLK, 2 * features), jnp.bfloat16),
        grid_spec=pltpu.PrefetchScalarGridSpec(
            num_scalar_prefetch=1,
            grid=(seq_count // per_step,),
            in_specs=in_specs,
            out_specs=pl.BlockSpec(
                (per_step, 2, BLK, 2 * features), lambda d, m: (d, 0, 0, 0)
            ),
        ),
    )(meta, *operands)


def half_swap(features):
    half = HD // 2
    rows = lax.broadcasted_iota(jnp.int32, (features, features), 0)
    cols = lax.broadcasted_iota(jnp.int32, (features, features), 1)
    first = cols % HD < half
    return jnp.where(
        first & (rows == cols + half),
        -1.0,
        jnp.where(jnp.logical_not(first) & (rows == cols - half), 1.0, 0.0),
    ).astype(jnp.bfloat16)


def projection_kernel(meta_ref, x_ref, gain_ref, freq_ref, *refs, parts):
    w_refs = refs[: len(parts)]
    out_ref = refs[len(parts)]
    rows = x_ref.shape[0]
    tok_count = rows * pl.num_programs(0)
    inputs = x_ref[...].astype(jnp.float32)
    inverse_rms = lax.rsqrt(jnp.mean(inputs * inputs, axis=-1, keepdims=True) + 1e-05)
    gain = gain_ref[...].astype(jnp.float32).reshape(1, inputs.shape[1])
    normed = (inputs * inverse_rms * gain).astype(jnp.bfloat16)
    for index, part in enumerate(parts):
        plain = jnp.dot(normed, w_refs[index][0], preferred_element_type=jnp.float32)
        if part == 2:
            out_ref[index] = plain.astype(out_ref.dtype)
            continue
        features = plain.shape[1]
        half = HD // 2
        group_len = meta_ref[0]
        group_requests = meta_ref[1]
        row = pl.program_id(0) * rows + lax.broadcasted_iota(jnp.int32, (rows, 1), 0)
        request = request_of(row, group_requests, tok_count)
        count = (jnp.zeros((rows, 1), jnp.int32) + group_requests).astype(jnp.float32)
        first = jnp.ceil((request * tok_count).astype(jnp.float32) / count).astype(jnp.int32)
        positions = (group_len + row - first).astype(jnp.float32)
        angles = positions * freq_ref[...]
        lane = lax.broadcasted_iota(jnp.int32, plain.shape, 1)
        ahead = pltpu.roll(plain, features - half, 1)
        behind = pltpu.roll(plain, half, 1)
        paired = jnp.where(lane % HD < half, -ahead, behind)
        rotated = plain * jnp.cos(angles) + paired * jnp.sin(angles)
        out_ref[index] = rotated.astype(out_ref.dtype)


def project(meta, tokens, gain, weights, frequency, parts):
    _, width, features = weights.shape
    tok_count = tokens.shape[0]
    rows = 128 if tok_count % 128 == 0 else tok_count

    def weight_spec(part):
        return pl.BlockSpec((1, width, features), lambda r, m: (part, 0, 0))

    return pl.pallas_call(
        functools.partial(projection_kernel, parts=parts),
        out_shape=jax.ShapeDtypeStruct((len(parts), tok_count, features), jnp.bfloat16),
        grid_spec=pltpu.PrefetchScalarGridSpec(
            num_scalar_prefetch=1,
            grid=(tok_count // rows,),
            in_specs=[
                pl.BlockSpec((rows, width), lambda r, m: (r, 0)),
                pl.BlockSpec((width,), lambda r, m: (0,)),
                pl.BlockSpec((1, features), lambda r, m: (0, 0)),
            ]
            + [weight_spec(part) for part in parts],
            out_specs=pl.BlockSpec((len(parts), rows, features), lambda r, m: (0, r, 0)),
        ),
    )(meta, tokens, gain, frequency, *(weights for _ in parts))


def local(tokens, norm_gain, w_qkv, w_out, kv_cache, cached_lengths, requests, block_start):
    group_idx = lax.axis_index("seq")
    tp_rank = lax.axis_index(("x", "core"))
    tp_count = lax.axis_size(("x", "core"))
    seq_count = lax.axis_size("seq")
    tok_count, model_width = tokens.shape
    features = w_qkv.shape[2]
    head_count = features // HD
    cache_len = kv_cache.shape[2]
    group_params = lax.dynamic_index_in_dim(
        jnp.stack([cached_lengths, requests, block_start], axis=1), group_idx, keepdims=False
    )
    group_len = group_params[0]
    group_requests = group_params[1]
    group_start = group_params[2]
    inputs = tokens.astype(jnp.float32)

    weights = jnp.transpose(w_qkv, (1, 0, 2))
    half_size = HD // 2
    frequency = jnp.exp(
        jnp.arange(half_size, dtype=jnp.float32) * (-2.0 * math.log(10000.0) / HD)
    )
    frequency = jnp.tile(frequency, features // half_size).reshape(1, features)
    gain = norm_gain
    core = lax.axis_index("core")
    swap_cores = [(0, 1), (1, 0)]
    mate_cache = lax.ppermute(kv_cache, "core", swap_cores)
    meta = jnp.concatenate([group_params, jnp.reshape(core, (1,))]).astype(jnp.int32)
    new_kv = project(meta, tokens, gain, weights, frequency, (1, 2))
    mate_new = lax.ppermute(new_kv, "core", swap_cores)
    joined = relay(meta, kv_cache, new_kv, mate_cache, mate_new, seq_count)
    queries = project(meta, tokens, gain, weights, frequency, (0,))[0]
    joined, attn_kv = lax.optimization_barrier((joined, new_kv))
    received = lax.all_to_all(joined, "seq", 0, 0, tiled=True)
    decode_cache = received.transpose(1, 0, 2, 3).reshape(2, 1, seq_count, 1, BLK, 2 * features)

    attended = attend(meta, queries, kv_cache, attn_kv)
    rows_dev = tok_count // tp_count
    partial = jnp.dot(attended, w_out, preferred_element_type=jnp.float32).astype(jnp.bfloat16)
    x_count = tp_count // 2
    x_rank = lax.axis_index("x")
    by_owner = partial.reshape(x_count, 2, rows_dev, model_width)
    mine = lax.dynamic_index_in_dim(by_owner, core, 1, keepdims=False)
    theirs = lax.dynamic_index_in_dim(by_owner, 1 - core, 1, keepdims=False)
    pair_sum = mine.astype(jnp.float32) + lax.ppermute(theirs, "core", swap_cores).astype(
        jnp.float32
    )
    pair_sent = pair_sum.astype(jnp.bfloat16)
    summed = lax.dynamic_index_in_dim(pair_sum, x_rank, 0, keepdims=False)
    for shift in range(1, x_count):
        target = (x_rank + shift) % x_count
        chunk = lax.dynamic_index_in_dim(pair_sent, target, 0, keepdims=False)
        pairs = [(source, (source + shift) % x_count) for source in range(x_count)]
        summed = summed + lax.ppermute(chunk, "x", pairs).astype(jnp.float32)
    own_rows = lax.dynamic_slice_in_dim(inputs, tp_rank * rows_dev, rows_dev, 0)
    layer_out = (own_rows + summed).astype(jnp.bfloat16)
    return (layer_out, decode_cache)


def solution(mesh):
    seq_count, tp_count = mesh.devices.shape
    split = Mesh(mesh.devices.reshape(seq_count, tp_count // 2, 2), ("seq", "x", "core"))
    tp = ("x", "core")
    placed = (
        P("seq", None),
        P(),
        P(None, None, tp),
        P(tp, None),
        P(None, "seq", None, tp),
        P(),
        P(),
        P(),
    )
    return jax.shard_map(
        local,
        mesh=split,
        in_specs=placed,
        out_specs=(P(("seq",) + tp, None), P(None, "seq", None, None, None, tp)),
        check_vma=False,
    )
```

```python
import functools
import math

import jax
import jax.numpy as jnp
from jax import lax
from jax.experimental import pallas as pl
from jax.experimental.pallas import tpu as pltpu
from jax.sharding import Mesh
from jax.sharding import PartitionSpec as P

HD = 96
BLK = 128
ROWS = 128


def rope_tables(positions, head_size):
    half_size = head_size // 2
    frequency = jnp.exp(
        jnp.arange(half_size, dtype=jnp.float32) * (-2.0 * math.log(10000.0) / head_size)
    )
    angles = positions.astype(jnp.float32)[:, None] * frequency[None, :]
    return (jnp.cos(angles), jnp.sin(angles))


def rope_pair(vectors, cosine_table, sine_table):
    half_size = vectors.shape[-1] // 2
    first_half = vectors[..., :half_size]
    second_half = vectors[..., half_size:]
    cos_wide = cosine_table[:, None, :]
    sin_wide = sine_table[:, None, :]
    return jnp.concatenate(
        [
            first_half * cos_wide - second_half * sin_wide,
            second_half * cos_wide + first_half * sin_wide,
        ],
        axis=-1,
    )


def request_of(index, group_requests, tok_count):
    scaled = index * group_requests
    if tok_count & (tok_count - 1) == 0:
        return lax.shift_right_logical(scaled, tok_count.bit_length() - 1)
    return scaled // tok_count


def head_picker(features, head):
    rows = lax.broadcasted_iota(jnp.int32, (features, HD), 0)
    cols = lax.broadcasted_iota(jnp.int32, (features, HD), 1)
    return (rows == cols + head * HD).astype(jnp.bfloat16)


def attention_kernel(
    meta_ref, q_ref, kc_ref, vc_ref, kn_ref, vn_ref, o_ref, kh_buf, vh_buf, qh_buf, acc_ref
):
    group_len = meta_ref[0]
    group_requests = meta_ref[1]
    head = pl.program_id(0)
    tok_count, features = q_ref.shape
    score_scale = 1.0 / math.sqrt(HD)
    picker = head_picker(features, head)

    def pick(values):
        return jnp.dot(values, picker, preferred_element_type=jnp.float32).astype(jnp.bfloat16)

    kh_buf[...] = pick(kc_ref[0, 0])
    vh_buf[...] = pick(vc_ref[0, 0])
    qh_buf[...] = pick(q_ref[...])
    kn = pick(kn_ref[0])
    vn = pick(vn_ref[0])
    dims = (((1,), (1,)), ((), ()))
    for chunk in range(tok_count // ROWS):
        rows = pl.ds(chunk * ROWS, ROWS)
        q = qh_buf[rows, :]
        s_old = lax.dot_general(q, kh_buf[...], dims, preferred_element_type=jnp.float32)
        s_new = lax.dot_general(q, kn, dims, preferred_element_type=jnp.float32)
        s_old = s_old * score_scale
        s_new = s_new * score_scale
        col = lax.broadcasted_iota(jnp.int32, s_old.shape, 1)
        s_old = jnp.where(col < group_len, s_old, -1e30)
        row = chunk * ROWS + lax.broadcasted_iota(jnp.int32, s_new.shape, 0)
        key = lax.broadcasted_iota(jnp.int32, s_new.shape, 1)
        same = request_of(row, group_requests, tok_count) == request_of(
            key, group_requests, tok_count
        )
        s_new = jnp.where(same & (key <= row), s_new, -1e30)
        peak = jnp.maximum(
            jnp.max(s_old, axis=1, keepdims=True), jnp.max(s_new, axis=1, keepdims=True)
        )
        e_old = jnp.exp(s_old - peak)
        e_new = jnp.exp(s_new - peak)
        total = jnp.sum(e_old, axis=1, keepdims=True) + jnp.sum(e_new, axis=1, keepdims=True)
        p_old = (e_old / total).astype(jnp.bfloat16)
        p_new = (e_new / total).astype(jnp.bfloat16)
        out = jnp.dot(p_old, vh_buf[...], preferred_element_type=jnp.float32) + jnp.dot(
            p_new, vn, preferred_element_type=jnp.float32
        )
        placed = lax.dot_general(
            out.astype(jnp.bfloat16), picker, dims, preferred_element_type=jnp.float32
        )

        @pl.when(head == 0)
        def _():
            acc_ref[rows, :] = placed

        @pl.when(head > 0)
        def _():
            acc_ref[rows, :] = acc_ref[rows, :] + placed

    @pl.when(head == pl.num_programs(0) - 1)
    def _():
        o_ref[...] = acc_ref[...].astype(jnp.bfloat16)


def attend(meta, queries, kv_cache, new_kv):
    tok_count, features = queries.shape
    cache_len = kv_cache.shape[2]
    full_q = pl.BlockSpec((tok_count, features), lambda h, m: (0, 0))
    cache_k = pl.BlockSpec((1, 1, cache_len, features), lambda h, m: (0, 0, 0, 0))
    cache_v = pl.BlockSpec((1, 1, cache_len, features), lambda h, m: (1, 0, 0, 0))
    new_k = pl.BlockSpec((1, tok_count, features), lambda h, m: (0, 0, 0))
    new_v = pl.BlockSpec((1, tok_count, features), lambda h, m: (1, 0, 0))
    return pl.pallas_call(
        attention_kernel,
        out_shape=jax.ShapeDtypeStruct(queries.shape, jnp.bfloat16),
        grid_spec=pltpu.PrefetchScalarGridSpec(
            num_scalar_prefetch=1,
            grid=(features // HD,),
            in_specs=[full_q, cache_k, cache_v, new_k, new_v],
            out_specs=full_q,
            scratch_shapes=[
                pltpu.VMEM((cache_len, HD), jnp.bfloat16),
                pltpu.VMEM((cache_len, HD), jnp.bfloat16),
                pltpu.VMEM((tok_count, HD), jnp.bfloat16),
                pltpu.VMEM((tok_count, features), jnp.float32),
            ],
        ),
    )(meta, queries, kv_cache, kv_cache, new_kv, new_kv)


def relay_kernel(meta_ref, *refs, new_blocks):
    out_ref = refs[-1]
    sources = refs[:-1]
    len_blocks = meta_ref[0] // BLK
    group_start = meta_ref[2]
    core = meta_ref[3]
    per_step = out_ref.shape[0]
    rank_count = 2 * pl.num_programs(0) * per_step
    features = sources[1].shape[2]
    zero = jnp.zeros(sources[1].shape[1:], sources[1].dtype)
    first = core == 0
    for slot in range(per_step):
        own_c, own_n, mate_c, mate_n = sources[4 * slot : 4 * slot + 4]
        dest = pl.program_id(0) * per_step + slot
        block = (2 * dest + core - group_start + rank_count) % rank_count
        old = block < len_blocks
        fresh = (block >= len_blocks) & (block < len_blocks + new_blocks)
        for kv in range(2):
            mine = jnp.where(old, own_c[kv, 0], jnp.where(fresh, own_n[kv], zero))
            mate = jnp.where(old, mate_c[kv, 0], jnp.where(fresh, mate_n[kv], zero))
            out_ref[slot, kv, :, :features] = jnp.where(first, mine, mate)
            out_ref[slot, kv, :, features:] = jnp.where(first, mate, mine)


def relay(meta, kv_cache, new_kv, mate_cache, mate_new, seq_count):
    features = kv_cache.shape[3]
    new_blocks = new_kv.shape[1] // BLK
    rank_count = 2 * seq_count
    per_step = 4 if seq_count % 4 == 0 else 1

    def block_of(d, slot, m):
        return (2 * (d * per_step + slot) + m[3] - m[2] + rank_count) % rank_count

    def cache_spec(slot):
        return pl.BlockSpec(
            (2, 1, BLK, features),
            lambda d, m: (0, 0, jnp.clip(block_of(d, slot, m), 0, m[0] // BLK - 1), 0),
        )

    def new_spec(slot):
        return pl.BlockSpec(
            (2, BLK, features),
            lambda d, m: (
                0,
                jnp.clip(block_of(d, slot, m) - m[0] // BLK, 0, new_blocks - 1),
                0,
            ),
        )

    in_specs = []
    operands = []
    for slot in range(per_step):
        in_specs += [cache_spec(slot), new_spec(slot), cache_spec(slot), new_spec(slot)]
        operands += [kv_cache, new_kv, mate_cache, mate_new]
    return pl.pallas_call(
        functools.partial(relay_kernel, new_blocks=new_blocks),
        out_shape=jax.ShapeDtypeStruct((seq_count, 2, BLK, 2 * features), jnp.bfloat16),
        grid_spec=pltpu.PrefetchScalarGridSpec(
            num_scalar_prefetch=1,
            grid=(seq_count // per_step,),
            in_specs=in_specs,
            out_specs=pl.BlockSpec(
                (per_step, 2, BLK, 2 * features), lambda d, m: (d, 0, 0, 0)
            ),
        ),
    )(meta, *operands)


def half_swap(features):
    half = HD // 2
    rows = lax.broadcasted_iota(jnp.int32, (features, features), 0)
    cols = lax.broadcasted_iota(jnp.int32, (features, features), 1)
    first = cols % HD < half
    return jnp.where(
        first & (rows == cols + half),
        -1.0,
        jnp.where(jnp.logical_not(first) & (rows == cols - half), 1.0, 0.0),
    ).astype(jnp.bfloat16)


def projection_kernel(meta_ref, x_ref, gain_ref, freq_ref, *refs, parts):
    w_refs = refs[: len(parts)]
    out_ref = refs[len(parts)]
    rows = x_ref.shape[0]
    tok_count = rows * pl.num_programs(0)
    inputs = x_ref[...].astype(jnp.float32)
    inverse_rms = lax.rsqrt(jnp.mean(inputs * inputs, axis=-1, keepdims=True) + 1e-05)
    gain = gain_ref[...].astype(jnp.float32).reshape(1, inputs.shape[1])
    normed = (inputs * inverse_rms * gain).astype(jnp.bfloat16)
    for index, part in enumerate(parts):
        plain = jnp.dot(normed, w_refs[index][0], preferred_element_type=jnp.float32)
        if part == 2:
            out_ref[index] = plain.astype(out_ref.dtype)
            continue
        features = plain.shape[1]
        half = HD // 2
        group_len = meta_ref[0]
        group_requests = meta_ref[1]
        row = pl.program_id(0) * rows + lax.broadcasted_iota(jnp.int32, (rows, 1), 0)
        request = request_of(row, group_requests, tok_count)
        count = (jnp.zeros((rows, 1), jnp.int32) + group_requests).astype(jnp.float32)
        first = jnp.ceil((request * tok_count).astype(jnp.float32) / count).astype(jnp.int32)
        positions = (group_len + row - first).astype(jnp.float32)
        angles = positions * freq_ref[...].reshape(1, features)
        lane = lax.broadcasted_iota(jnp.int32, plain.shape, 1)
        ahead = pltpu.roll(plain, features - half, 1)
        behind = pltpu.roll(plain, half, 1)
        paired = jnp.where(lane % HD < half, -ahead, behind)
        rotated = plain * jnp.cos(angles) + paired * jnp.sin(angles)
        out_ref[index] = rotated.astype(out_ref.dtype)


def project(meta, tokens, gain, weights, frequency, parts):
    _, width, features = weights.shape
    tok_count = tokens.shape[0]
    rows = 128 if tok_count % 128 == 0 else tok_count

    def weight_spec(part):
        return pl.BlockSpec((1, width, features), lambda r, m: (part, 0, 0))

    return pl.pallas_call(
        functools.partial(projection_kernel, parts=parts),
        out_shape=jax.ShapeDtypeStruct((len(parts), tok_count, features), jnp.bfloat16),
        grid_spec=pltpu.PrefetchScalarGridSpec(
            num_scalar_prefetch=1,
            grid=(tok_count // rows,),
            in_specs=[
                pl.BlockSpec((rows, width), lambda r, m: (r, 0)),
                pl.BlockSpec((width,), lambda r, m: (0,)),
                pl.BlockSpec((features,), lambda r, m: (0,)),
            ]
            + [weight_spec(part) for part in parts],
            out_specs=pl.BlockSpec((len(parts), rows, features), lambda r, m: (0, r, 0)),
        ),
    )(meta, tokens, gain, frequency, *(weights for _ in parts))


def local(tokens, norm_gain, w_qkv, w_out, kv_cache, cached_lengths, requests, block_start):
    group_idx = lax.axis_index("seq")
    tp_rank = lax.axis_index(("x", "core"))
    tp_count = lax.axis_size(("x", "core"))
    seq_count = lax.axis_size("seq")
    tok_count, model_width = tokens.shape
    features = w_qkv.shape[2]
    head_count = features // HD
    cache_len = kv_cache.shape[2]
    group_params = lax.dynamic_index_in_dim(
        jnp.stack([cached_lengths, requests, block_start], axis=1), group_idx, keepdims=False
    )
    group_len = group_params[0]
    group_requests = group_params[1]
    group_start = group_params[2]
    inputs = tokens.astype(jnp.float32)

    weights = jnp.transpose(w_qkv, (1, 0, 2))
    half_size = HD // 2
    frequency = jnp.exp(
        jnp.arange(half_size, dtype=jnp.float32) * (-2.0 * math.log(10000.0) / HD)
    )
    frequency = jnp.tile(frequency, features // half_size)
    gain = norm_gain
    core = lax.axis_index("core")
    swap_cores = [(0, 1), (1, 0)]
    mate_cache = lax.ppermute(kv_cache, "core", swap_cores)
    meta = jnp.concatenate([group_params, jnp.reshape(core, (1,))]).astype(jnp.int32)
    new_kv = project(meta, tokens, gain, weights, frequency, (1, 2))
    mate_new = lax.ppermute(new_kv, "core", swap_cores)
    joined = relay(meta, kv_cache, new_kv, mate_cache, mate_new, seq_count)
    queries = project(meta, tokens, gain, weights, frequency, (0,))[0]
    joined, attn_kv = lax.optimization_barrier((joined, new_kv))
    received = lax.all_to_all(joined, "seq", 0, 0, tiled=True)
    decode_cache = received.transpose(1, 0, 2, 3).reshape(2, 1, seq_count, 1, BLK, 2 * features)

    attended = attend(meta, queries, kv_cache, attn_kv)
    rows_dev = tok_count // tp_count
    partial = jnp.dot(attended, w_out, preferred_element_type=jnp.float32).astype(jnp.bfloat16)
    x_count = tp_count // 2
    x_rank = lax.axis_index("x")
    by_owner = partial.reshape(x_count, 2, rows_dev, model_width)
    mine = lax.dynamic_index_in_dim(by_owner, core, 1, keepdims=False)
    theirs = lax.dynamic_index_in_dim(by_owner, 1 - core, 1, keepdims=False)
    pair_sum = mine.astype(jnp.float32) + lax.ppermute(theirs, "core", swap_cores).astype(
        jnp.float32
    )
    pair_sent = pair_sum.astype(jnp.bfloat16)
    summed = lax.dynamic_index_in_dim(pair_sum, x_rank, 0, keepdims=False)
    for shift in range(1, x_count):
        target = (x_rank + shift) % x_count
        chunk = lax.dynamic_index_in_dim(pair_sent, target, 0, keepdims=False)
        pairs = [(source, (source + shift) % x_count) for source in range(x_count)]
        summed = summed + lax.ppermute(chunk, "x", pairs).astype(jnp.float32)
    own_rows = lax.dynamic_slice_in_dim(inputs, tp_rank * rows_dev, rows_dev, 0)
    layer_out = (own_rows + summed).astype(jnp.bfloat16)
    return (layer_out, decode_cache)


def solution(mesh):
    seq_count, tp_count = mesh.devices.shape
    split = Mesh(mesh.devices.reshape(seq_count, tp_count // 2, 2), ("seq", "x", "core"))
    tp = ("x", "core")
    placed = (
        P("seq", None),
        P(),
        P(None, None, tp),
        P(tp, None),
        P(None, "seq", None, tp),
        P(),
        P(),
        P(),
    )
    return jax.shard_map(
        local,
        mesh=split,
        in_specs=placed,
        out_specs=(P(("seq",) + tp, None), P(None, "seq", None, None, None, tp)),
        check_vma=False,
    )
```

```python
import functools
import math

import jax
import jax.numpy as jnp
from jax import lax
from jax.experimental import pallas as pl
from jax.experimental.pallas import tpu as pltpu
from jax.sharding import Mesh
from jax.sharding import PartitionSpec as P

HD = 96
BLK = 128
ROWS = 128


def rope_tables(positions, head_size):
    half_size = head_size // 2
    frequency = jnp.exp(
        jnp.arange(half_size, dtype=jnp.float32) * (-2.0 * math.log(10000.0) / head_size)
    )
    angles = positions.astype(jnp.float32)[:, None] * frequency[None, :]
    return (jnp.cos(angles), jnp.sin(angles))


def rope_pair(vectors, cosine_table, sine_table):
    half_size = vectors.shape[-1] // 2
    first_half = vectors[..., :half_size]
    second_half = vectors[..., half_size:]
    cos_wide = cosine_table[:, None, :]
    sin_wide = sine_table[:, None, :]
    return jnp.concatenate(
        [
            first_half * cos_wide - second_half * sin_wide,
            second_half * cos_wide + first_half * sin_wide,
        ],
        axis=-1,
    )


def request_of(index, group_requests, tok_count):
    scaled = index * group_requests
    if tok_count & (tok_count - 1) == 0:
        return lax.shift_right_logical(scaled, tok_count.bit_length() - 1)
    return scaled // tok_count


def head_picker(features, head):
    rows = lax.broadcasted_iota(jnp.int32, (features, HD), 0)
    cols = lax.broadcasted_iota(jnp.int32, (features, HD), 1)
    return (rows == cols + head * HD).astype(jnp.bfloat16)


def attention_kernel(
    meta_ref, q_ref, kc_ref, vc_ref, kn_ref, vn_ref, o_ref, kh_buf, vh_buf, qh_buf, acc_ref
):
    group_len = meta_ref[0]
    group_requests = meta_ref[1]
    head = pl.program_id(0)
    tok_count, features = q_ref.shape
    score_scale = 1.0 / math.sqrt(HD)
    picker = head_picker(features, head)

    def pick(values):
        return jnp.dot(values, picker, preferred_element_type=jnp.float32).astype(jnp.bfloat16)

    kh_buf[...] = pick(kc_ref[0, 0])
    vh_buf[...] = pick(vc_ref[0, 0])
    qh_buf[...] = pick(q_ref[...])
    kn = pick(kn_ref[0])
    vn = pick(vn_ref[0])
    dims = (((1,), (1,)), ((), ()))
    for chunk in range(tok_count // ROWS):
        rows = pl.ds(chunk * ROWS, ROWS)
        q = qh_buf[rows, :]
        s_old = lax.dot_general(q, kh_buf[...], dims, preferred_element_type=jnp.float32)
        s_new = lax.dot_general(q, kn, dims, preferred_element_type=jnp.float32)
        s_old = s_old * score_scale
        s_new = s_new * score_scale
        col = lax.broadcasted_iota(jnp.int32, s_old.shape, 1)
        s_old = jnp.where(col < group_len, s_old, -1e30)
        row = chunk * ROWS + lax.broadcasted_iota(jnp.int32, s_new.shape, 0)
        key = lax.broadcasted_iota(jnp.int32, s_new.shape, 1)
        same = request_of(row, group_requests, tok_count) == request_of(
            key, group_requests, tok_count
        )
        s_new = jnp.where(same & (key <= row), s_new, -1e30)
        peak = jnp.maximum(
            jnp.max(s_old, axis=1, keepdims=True), jnp.max(s_new, axis=1, keepdims=True)
        )
        e_old = jnp.exp(s_old - peak)
        e_new = jnp.exp(s_new - peak)
        total = jnp.sum(e_old, axis=1, keepdims=True) + jnp.sum(e_new, axis=1, keepdims=True)
        p_old = (e_old / total).astype(jnp.bfloat16)
        p_new = (e_new / total).astype(jnp.bfloat16)
        out = jnp.dot(p_old, vh_buf[...], preferred_element_type=jnp.float32) + jnp.dot(
            p_new, vn, preferred_element_type=jnp.float32
        )
        placed = lax.dot_general(
            out.astype(jnp.bfloat16), picker, dims, preferred_element_type=jnp.float32
        )

        @pl.when(head == 0)
        def _():
            acc_ref[rows, :] = placed

        @pl.when(head > 0)
        def _():
            acc_ref[rows, :] = acc_ref[rows, :] + placed

    @pl.when(head == pl.num_programs(0) - 1)
    def _():
        o_ref[...] = acc_ref[...].astype(jnp.bfloat16)


def attend(meta, queries, kv_cache, new_kv):
    tok_count, features = queries.shape
    cache_len = kv_cache.shape[2]
    full_q = pl.BlockSpec((tok_count, features), lambda h, m: (0, 0))
    cache_k = pl.BlockSpec((1, 1, cache_len, features), lambda h, m: (0, 0, 0, 0))
    cache_v = pl.BlockSpec((1, 1, cache_len, features), lambda h, m: (1, 0, 0, 0))
    new_k = pl.BlockSpec((1, tok_count, features), lambda h, m: (0, 0, 0))
    new_v = pl.BlockSpec((1, tok_count, features), lambda h, m: (1, 0, 0))
    return pl.pallas_call(
        attention_kernel,
        out_shape=jax.ShapeDtypeStruct(queries.shape, jnp.bfloat16),
        grid_spec=pltpu.PrefetchScalarGridSpec(
            num_scalar_prefetch=1,
            grid=(features // HD,),
            in_specs=[full_q, cache_k, cache_v, new_k, new_v],
            out_specs=full_q,
            scratch_shapes=[
                pltpu.VMEM((cache_len, HD), jnp.bfloat16),
                pltpu.VMEM((cache_len, HD), jnp.bfloat16),
                pltpu.VMEM((tok_count, HD), jnp.bfloat16),
                pltpu.VMEM((tok_count, features), jnp.float32),
            ],
        ),
    )(meta, queries, kv_cache, kv_cache, new_kv, new_kv)


def relay_kernel(meta_ref, *refs, new_blocks):
    out_ref = refs[-1]
    sources = refs[:-1]
    len_blocks = meta_ref[0] // BLK
    group_start = meta_ref[2]
    core = meta_ref[3]
    per_step = out_ref.shape[0]
    rank_count = 2 * pl.num_programs(0) * per_step
    features = sources[1].shape[2]
    zero = jnp.zeros(sources[1].shape[1:], sources[1].dtype)
    first = core == 0
    for slot in range(per_step):
        own_c, own_n, mate_c, mate_n = sources[4 * slot : 4 * slot + 4]
        dest = pl.program_id(0) * per_step + slot
        block = (2 * dest + core - group_start + rank_count) % rank_count
        old = block < len_blocks
        fresh = (block >= len_blocks) & (block < len_blocks + new_blocks)
        for kv in range(2):
            mine = jnp.where(old, own_c[kv, 0], jnp.where(fresh, own_n[kv], zero))
            mate = jnp.where(old, mate_c[kv, 0], jnp.where(fresh, mate_n[kv], zero))
            out_ref[slot, kv, :, :features] = jnp.where(first, mine, mate)
            out_ref[slot, kv, :, features:] = jnp.where(first, mate, mine)


def relay(meta, kv_cache, new_kv, mate_cache, mate_new, seq_count):
    features = kv_cache.shape[3]
    new_blocks = new_kv.shape[1] // BLK
    rank_count = 2 * seq_count
    per_step = 4 if seq_count % 4 == 0 else 1

    def block_of(d, slot, m):
        return (2 * (d * per_step + slot) + m[3] - m[2] + rank_count) % rank_count

    def cache_spec(slot):
        return pl.BlockSpec(
            (2, 1, BLK, features),
            lambda d, m: (0, 0, jnp.clip(block_of(d, slot, m), 0, m[0] // BLK - 1), 0),
        )

    def new_spec(slot):
        return pl.BlockSpec(
            (2, BLK, features),
            lambda d, m: (
                0,
                jnp.clip(block_of(d, slot, m) - m[0] // BLK, 0, new_blocks - 1),
                0,
            ),
        )

    in_specs = []
    operands = []
    for slot in range(per_step):
        in_specs += [cache_spec(slot), new_spec(slot), cache_spec(slot), new_spec(slot)]
        operands += [kv_cache, new_kv, mate_cache, mate_new]
    return pl.pallas_call(
        functools.partial(relay_kernel, new_blocks=new_blocks),
        out_shape=jax.ShapeDtypeStruct((seq_count, 2, BLK, 2 * features), jnp.bfloat16),
        grid_spec=pltpu.PrefetchScalarGridSpec(
            num_scalar_prefetch=1,
            grid=(seq_count // per_step,),
            in_specs=in_specs,
            out_specs=pl.BlockSpec(
                (per_step, 2, BLK, 2 * features), lambda d, m: (d, 0, 0, 0)
            ),
        ),
    )(meta, *operands)


def half_swap(features):
    half = HD // 2
    rows = lax.broadcasted_iota(jnp.int32, (features, features), 0)
    cols = lax.broadcasted_iota(jnp.int32, (features, features), 1)
    first = cols % HD < half
    return jnp.where(
        first & (rows == cols + half),
        -1.0,
        jnp.where(jnp.logical_not(first) & (rows == cols - half), 1.0, 0.0),
    ).astype(jnp.bfloat16)


def projection_kernel(meta_ref, x_ref, gain_ref, freq_ref, *refs, parts):
    w_refs = refs[: len(parts)]
    out_ref = refs[len(parts)]
    rows = x_ref.shape[0]
    tok_count = rows * pl.num_programs(0)
    inputs = x_ref[...].astype(jnp.float32)
    inverse_rms = lax.rsqrt(jnp.mean(inputs * inputs, axis=-1, keepdims=True) + 1e-05)
    gain = gain_ref[...].astype(jnp.float32).reshape(1, inputs.shape[1])
    normed = (inputs * inverse_rms * gain).astype(jnp.bfloat16)
    for index, part in enumerate(parts):
        plain = jnp.dot(normed, w_refs[index][0], preferred_element_type=jnp.float32)
        if part == 2:
            out_ref[index] = plain.astype(out_ref.dtype)
            continue
        features = plain.shape[1]
        half = HD // 2
        group_len = meta_ref[0]
        group_requests = meta_ref[1]
        row = pl.program_id(0) * rows + lax.broadcasted_iota(jnp.int32, (rows, 1), 0)
        request = request_of(row, group_requests, tok_count)
        count = (jnp.zeros((rows, 1), jnp.int32) + group_requests).astype(jnp.float32)
        first = jnp.ceil((request * tok_count).astype(jnp.float32) / count).astype(jnp.int32)
        positions = (group_len + row - first).astype(jnp.float32)
        angles = positions * freq_ref[...]
        lane = lax.broadcasted_iota(jnp.int32, plain.shape, 1)
        ahead = pltpu.roll(plain, features - half, 1)
        behind = pltpu.roll(plain, half, 1)
        paired = jnp.where(lane % HD < half, -ahead, behind)
        rotated = plain * jnp.cos(angles) + paired * jnp.sin(angles)
        out_ref[index] = rotated.astype(out_ref.dtype)


def project(meta, tokens, gain, weights, frequency, parts):
    _, width, features = weights.shape
    tok_count = tokens.shape[0]
    rows = 128 if tok_count % 128 == 0 else tok_count

    def weight_spec(part):
        return pl.BlockSpec((1, width, features), lambda r, m: (part, 0, 0))

    return pl.pallas_call(
        functools.partial(projection_kernel, parts=parts),
        out_shape=jax.ShapeDtypeStruct((len(parts), tok_count, features), jnp.bfloat16),
        grid_spec=pltpu.PrefetchScalarGridSpec(
            num_scalar_prefetch=1,
            grid=(tok_count // rows,),
            in_specs=[
                pl.BlockSpec((rows, width), lambda r, m: (r, 0)),
                pl.BlockSpec((width,), lambda r, m: (0,)),
                pl.BlockSpec((1, features), lambda r, m: (0, 0)),
            ]
            + [weight_spec(part) for part in parts],
            out_specs=pl.BlockSpec((len(parts), rows, features), lambda r, m: (0, r, 0)),
        ),
    )(meta, tokens, gain, frequency, *(weights for _ in parts))


def local(tokens, norm_gain, w_qkv, w_out, kv_cache, cached_lengths, requests, block_start):
    group_idx = lax.axis_index("seq")
    tp_rank = lax.axis_index(("x", "core"))
    tp_count = lax.axis_size(("x", "core"))
    seq_count = lax.axis_size("seq")
    tok_count, model_width = tokens.shape
    features = w_qkv.shape[2]
    head_count = features // HD
    cache_len = kv_cache.shape[2]
    core = lax.axis_index("core")
    group_table = jnp.stack(
        [cached_lengths, requests, block_start, jnp.zeros_like(cached_lengths) + core], axis=1
    )
    group_params = lax.dynamic_index_in_dim(group_table, group_idx, keepdims=False).astype(
        jnp.int32
    )
    group_len = group_params[0]
    group_requests = group_params[1]
    group_start = group_params[2]
    inputs = tokens.astype(jnp.float32)

    weights = jnp.transpose(w_qkv, (1, 0, 2))
    half_size = HD // 2
    frequency = jnp.exp(
        jnp.arange(half_size, dtype=jnp.float32) * (-2.0 * math.log(10000.0) / HD)
    )
    frequency = jnp.tile(frequency, features // half_size).reshape(1, features)
    gain = norm_gain
    swap_cores = [(0, 1), (1, 0)]
    mate_cache = lax.ppermute(kv_cache, "core", swap_cores)
    meta = group_params
    new_kv = project(meta, tokens, gain, weights, frequency, (1, 2))
    mate_new = lax.ppermute(new_kv, "core", swap_cores)
    joined = relay(meta, kv_cache, new_kv, mate_cache, mate_new, seq_count)
    queries = project(meta, tokens, gain, weights, frequency, (0,))[0]
    joined, attn_kv = lax.optimization_barrier((joined, new_kv))
    received = lax.all_to_all(joined, "seq", 0, 0, tiled=True)
    decode_cache = received.transpose(1, 0, 2, 3).reshape(2, 1, seq_count, 1, BLK, 2 * features)

    attended = attend(meta, queries, kv_cache, attn_kv)
    rows_dev = tok_count // tp_count
    partial = jnp.dot(attended, w_out, preferred_element_type=jnp.float32).astype(jnp.bfloat16)
    x_count = tp_count // 2
    x_rank = lax.axis_index("x")
    by_owner = partial.reshape(x_count, 2, rows_dev, model_width)
    mine = lax.dynamic_index_in_dim(by_owner, core, 1, keepdims=False)
    theirs = lax.dynamic_index_in_dim(by_owner, 1 - core, 1, keepdims=False)
    pair_sum = mine.astype(jnp.float32) + lax.ppermute(theirs, "core", swap_cores).astype(
        jnp.float32
    )
    pair_sent = pair_sum.astype(jnp.bfloat16)
    summed = lax.dynamic_index_in_dim(pair_sum, x_rank, 0, keepdims=False)
    for shift in range(1, x_count):
        target = (x_rank + shift) % x_count
        chunk = lax.dynamic_index_in_dim(pair_sent, target, 0, keepdims=False)
        pairs = [(source, (source + shift) % x_count) for source in range(x_count)]
        summed = summed + lax.ppermute(chunk, "x", pairs).astype(jnp.float32)
    own_rows = lax.dynamic_slice_in_dim(inputs, tp_rank * rows_dev, rows_dev, 0)
    layer_out = (own_rows + summed).astype(jnp.bfloat16)
    return (layer_out, decode_cache)


def solution(mesh):
    seq_count, tp_count = mesh.devices.shape
    split = Mesh(mesh.devices.reshape(seq_count, tp_count // 2, 2), ("seq", "x", "core"))
    tp = ("x", "core")
    placed = (
        P("seq", None),
        P(),
        P(None, None, tp),
        P(tp, None),
        P(None, "seq", None, tp),
        P(),
        P(),
        P(),
    )
    return jax.shard_map(
        local,
        mesh=split,
        in_specs=placed,
        out_specs=(P(("seq",) + tp, None), P(None, "seq", None, None, None, tp)),
        check_vma=False,
    )
```

```python
import functools
import math

import jax
import jax.numpy as jnp
from jax import lax
from jax.experimental import pallas as pl
from jax.experimental.pallas import tpu as pltpu
from jax.sharding import Mesh
from jax.sharding import PartitionSpec as P

HD = 96
BLK = 128
ROWS = 128


def rope_tables(positions, head_size):
    half_size = head_size // 2
    frequency = jnp.exp(
        jnp.arange(half_size, dtype=jnp.float32) * (-2.0 * math.log(10000.0) / head_size)
    )
    angles = positions.astype(jnp.float32)[:, None] * frequency[None, :]
    return (jnp.cos(angles), jnp.sin(angles))


def rope_pair(vectors, cosine_table, sine_table):
    half_size = vectors.shape[-1] // 2
    first_half = vectors[..., :half_size]
    second_half = vectors[..., half_size:]
    cos_wide = cosine_table[:, None, :]
    sin_wide = sine_table[:, None, :]
    return jnp.concatenate(
        [
            first_half * cos_wide - second_half * sin_wide,
            second_half * cos_wide + first_half * sin_wide,
        ],
        axis=-1,
    )


def request_of(index, group_requests, tok_count):
    scaled = index * group_requests
    if tok_count & (tok_count - 1) == 0:
        return lax.shift_right_logical(scaled, tok_count.bit_length() - 1)
    return scaled // tok_count


def head_picker(features, head):
    rows = lax.broadcasted_iota(jnp.int32, (features, HD), 0)
    cols = lax.broadcasted_iota(jnp.int32, (features, HD), 1)
    return (rows == cols + head * HD).astype(jnp.bfloat16)


def attention_kernel(
    meta_ref, q_ref, kc_ref, vc_ref, kn_ref, vn_ref, o_ref, kh_buf, vh_buf, qh_buf, acc_ref
):
    group_len = meta_ref[0]
    group_requests = meta_ref[1]
    head = pl.program_id(0)
    tok_count, features = q_ref.shape
    score_scale = 1.0 / math.sqrt(HD)
    picker = head_picker(features, head)

    def pick(values):
        return jnp.dot(values, picker, preferred_element_type=jnp.float32).astype(jnp.bfloat16)

    kh_buf[...] = pick(kc_ref[0, 0])
    vh_buf[...] = pick(vc_ref[0, 0])
    qh_buf[...] = pick(q_ref[...])
    kn = pick(kn_ref[0])
    vn = pick(vn_ref[0])
    dims = (((1,), (1,)), ((), ()))
    for chunk in range(tok_count // ROWS):
        rows = pl.ds(chunk * ROWS, ROWS)
        q = qh_buf[rows, :]
        s_old = lax.dot_general(q, kh_buf[...], dims, preferred_element_type=jnp.float32)
        s_new = lax.dot_general(q, kn, dims, preferred_element_type=jnp.float32)
        s_old = s_old * score_scale
        s_new = s_new * score_scale
        col = lax.broadcasted_iota(jnp.int32, s_old.shape, 1)
        s_old = jnp.where(col < group_len, s_old, -1e30)
        row = chunk * ROWS + lax.broadcasted_iota(jnp.int32, s_new.shape, 0)
        key = lax.broadcasted_iota(jnp.int32, s_new.shape, 1)
        same = request_of(row, group_requests, tok_count) == request_of(
            key, group_requests, tok_count
        )
        s_new = jnp.where(same & (key <= row), s_new, -1e30)
        peak = jnp.maximum(
            jnp.max(s_old, axis=1, keepdims=True), jnp.max(s_new, axis=1, keepdims=True)
        )
        e_old = jnp.exp(s_old - peak)
        e_new = jnp.exp(s_new - peak)
        total = jnp.sum(e_old, axis=1, keepdims=True) + jnp.sum(e_new, axis=1, keepdims=True)
        p_old = (e_old / total).astype(jnp.bfloat16)
        p_new = (e_new / total).astype(jnp.bfloat16)
        out = jnp.dot(p_old, vh_buf[...], preferred_element_type=jnp.float32) + jnp.dot(
            p_new, vn, preferred_element_type=jnp.float32
        )
        placed = lax.dot_general(
            out.astype(jnp.bfloat16), picker, dims, preferred_element_type=jnp.float32
        )

        @pl.when(head == 0)
        def _():
            acc_ref[rows, :] = placed

        @pl.when(head > 0)
        def _():
            acc_ref[rows, :] = acc_ref[rows, :] + placed

    @pl.when(head == pl.num_programs(0) - 1)
    def _():
        o_ref[...] = acc_ref[...].astype(jnp.bfloat16)


def attend(meta, queries, kv_cache, new_kv):
    tok_count, features = queries.shape
    cache_len = kv_cache.shape[2]
    full_q = pl.BlockSpec((tok_count, features), lambda h, m: (0, 0))
    cache_k = pl.BlockSpec((1, 1, cache_len, features), lambda h, m: (0, 0, 0, 0))
    cache_v = pl.BlockSpec((1, 1, cache_len, features), lambda h, m: (1, 0, 0, 0))
    new_k = pl.BlockSpec((1, tok_count, features), lambda h, m: (0, 0, 0))
    new_v = pl.BlockSpec((1, tok_count, features), lambda h, m: (1, 0, 0))
    return pl.pallas_call(
        attention_kernel,
        out_shape=jax.ShapeDtypeStruct(queries.shape, jnp.bfloat16),
        grid_spec=pltpu.PrefetchScalarGridSpec(
            num_scalar_prefetch=1,
            grid=(features // HD,),
            in_specs=[full_q, cache_k, cache_v, new_k, new_v],
            out_specs=full_q,
            scratch_shapes=[
                pltpu.VMEM((cache_len, HD), jnp.bfloat16),
                pltpu.VMEM((cache_len, HD), jnp.bfloat16),
                pltpu.VMEM((tok_count, HD), jnp.bfloat16),
                pltpu.VMEM((tok_count, features), jnp.float32),
            ],
        ),
    )(meta, queries, kv_cache, kv_cache, new_kv, new_kv)


def relay_kernel(meta_ref, *refs, new_blocks):
    out_ref = refs[-1]
    sources = refs[:-1]
    len_blocks = meta_ref[0] // BLK
    group_start = meta_ref[2]
    core = meta_ref[3]
    per_step = out_ref.shape[0]
    rank_count = 2 * pl.num_programs(0) * per_step
    features = sources[1].shape[2]
    zero = jnp.zeros(sources[1].shape[1:], sources[1].dtype)
    first = core == 0
    for slot in range(per_step):
        own_c, own_n, mate_c, mate_n = sources[4 * slot : 4 * slot + 4]
        dest = pl.program_id(0) * per_step + slot
        block = (2 * dest + core - group_start + rank_count) % rank_count
        old = block < len_blocks
        fresh = (block >= len_blocks) & (block < len_blocks + new_blocks)
        for kv in range(2):
            mine = jnp.where(old, own_c[kv, 0], jnp.where(fresh, own_n[kv], zero))
            mate = jnp.where(old, mate_c[kv, 0], jnp.where(fresh, mate_n[kv], zero))
            out_ref[slot, kv, :, :features] = jnp.where(first, mine, mate)
            out_ref[slot, kv, :, features:] = jnp.where(first, mate, mine)


def relay(meta, kv_cache, new_kv, mate_cache, mate_new, seq_count):
    features = kv_cache.shape[3]
    new_blocks = new_kv.shape[1] // BLK
    rank_count = 2 * seq_count
    per_step = 4 if seq_count % 4 == 0 else 1

    def block_of(d, slot, m):
        return (2 * (d * per_step + slot) + m[3] - m[2] + rank_count) % rank_count

    def cache_spec(slot):
        return pl.BlockSpec(
            (2, 1, BLK, features),
            lambda d, m: (0, 0, jnp.clip(block_of(d, slot, m), 0, m[0] // BLK - 1), 0),
        )

    def new_spec(slot):
        return pl.BlockSpec(
            (2, BLK, features),
            lambda d, m: (
                0,
                jnp.clip(block_of(d, slot, m) - m[0] // BLK, 0, new_blocks - 1),
                0,
            ),
        )

    in_specs = []
    operands = []
    for slot in range(per_step):
        in_specs += [cache_spec(slot), new_spec(slot), cache_spec(slot), new_spec(slot)]
        operands += [kv_cache, new_kv, mate_cache, mate_new]
    return pl.pallas_call(
        functools.partial(relay_kernel, new_blocks=new_blocks),
        out_shape=jax.ShapeDtypeStruct((seq_count, 2, BLK, 2 * features), jnp.bfloat16),
        grid_spec=pltpu.PrefetchScalarGridSpec(
            num_scalar_prefetch=1,
            grid=(seq_count // per_step,),
            in_specs=in_specs,
            out_specs=pl.BlockSpec(
                (per_step, 2, BLK, 2 * features), lambda d, m: (d, 0, 0, 0)
            ),
        ),
    )(meta, *operands)


def half_swap(features):
    half = HD // 2
    rows = lax.broadcasted_iota(jnp.int32, (features, features), 0)
    cols = lax.broadcasted_iota(jnp.int32, (features, features), 1)
    first = cols % HD < half
    return jnp.where(
        first & (rows == cols + half),
        -1.0,
        jnp.where(jnp.logical_not(first) & (rows == cols - half), 1.0, 0.0),
    ).astype(jnp.bfloat16)


def projection_kernel(meta_ref, x_ref, gain_ref, freq_ref, *refs, parts):
    w_refs = refs[: len(parts)]
    out_ref = refs[len(parts)]
    rows = x_ref.shape[0]
    tok_count = rows * pl.num_programs(0)
    inputs = x_ref[...].astype(jnp.float32)
    inverse_rms = lax.rsqrt(jnp.mean(inputs * inputs, axis=-1, keepdims=True) + 1e-05)
    gain = gain_ref[...].astype(jnp.float32).reshape(1, inputs.shape[1])
    normed = (inputs * inverse_rms * gain).astype(jnp.bfloat16)
    for index, part in enumerate(parts):
        plain = jnp.dot(normed, w_refs[index][0], preferred_element_type=jnp.float32)
        if part == 2:
            out_ref[index] = plain.astype(out_ref.dtype)
            continue
        features = plain.shape[1]
        half = HD // 2
        group_len = meta_ref[0]
        group_requests = meta_ref[1]
        row = pl.program_id(0) * rows + lax.broadcasted_iota(jnp.int32, (rows, 1), 0)
        request = request_of(row, group_requests, tok_count)
        count = (jnp.zeros((rows, 1), jnp.int32) + group_requests).astype(jnp.float32)
        first = jnp.ceil((request * tok_count).astype(jnp.float32) / count).astype(jnp.int32)
        positions = (group_len + row - first).astype(jnp.float32)
        angles = positions * freq_ref[...]
        lane = lax.broadcasted_iota(jnp.int32, plain.shape, 1)
        ahead = pltpu.roll(plain, features - half, 1)
        behind = pltpu.roll(plain, half, 1)
        paired = jnp.where(lane % HD < half, -ahead, behind)
        rotated = plain * jnp.cos(angles) + paired * jnp.sin(angles)
        out_ref[index] = rotated.astype(out_ref.dtype)


def project(meta, tokens, gain, weights, frequency, parts):
    _, width, features = weights.shape
    tok_count = tokens.shape[0]
    rows = 256 if tok_count % 256 == 0 else tok_count

    def weight_spec(part):
        return pl.BlockSpec((1, width, features), lambda r, m: (part, 0, 0))

    return pl.pallas_call(
        functools.partial(projection_kernel, parts=parts),
        out_shape=jax.ShapeDtypeStruct((len(parts), tok_count, features), jnp.bfloat16),
        grid_spec=pltpu.PrefetchScalarGridSpec(
            num_scalar_prefetch=1,
            grid=(tok_count // rows,),
            in_specs=[
                pl.BlockSpec((rows, width), lambda r, m: (r, 0)),
                pl.BlockSpec((width,), lambda r, m: (0,)),
                pl.BlockSpec((1, features), lambda r, m: (0, 0)),
            ]
            + [weight_spec(part) for part in parts],
            out_specs=pl.BlockSpec((len(parts), rows, features), lambda r, m: (0, r, 0)),
        ),
    )(meta, tokens, gain, frequency, *(weights for _ in parts))


def local(tokens, norm_gain, w_qkv, w_out, kv_cache, cached_lengths, requests, block_start):
    group_idx = lax.axis_index("seq")
    tp_rank = lax.axis_index(("x", "core"))
    tp_count = lax.axis_size(("x", "core"))
    seq_count = lax.axis_size("seq")
    tok_count, model_width = tokens.shape
    features = w_qkv.shape[2]
    head_count = features // HD
    cache_len = kv_cache.shape[2]
    group_params = lax.dynamic_index_in_dim(
        jnp.stack([cached_lengths, requests, block_start], axis=1), group_idx, keepdims=False
    )
    group_len = group_params[0]
    group_requests = group_params[1]
    group_start = group_params[2]
    inputs = tokens.astype(jnp.float32)

    weights = jnp.transpose(w_qkv, (1, 0, 2))
    half_size = HD // 2
    frequency = jnp.exp(
        jnp.arange(half_size, dtype=jnp.float32) * (-2.0 * math.log(10000.0) / HD)
    )
    frequency = jnp.tile(frequency, features // half_size).reshape(1, features)
    gain = norm_gain
    core = lax.axis_index("core")
    swap_cores = [(0, 1), (1, 0)]
    mate_cache = lax.ppermute(kv_cache, "core", swap_cores)
    meta = jnp.concatenate([group_params, jnp.reshape(core, (1,))]).astype(jnp.int32)
    new_kv = project(meta, tokens, gain, weights, frequency, (1, 2))
    mate_new = lax.ppermute(new_kv, "core", swap_cores)
    joined = relay(meta, kv_cache, new_kv, mate_cache, mate_new, seq_count)
    queries = project(meta, tokens, gain, weights, frequency, (0,))[0]
    joined, attn_kv = lax.optimization_barrier((joined, new_kv))
    received = lax.all_to_all(joined, "seq", 0, 0, tiled=True)
    decode_cache = received.transpose(1, 0, 2, 3).reshape(2, 1, seq_count, 1, BLK, 2 * features)

    attended = attend(meta, queries, kv_cache, attn_kv)
    rows_dev = tok_count // tp_count
    partial = jnp.dot(attended, w_out, preferred_element_type=jnp.float32).astype(jnp.bfloat16)
    x_count = tp_count // 2
    x_rank = lax.axis_index("x")
    by_owner = partial.reshape(x_count, 2, rows_dev, model_width)
    mine = lax.dynamic_index_in_dim(by_owner, core, 1, keepdims=False)
    theirs = lax.dynamic_index_in_dim(by_owner, 1 - core, 1, keepdims=False)
    pair_sum = mine.astype(jnp.float32) + lax.ppermute(theirs, "core", swap_cores).astype(
        jnp.float32
    )
    pair_sent = pair_sum.astype(jnp.bfloat16)
    summed = lax.dynamic_index_in_dim(pair_sum, x_rank, 0, keepdims=False)
    for shift in range(1, x_count):
        target = (x_rank + shift) % x_count
        chunk = lax.dynamic_index_in_dim(pair_sent, target, 0, keepdims=False)
        pairs = [(source, (source + shift) % x_count) for source in range(x_count)]
        summed = summed + lax.ppermute(chunk, "x", pairs).astype(jnp.float32)
    own_rows = lax.dynamic_slice_in_dim(inputs, tp_rank * rows_dev, rows_dev, 0)
    layer_out = (own_rows + summed).astype(jnp.bfloat16)
    return (layer_out, decode_cache)


def solution(mesh):
    seq_count, tp_count = mesh.devices.shape
    split = Mesh(mesh.devices.reshape(seq_count, tp_count // 2, 2), ("seq", "x", "core"))
    tp = ("x", "core")
    placed = (
        P("seq", None),
        P(),
        P(None, None, tp),
        P(tp, None),
        P(None, "seq", None, tp),
        P(),
        P(),
        P(),
    )
    return jax.shard_map(
        local,
        mesh=split,
        in_specs=placed,
        out_specs=(P(("seq",) + tp, None), P(None, "seq", None, None, None, tp)),
        check_vma=False,
    )
```

```python
import functools
import math

import jax
import jax.numpy as jnp
from jax import lax
from jax.experimental import pallas as pl
from jax.experimental.pallas import tpu as pltpu
from jax.sharding import Mesh
from jax.sharding import PartitionSpec as P

HD = 96
BLK = 128
ROWS = 128


def rope_tables(positions, head_size):
    half_size = head_size // 2
    frequency = jnp.exp(
        jnp.arange(half_size, dtype=jnp.float32) * (-2.0 * math.log(10000.0) / head_size)
    )
    angles = positions.astype(jnp.float32)[:, None] * frequency[None, :]
    return (jnp.cos(angles), jnp.sin(angles))


def rope_pair(vectors, cosine_table, sine_table):
    half_size = vectors.shape[-1] // 2
    first_half = vectors[..., :half_size]
    second_half = vectors[..., half_size:]
    cos_wide = cosine_table[:, None, :]
    sin_wide = sine_table[:, None, :]
    return jnp.concatenate(
        [
            first_half * cos_wide - second_half * sin_wide,
            second_half * cos_wide + first_half * sin_wide,
        ],
        axis=-1,
    )


def request_of(index, group_requests, tok_count):
    scaled = index * group_requests
    if tok_count & (tok_count - 1) == 0:
        return lax.shift_right_logical(scaled, tok_count.bit_length() - 1)
    return scaled // tok_count


def head_picker(features, head):
    rows = lax.broadcasted_iota(jnp.int32, (features, HD), 0)
    cols = lax.broadcasted_iota(jnp.int32, (features, HD), 1)
    return (rows == cols + head * HD).astype(jnp.bfloat16)


def attention_kernel(
    meta_ref, q_ref, kc_ref, vc_ref, kn_ref, vn_ref, o_ref, kh_buf, vh_buf, qh_buf, acc_ref
):
    group_len = meta_ref[0]
    group_requests = meta_ref[1]
    head = pl.program_id(0)
    tok_count, features = q_ref.shape
    score_scale = 1.0 / math.sqrt(HD)
    picker = head_picker(features, head)

    def pick(values):
        return jnp.dot(values, picker, preferred_element_type=jnp.float32).astype(jnp.bfloat16)

    kh_buf[...] = pick(kc_ref[0, 0])
    vh_buf[...] = pick(vc_ref[0, 0])
    qh_buf[...] = pick(q_ref[...])
    kn = pick(kn_ref[0])
    vn = pick(vn_ref[0])
    dims = (((1,), (1,)), ((), ()))
    for chunk in range(tok_count // ROWS):
        rows = pl.ds(chunk * ROWS, ROWS)
        q = qh_buf[rows, :]
        s_old = lax.dot_general(q, kh_buf[...], dims, preferred_element_type=jnp.float32)
        s_new = lax.dot_general(q, kn, dims, preferred_element_type=jnp.float32)
        s_old = s_old * score_scale
        s_new = s_new * score_scale
        col = lax.broadcasted_iota(jnp.int32, s_old.shape, 1)
        s_old = jnp.where(col < group_len, s_old, -1e30)
        row = chunk * ROWS + lax.broadcasted_iota(jnp.int32, s_new.shape, 0)
        key = lax.broadcasted_iota(jnp.int32, s_new.shape, 1)
        same = request_of(row, group_requests, tok_count) == request_of(
            key, group_requests, tok_count
        )
        s_new = jnp.where(same & (key <= row), s_new, -1e30)
        peak = jnp.maximum(
            jnp.max(s_old, axis=1, keepdims=True), jnp.max(s_new, axis=1, keepdims=True)
        )
        e_old = jnp.exp(s_old - peak)
        e_new = jnp.exp(s_new - peak)
        total = jnp.sum(e_old, axis=1, keepdims=True) + jnp.sum(e_new, axis=1, keepdims=True)
        p_old = (e_old / total).astype(jnp.bfloat16)
        p_new = (e_new / total).astype(jnp.bfloat16)
        out = jnp.dot(p_old, vh_buf[...], preferred_element_type=jnp.float32) + jnp.dot(
            p_new, vn, preferred_element_type=jnp.float32
        )
        placed = lax.dot_general(
            out.astype(jnp.bfloat16), picker, dims, preferred_element_type=jnp.float32
        )

        @pl.when(head == 0)
        def _():
            acc_ref[rows, :] = placed

        @pl.when(head > 0)
        def _():
            acc_ref[rows, :] = acc_ref[rows, :] + placed

    @pl.when(head == pl.num_programs(0) - 1)
    def _():
        o_ref[...] = acc_ref[...].astype(jnp.bfloat16)


def attend(meta, queries, kv_cache, new_kv):
    tok_count, features = queries.shape
    cache_len = kv_cache.shape[2]
    full_q = pl.BlockSpec((tok_count, features), lambda h, m: (0, 0))
    cache_k = pl.BlockSpec((1, 1, cache_len, features), lambda h, m: (0, 0, 0, 0))
    cache_v = pl.BlockSpec((1, 1, cache_len, features), lambda h, m: (1, 0, 0, 0))
    new_k = pl.BlockSpec((1, tok_count, features), lambda h, m: (0, 0, 0))
    new_v = pl.BlockSpec((1, tok_count, features), lambda h, m: (1, 0, 0))
    return pl.pallas_call(
        attention_kernel,
        out_shape=jax.ShapeDtypeStruct(queries.shape, jnp.bfloat16),
        grid_spec=pltpu.PrefetchScalarGridSpec(
            num_scalar_prefetch=1,
            grid=(features // HD,),
            in_specs=[full_q, cache_k, cache_v, new_k, new_v],
            out_specs=full_q,
            scratch_shapes=[
                pltpu.VMEM((cache_len, HD), jnp.bfloat16),
                pltpu.VMEM((cache_len, HD), jnp.bfloat16),
                pltpu.VMEM((tok_count, HD), jnp.bfloat16),
                pltpu.VMEM((tok_count, features), jnp.float32),
            ],
        ),
    )(meta, queries, kv_cache, kv_cache, new_kv, new_kv)


def relay_kernel(meta_ref, *refs, new_blocks):
    out_ref = refs[-1]
    sources = refs[:-1]
    len_blocks = meta_ref[0] // BLK
    group_start = meta_ref[2]
    core = meta_ref[3]
    per_step = out_ref.shape[0]
    rank_count = 2 * pl.num_programs(0) * per_step
    features = sources[1].shape[2]
    zero = jnp.zeros(sources[1].shape[1:], sources[1].dtype)
    first = core == 0
    for slot in range(per_step):
        own_c, own_n, mate_c, mate_n = sources[4 * slot : 4 * slot + 4]
        dest = pl.program_id(0) * per_step + slot
        block = (2 * dest + core - group_start + rank_count) % rank_count
        old = block < len_blocks
        fresh = (block >= len_blocks) & (block < len_blocks + new_blocks)
        for kv in range(2):
            mine = jnp.where(old, own_c[kv, 0], jnp.where(fresh, own_n[kv], zero))
            mate = jnp.where(old, mate_c[kv, 0], jnp.where(fresh, mate_n[kv], zero))
            out_ref[slot, kv, :, :features] = jnp.where(first, mine, mate)
            out_ref[slot, kv, :, features:] = jnp.where(first, mate, mine)


def relay(meta, kv_cache, new_kv, mate_cache, mate_new, seq_count):
    features = kv_cache.shape[3]
    new_blocks = new_kv.shape[1] // BLK
    rank_count = 2 * seq_count
    per_step = 8 if seq_count % 8 == 0 else 1

    def block_of(d, slot, m):
        return (2 * (d * per_step + slot) + m[3] - m[2] + rank_count) % rank_count

    def cache_spec(slot):
        return pl.BlockSpec(
            (2, 1, BLK, features),
            lambda d, m: (0, 0, jnp.clip(block_of(d, slot, m), 0, m[0] // BLK - 1), 0),
        )

    def new_spec(slot):
        return pl.BlockSpec(
            (2, BLK, features),
            lambda d, m: (
                0,
                jnp.clip(block_of(d, slot, m) - m[0] // BLK, 0, new_blocks - 1),
                0,
            ),
        )

    in_specs = []
    operands = []
    for slot in range(per_step):
        in_specs += [cache_spec(slot), new_spec(slot), cache_spec(slot), new_spec(slot)]
        operands += [kv_cache, new_kv, mate_cache, mate_new]
    return pl.pallas_call(
        functools.partial(relay_kernel, new_blocks=new_blocks),
        out_shape=jax.ShapeDtypeStruct((seq_count, 2, BLK, 2 * features), jnp.bfloat16),
        grid_spec=pltpu.PrefetchScalarGridSpec(
            num_scalar_prefetch=1,
            grid=(seq_count // per_step,),
            in_specs=in_specs,
            out_specs=pl.BlockSpec(
                (per_step, 2, BLK, 2 * features), lambda d, m: (d, 0, 0, 0)
            ),
        ),
    )(meta, *operands)


def half_swap(features):
    half = HD // 2
    rows = lax.broadcasted_iota(jnp.int32, (features, features), 0)
    cols = lax.broadcasted_iota(jnp.int32, (features, features), 1)
    first = cols % HD < half
    return jnp.where(
        first & (rows == cols + half),
        -1.0,
        jnp.where(jnp.logical_not(first) & (rows == cols - half), 1.0, 0.0),
    ).astype(jnp.bfloat16)


def projection_kernel(meta_ref, x_ref, gain_ref, freq_ref, *refs, parts):
    w_refs = refs[: len(parts)]
    out_ref = refs[len(parts)]
    rows = x_ref.shape[0]
    tok_count = rows * pl.num_programs(0)
    inputs = x_ref[...].astype(jnp.float32)
    inverse_rms = lax.rsqrt(jnp.mean(inputs * inputs, axis=-1, keepdims=True) + 1e-05)
    gain = gain_ref[...].astype(jnp.float32).reshape(1, inputs.shape[1])
    normed = (inputs * inverse_rms * gain).astype(jnp.bfloat16)
    for index, part in enumerate(parts):
        plain = jnp.dot(normed, w_refs[index][0], preferred_element_type=jnp.float32)
        if part == 2:
            out_ref[index] = plain.astype(out_ref.dtype)
            continue
        features = plain.shape[1]
        half = HD // 2
        group_len = meta_ref[0]
        group_requests = meta_ref[1]
        row = pl.program_id(0) * rows + lax.broadcasted_iota(jnp.int32, (rows, 1), 0)
        request = request_of(row, group_requests, tok_count)
        count = (jnp.zeros((rows, 1), jnp.int32) + group_requests).astype(jnp.float32)
        first = jnp.ceil((request * tok_count).astype(jnp.float32) / count).astype(jnp.int32)
        positions = (group_len + row - first).astype(jnp.float32)
        angles = positions * freq_ref[...]
        lane = lax.broadcasted_iota(jnp.int32, plain.shape, 1)
        ahead = pltpu.roll(plain, features - half, 1)
        behind = pltpu.roll(plain, half, 1)
        paired = jnp.where(lane % HD < half, -ahead, behind)
        rotated = plain * jnp.cos(angles) + paired * jnp.sin(angles)
        out_ref[index] = rotated.astype(out_ref.dtype)


def project(meta, tokens, gain, weights, frequency, parts):
    _, width, features = weights.shape
    tok_count = tokens.shape[0]
    rows = 128 if tok_count % 128 == 0 else tok_count

    def weight_spec(part):
        return pl.BlockSpec((1, width, features), lambda r, m: (part, 0, 0))

    return pl.pallas_call(
        functools.partial(projection_kernel, parts=parts),
        out_shape=jax.ShapeDtypeStruct((len(parts), tok_count, features), jnp.bfloat16),
        grid_spec=pltpu.PrefetchScalarGridSpec(
            num_scalar_prefetch=1,
            grid=(tok_count // rows,),
            in_specs=[
                pl.BlockSpec((rows, width), lambda r, m: (r, 0)),
                pl.BlockSpec((width,), lambda r, m: (0,)),
                pl.BlockSpec((1, features), lambda r, m: (0, 0)),
            ]
            + [weight_spec(part) for part in parts],
            out_specs=pl.BlockSpec((len(parts), rows, features), lambda r, m: (0, r, 0)),
        ),
    )(meta, tokens, gain, frequency, *(weights for _ in parts))


def local(tokens, norm_gain, w_qkv, w_out, kv_cache, cached_lengths, requests, block_start):
    group_idx = lax.axis_index("seq")
    tp_rank = lax.axis_index(("x", "core"))
    tp_count = lax.axis_size(("x", "core"))
    seq_count = lax.axis_size("seq")
    tok_count, model_width = tokens.shape
    features = w_qkv.shape[2]
    head_count = features // HD
    cache_len = kv_cache.shape[2]
    group_params = lax.dynamic_index_in_dim(
        jnp.stack([cached_lengths, requests, block_start], axis=1), group_idx, keepdims=False
    )
    group_len = group_params[0]
    group_requests = group_params[1]
    group_start = group_params[2]
    inputs = tokens.astype(jnp.float32)

    weights = jnp.transpose(w_qkv, (1, 0, 2))
    half_size = HD // 2
    frequency = jnp.exp(
        jnp.arange(half_size, dtype=jnp.float32) * (-2.0 * math.log(10000.0) / HD)
    )
    frequency = jnp.tile(frequency, features // half_size).reshape(1, features)
    gain = norm_gain
    core = lax.axis_index("core")
    swap_cores = [(0, 1), (1, 0)]
    mate_cache = lax.ppermute(kv_cache, "core", swap_cores)
    meta = jnp.concatenate([group_params, jnp.reshape(core, (1,))]).astype(jnp.int32)
    new_kv = project(meta, tokens, gain, weights, frequency, (1, 2))
    mate_new = lax.ppermute(new_kv, "core", swap_cores)
    joined = relay(meta, kv_cache, new_kv, mate_cache, mate_new, seq_count)
    queries = project(meta, tokens, gain, weights, frequency, (0,))[0]
    joined, attn_kv = lax.optimization_barrier((joined, new_kv))
    received = lax.all_to_all(joined, "seq", 0, 0, tiled=True)
    decode_cache = received.transpose(1, 0, 2, 3).reshape(2, 1, seq_count, 1, BLK, 2 * features)

    attended = attend(meta, queries, kv_cache, attn_kv)
    rows_dev = tok_count // tp_count
    partial = jnp.dot(attended, w_out, preferred_element_type=jnp.float32).astype(jnp.bfloat16)
    x_count = tp_count // 2
    x_rank = lax.axis_index("x")
    by_owner = partial.reshape(x_count, 2, rows_dev, model_width)
    mine = lax.dynamic_index_in_dim(by_owner, core, 1, keepdims=False)
    theirs = lax.dynamic_index_in_dim(by_owner, 1 - core, 1, keepdims=False)
    pair_sum = mine.astype(jnp.float32) + lax.ppermute(theirs, "core", swap_cores).astype(
        jnp.float32
    )
    pair_sent = pair_sum.astype(jnp.bfloat16)
    summed = lax.dynamic_index_in_dim(pair_sum, x_rank, 0, keepdims=False)
    for shift in range(1, x_count):
        target = (x_rank + shift) % x_count
        chunk = lax.dynamic_index_in_dim(pair_sent, target, 0, keepdims=False)
        pairs = [(source, (source + shift) % x_count) for source in range(x_count)]
        summed = summed + lax.ppermute(chunk, "x", pairs).astype(jnp.float32)
    own_rows = lax.dynamic_slice_in_dim(inputs, tp_rank * rows_dev, rows_dev, 0)
    layer_out = (own_rows + summed).astype(jnp.bfloat16)
    return (layer_out, decode_cache)


def solution(mesh):
    seq_count, tp_count = mesh.devices.shape
    split = Mesh(mesh.devices.reshape(seq_count, tp_count // 2, 2), ("seq", "x", "core"))
    tp = ("x", "core")
    placed = (
        P("seq", None),
        P(),
        P(None, None, tp),
        P(tp, None),
        P(None, "seq", None, tp),
        P(),
        P(),
        P(),
    )
    return jax.shard_map(
        local,
        mesh=split,
        in_specs=placed,
        out_specs=(P(("seq",) + tp, None), P(None, "seq", None, None, None, tp)),
        check_vma=False,
    )
```
